32 devices in a mesh: rep: 2 (over y), tp: 8 (over z, x), sub: 2 (over core).
Axes of the slice: x: 2, y: 2, z: 4, core: 2. Of those that a mesh axis runs over, the one named last changes fastest.
Arguments:
- queries: bfloat16 [2, 16, 16384], P(None, ('rep', 'sub'), 'tp'), parts along dimension 1, may hold values from -53 to 53
- prefix_kv: bfloat16 [2, 16384, 1024], P(None, ('rep', 'tp')), parts along dimension 1, may hold values from -6 to 6
- tail_kv: bfloat16 [2, 16, 1024, 1024], P(None, ('rep', 'sub'), 'tp'), parts along dimension 1, may hold values from -6 to 6
- tail_lengths: int32 [16], P(('rep', 'sub')), parts along dimension 0, may hold values from 1 to 1024, as said below
- fresh_kv: bfloat16 [2, 2, 16, 1024], P(None, None, ('rep', 'sub')), parts along dimension 2, may hold values from -6 to 6
- out_weight: bfloat16 [16384, 16384], P('tp', 'sub'), may hold values from -0.5 to 0.5
- scale_in: int32 [128], replicated, may hold values from 9 to 14
- scale_out: int32 [128], replicated, may hold values from 5 to 10
- residual: bfloat16 [2, 16, 16384], P(None, 'rep', 'sub'), parts along dimension 1, may hold values from -1.5 to 1.5
Outputs:
- hidden: bfloat16 [2, 16, 16384], P(None, 'rep', 'sub'), parts along dimension 1
The draws below stay inside these ranges and needn't reach their ends.
There are 2 independent parts, one for each index of `rep`. The reference program is written for one: setup_inputs(seed, part) draws one part's arguments, and reference() takes and returns one part's arrays. A program takes and returns all parts, laid end to end along the dimension named above; an argument that names none is the same for every part. Nothing has to cross between parts.
Inputs may be any that keep to these rules, and one draw needn't show every extreme that they name: `tail_lengths`: some sample's tail reaches 1024 tokens.
All inputs are finite; a program needn't handle non-finite values.
Results may differ from the reference program's by a relative error of at most 0.0065.
Values may be sent and summed in bfloat16 or wider, within the bound.
No kernel may reach another device: no remote copies, remote signals or barrier semaphores. Data moves between devices by JAX's collectives and lax.ppermute only.
A program may use at most 192 MiB of HBM per device.

```python
import math
import jax
import jax.numpy as jnp
from jax import lax

D = 16384
H = 128
KVH = 8
DH = 128
P_SIZE = 8192
TAIL = 1024
B = 8
STEPS = 2


def shared_cache_queries(key):
    prompt_values = jnp.clip(jax.random.normal(jax.random.fold_in(key, 11), (2, P_SIZE, KVH * DH), jnp.float32), -6.0, 6.0)
    query_values = jnp.clip(jax.random.normal(jax.random.fold_in(key, 12), (STEPS, B, H * DH), jnp.float32), -6.0, 6.0)
    return (prompt_values, query_values)


def draw_prefix_kv(key, part):
    return shared_cache_queries(key)[0].astype(jnp.bfloat16)


def draw_queries(key, part):
    return shared_cache_queries(key)[1].astype(jnp.bfloat16)


def draw_tail_lengths(key, part):
    lengths = jax.random.randint(jax.random.fold_in(key, 21), (B,), 1, TAIL + 1, jnp.int32)
    chosen = jax.random.randint(jax.random.fold_in(key, 22), (), 0, B, jnp.int32)
    return lengths.at[chosen].set(TAIL)


def touch_ends(array, stream_key, smallest, top_value):
    dims = array.shape
    place = [jax.random.randint(jax.random.fold_in(stream_key, axis), (), 0, dims[axis]) for axis in range(len(dims))]
    array = array.at[tuple(place)].set(smallest)
    longest = dims.index(max(dims))
    place[longest] = (place[longest] + 1) % dims[longest]
    return array.at[tuple(place)].set(top_value)


def level_of(rng, extent, split, smallest, largest):
    loudness, own = 1.0, jax.random.fold_in(rng, 6)
    for dim, shards_of in split:
        steps = jnp.exp(jax.random.uniform(jax.random.fold_in(own, dim), (shards_of,), jnp.float32, smallest / len(split), largest / len(split)))
        loudness = loudness * jnp.repeat(steps, extent[dim] // shards_of).reshape([-1 if axis == dim else 1 for axis in range(len(extent))])
    return loudness


def centred(rng, dims, deviation, bound, split=(), kind=jnp.bfloat16):
    gain = level_of(rng, dims, split, -0.22, 0.18) if split else 1.0
    array = jax.random.normal(rng, dims, jnp.float32) * deviation * gain
    return jnp.minimum(jnp.maximum(array, -bound), bound).astype(kind)


def setup_inputs(seed: int = 0, part: int = 0) -> dict:
    arg_keys = jax.random.split(jax.random.key(seed), 10)
    own_keys = jax.random.split(jax.random.fold_in(arg_keys[9], part), 10)
    return {
        "queries": draw_queries(jax.random.fold_in(jax.random.fold_in(arg_keys[9], part), 71), part),
        "prefix_kv": draw_prefix_kv(jax.random.fold_in(jax.random.fold_in(arg_keys[9], part), 71), part),
        "tail_kv": centred(own_keys[2], (2, B, TAIL, KVH * DH), 1.0, 6.0, ((1, 2), (2, 8))),
        "tail_lengths": draw_tail_lengths(jax.random.fold_in(jax.random.fold_in(arg_keys[9], part), 71), part),
        "fresh_kv": centred(own_keys[4], (2, STEPS, B, KVH * DH), 1.0, 6.0, ((2, 2),)),
        "out_weight": centred(arg_keys[5], (H * DH, D), DH ** -0.5, 0.5, ((0, 8), (1, 2))),
        "scale_in": touch_ends(jax.random.randint(arg_keys[6], (D // 128,), 9, 15), jax.random.fold_in(arg_keys[6], 1), 9, 14).astype(jnp.int32),
        "scale_out": touch_ends(jax.random.randint(arg_keys[7], (D // 128,), 5, 11), jax.random.fold_in(arg_keys[7], 1), 5, 10).astype(jnp.int32),
        "residual": centred(own_keys[8], (STEPS, B, D), 0.25, 1.5, ((2, 2),)),
    }


NEG_FILL = -1e+30

def attend_head(query_head, prompt_keys, prompt_vals, tail_keys, tail_vals, fresh_keys, fresh_vals, tail_lengths):
    score_scale = 1.0 / math.sqrt(DH)
    flat_query = query_head.reshape(STEPS * B, DH)
    prompt_scores = jnp.dot(flat_query, prompt_keys.T, preferred_element_type=jnp.float32).reshape(STEPS, B, P_SIZE) * score_scale
    tail_scores = jnp.einsum('sbd,btd->sbt', query_head.astype(jnp.float32), tail_keys.astype(jnp.float32)) * score_scale
    tail_live = jnp.arange(TAIL, dtype=jnp.int32)[None, :] < tail_lengths[:, None]
    tail_scores = jnp.where(tail_live[None, :, :], tail_scores, NEG_FILL)
    fresh_scores = jnp.einsum('sbd,ubd->sbu', query_head.astype(jnp.float32), fresh_keys.astype(jnp.float32)) * score_scale
    fresh_live = jnp.arange(STEPS, dtype=jnp.int32)[None, :] <= jnp.arange(STEPS, dtype=jnp.int32)[:, None]
    fresh_scores = jnp.where(fresh_live[:, None, :], fresh_scores, NEG_FILL)
    peak = jnp.maximum(jnp.maximum(prompt_scores.max(-1), tail_scores.max(-1)), fresh_scores.max(-1))
    prompt_weights = jnp.exp(prompt_scores - peak[..., None])
    tail_weights = jnp.exp(tail_scores - peak[..., None])
    fresh_weights = jnp.exp(fresh_scores - peak[..., None])
    mass = prompt_weights.sum(-1) + tail_weights.sum(-1) + fresh_weights.sum(-1)
    numer = jnp.dot(prompt_weights.astype(jnp.bfloat16).reshape(STEPS * B, P_SIZE), prompt_vals, preferred_element_type=jnp.float32).reshape(STEPS, B, DH)
    numer = numer + jnp.einsum('sbt,btd->sbd', tail_weights.astype(jnp.bfloat16).astype(jnp.float32), tail_vals.astype(jnp.float32))
    numer = numer + jnp.einsum('sbu,ubd->sbd', fresh_weights.astype(jnp.bfloat16).astype(jnp.float32), fresh_vals.astype(jnp.float32))
    return (numer / mass[..., None]).astype(jnp.bfloat16)

def reference(queries, prefix_kv, tail_kv, tail_lengths, fresh_kv, out_weight, scale_in, scale_out, residual):
    group_size = H // KVH

    def per_head(head_index):
        query_head = lax.dynamic_slice_in_dim(queries, head_index * DH, DH, 2)
        column = head_index // group_size * DH
        prompt_keys = lax.dynamic_slice_in_dim(prefix_kv[0], column, DH, 1)
        prompt_vals = lax.dynamic_slice_in_dim(prefix_kv[1], column, DH, 1)
        tail_keys = lax.dynamic_slice_in_dim(tail_kv[0], column, DH, 2)
        tail_vals = lax.dynamic_slice_in_dim(tail_kv[1], column, DH, 2)
        fresh_keys = lax.dynamic_slice_in_dim(fresh_kv[0], column, DH, 2)
        fresh_vals = lax.dynamic_slice_in_dim(fresh_kv[1], column, DH, 2)
        return attend_head(query_head, prompt_keys, prompt_vals, tail_keys, tail_vals, fresh_keys, fresh_vals, tail_lengths)
    heads_out = lax.map(per_head, jnp.arange(H, dtype=jnp.int32))
    attended = jnp.transpose(heads_out, (1, 2, 0, 3)).reshape(STEPS * B, H * DH)
    scale_a = jnp.repeat(jnp.exp2(-scale_in.astype(jnp.float32)), 128)
    scale_b = jnp.repeat(jnp.exp2(-scale_out.astype(jnp.float32)), 128)

    def add_head(summed, head_index):
        rows_in = lax.dynamic_slice_in_dim(attended, head_index * DH, DH, 1)
        weights_in = lax.dynamic_slice_in_dim(out_weight, head_index * DH, DH, 0)
        term = jnp.dot(rows_in, weights_in, preferred_element_type=jnp.float32)
        return (summed + jnp.clip(term / scale_a, -127.0, 127.0), None)
    summed, unused = lax.scan(add_head, jnp.zeros((STEPS * B, D), jnp.float32), jnp.arange(H, dtype=jnp.int32))
    levels = jnp.clip(summed * scale_a / scale_b, -127.0, 127.0).astype(jnp.bfloat16)
    restored = levels.astype(jnp.float32) * scale_b
    hidden = residual.reshape(STEPS * B, D).astype(jnp.float32) + restored
    return hidden.astype(jnp.bfloat16).reshape(STEPS, B, D)
```

```python
import math

import jax
import jax.numpy as jnp
from jax import lax
from jax.sharding import PartitionSpec as P

DH = 128


NEG_FILL = -1e30


def _is_pow2(n):
    return n >= 1 and (n & (n - 1)) == 0


def _gather_blocks(x, axis_name, count):
    if count == 1:
        return x[None]
    if not _is_pow2(count):
        return lax.all_gather(x, axis_name, axis=0, tiled=False)
    me = lax.axis_index(axis_name)
    cur = x[None]
    k = 1
    while k < count:
        other = lax.ppermute(cur, axis_name, [(i, i ^ k) for i in range(count)])
        low = (me // k) % 2 == 0
        cur = jnp.where(low, jnp.concatenate([cur, other]), jnp.concatenate([other, cur]))
        k *= 2
    return cur


def _exchange(blocks, axis_name, count, direct_max=8):
    if count == 1:
        return blocks
    if count > direct_max:
        return jax.tree.map(
            lambda b: lax.all_to_all(b, axis_name, split_axis=0, concat_axis=0, tiled=True), blocks
        )
    me = lax.axis_index(axis_name)
    got = [jax.tree.map(lambda b: lax.dynamic_index_in_dim(b, me, 0, keepdims=False), blocks)]
    for k in range(1, count):
        dst = (me + k) % count
        send = jax.tree.map(lambda b: lax.dynamic_index_in_dim(b, dst, 0, keepdims=False), blocks)
        got.append(lax.ppermute(send, axis_name, [(i, (i + k) % count) for i in range(count)]))
    return jax.tree.map(lambda *xs: jnp.stack(xs), *got)


def per_device(
    queries, prefix_kv, tail_kv, tail_lengths, fresh_kv, out_weight, scale_in, scale_out, residual
):
    steps_n, rows_dev, width_dev = queries.shape
    heads_dev = width_dev // DH
    tp_count = lax.axis_size("tp")
    tp_rank = lax.axis_index("tp")
    sub_rank = lax.axis_index("sub")
    kv_heads = prefix_kv.shape[2] // DH
    heads_all = heads_dev * tp_count
    group = heads_all // kv_heads
    prefix_dev = prefix_kv.shape[1]
    tail_dev = tail_kv.shape[2]
    score_scale = 1.0 / math.sqrt(DH)

    q_blocks = _gather_blocks(queries, "tp", tp_count)
    q_all = jnp.moveaxis(q_blocks, 0, 2).reshape(steps_n, rows_dev, kv_heads, group, DH)

    p_keys = prefix_kv[0].reshape(prefix_dev, kv_heads, DH)
    p_vals = prefix_kv[1].reshape(prefix_dev, kv_heads, DH)
    t_keys = tail_kv[0].reshape(rows_dev, tail_dev, kv_heads, DH)
    t_vals = tail_kv[1].reshape(rows_dev, tail_dev, kv_heads, DH)
    p_scores = (
        jnp.einsum("sbkgd,pkd->sbkgp", q_all, p_keys, preferred_element_type=jnp.float32)
        * score_scale
    )
    t_scores = (
        jnp.einsum("sbkgd,btkd->sbkgt", q_all, t_keys, preferred_element_type=jnp.float32)
        * score_scale
    )
    t_pos = tp_rank * tail_dev + jnp.arange(tail_dev)
    t_live = t_pos[None, :] < tail_lengths[:, None]
    t_scores = jnp.where(t_live[None, :, None, None, :], t_scores, NEG_FILL)
    loc_peak = jnp.maximum(p_scores.max(-1), t_scores.max(-1))
    p_w = jnp.exp(p_scores - loc_peak[..., None])
    t_w = jnp.exp(t_scores - loc_peak[..., None])
    loc_mass = p_w.sum(-1) + t_w.sum(-1)
    loc_numer = jnp.einsum(
        "sbkgp,pkd->sbkgd", p_w.astype(jnp.bfloat16), p_vals, preferred_element_type=jnp.float32
    )
    loc_numer = loc_numer + jnp.einsum(
        "sbkgt,btkd->sbkgd", t_w.astype(jnp.bfloat16), t_vals, preferred_element_type=jnp.float32
    )

    def by_owner(x):
        x = x.reshape((steps_n, rows_dev, tp_count, heads_dev) + x.shape[4:])
        return jnp.moveaxis(x, 2, 0)

    stats = jnp.stack([by_owner(loc_peak), by_owner(loc_mass)], axis=1)
    got_numer, got_stats = _exchange(
        (by_owner(loc_numer), stats.reshape(tp_count, 2, -1)), "tp", tp_count
    )
    got_stats = got_stats.reshape(tp_count, 2, steps_n, rows_dev, heads_dev)
    got_peak = got_stats[:, 0]
    got_mass = got_stats[:, 1]

    own_query = queries.reshape(steps_n, rows_dev, heads_dev, DH)
    f_kv = fresh_kv.reshape(2, steps_n, rows_dev, kv_heads, DH)
    if group % heads_dev == 0:
        one_kv = lax.dynamic_index_in_dim(f_kv, tp_rank * heads_dev // group, 3, keepdims=True)
        f_kv = jnp.broadcast_to(one_kv, (2, steps_n, rows_dev, heads_dev, DH))
    else:
        kv_of_head = (tp_rank * heads_dev + jnp.arange(heads_dev)) // group
        f_kv = jnp.take(f_kv, kv_of_head, axis=3)
    f_scores = (
        jnp.einsum("sbhd,ubhd->sbhu", own_query, f_kv[0], preferred_element_type=jnp.float32)
        * score_scale
    )
    fresh_live = jnp.arange(steps_n)[None, :] <= jnp.arange(steps_n)[:, None]
    f_scores = jnp.where(fresh_live[:, None, None, :], f_scores, NEG_FILL)

    peak = jnp.maximum(got_peak.max(0), f_scores.max(-1))
    rescale = jnp.exp(got_peak - peak[None])
    f_w = jnp.exp(f_scores - peak[..., None])
    mass = (got_mass * rescale).sum(0) + f_w.sum(-1)
    numer = (got_numer * rescale[..., None]).sum(0)
    numer = numer + jnp.einsum(
        "sbhu,ubhd->sbhd", f_w.astype(jnp.bfloat16), f_kv[1], preferred_element_type=jnp.float32
    )
    attended = (numer / mass[..., None]).astype(jnp.bfloat16).reshape(steps_n, rows_dev, width_dev)

    gathered = lax.all_gather(attended, "sub", axis=1, tiled=True)
    samples = gathered.shape[1]
    local_width = out_weight.shape[1]
    head_rows_in = gathered.reshape(steps_n * samples, heads_dev, DH)
    head_weights = out_weight.reshape(heads_dev, DH, local_width)
    scale_a = jnp.repeat(jnp.exp2(-scale_in.astype(jnp.float32)), 128)
    scale_b = jnp.repeat(jnp.exp2(-scale_out.astype(jnp.float32)), 128)
    local_a = lax.dynamic_slice_in_dim(scale_a, sub_rank * local_width, local_width, 0)
    local_b = lax.dynamic_slice_in_dim(scale_b, sub_rank * local_width, local_width, 0)
    per_head_term = jnp.einsum(
        "rhd,hdf->rhf", head_rows_in, head_weights, preferred_element_type=jnp.float32
    )
    clipped = jnp.clip(per_head_term / local_a[None, None, :], -127.0, 127.0).sum(1)

    piece_cols = local_width // tp_count
    pieces = jnp.moveaxis(clipped.reshape(steps_n * samples, tp_count, piece_cols), 1, 0)
    got_pieces = _exchange(pieces, "tp", tp_count)
    summed = got_pieces.sum(0)
    piece_start = sub_rank * local_width + tp_rank * piece_cols
    piece_a = lax.dynamic_slice_in_dim(scale_a, piece_start, piece_cols, 0)
    piece_b = lax.dynamic_slice_in_dim(scale_b, piece_start, piece_cols, 0)
    levels = jnp.clip(summed * piece_a / piece_b, -127.0, 127.0).astype(jnp.bfloat16)
    level_blocks = _gather_blocks(levels, "tp", tp_count)
    all_levels = jnp.moveaxis(level_blocks, 0, 1).reshape(steps_n * samples, local_width)
    restored = all_levels.astype(jnp.float32) * local_b
    hidden = residual.reshape(steps_n * samples, local_width).astype(jnp.float32) + restored
    return hidden.astype(jnp.bfloat16).reshape(steps_n, samples, local_width)


def solution(mesh):
    return jax.shard_map(
        per_device,
        mesh=mesh,
        in_specs=(
            P(None, ("rep", "sub"), "tp"),
            P(None, ("rep", "tp"), None),
            P(None, ("rep", "sub"), "tp", None),
            P(("rep", "sub")),
            P(None, None, ("rep", "sub"), None),
            P("tp", "sub"),
            P(),
            P(),
            P(None, "rep", "sub"),
        ),
        out_specs=P(None, "rep", "sub"),
        check_vma=False,
    )
```

```python
import math

import jax
import jax.numpy as jnp
from jax import lax
from jax.sharding import PartitionSpec as P

DH = 128


NEG_FILL = -1e30


def _is_pow2(n):
    return n >= 1 and (n & (n - 1)) == 0


def _gather_blocks(x, axis_name, count):
    if count == 1:
        return x[None]
    if not _is_pow2(count):
        return lax.all_gather(x, axis_name, axis=0, tiled=False)
    me = lax.axis_index(axis_name)
    cur = x[None]
    k = 1
    while k < count:
        other = lax.ppermute(cur, axis_name, [(i, i ^ k) for i in range(count)])
        low = (me // k) % 2 == 0
        cur = jnp.where(low, jnp.concatenate([cur, other]), jnp.concatenate([other, cur]))
        k *= 2
    return cur


def _exchange(blocks, axis_name, count, direct_max=8):
    if count == 1:
        return blocks
    if count > direct_max:
        return jax.tree.map(
            lambda b: lax.all_to_all(b, axis_name, split_axis=0, concat_axis=0, tiled=True), blocks
        )
    me = lax.axis_index(axis_name)
    got = [jax.tree.map(lambda b: lax.dynamic_index_in_dim(b, me, 0, keepdims=False), blocks)]
    for k in range(1, count):
        dst = (me + k) % count
        send = jax.tree.map(lambda b: lax.dynamic_index_in_dim(b, dst, 0, keepdims=False), blocks)
        got.append(lax.ppermute(send, axis_name, [(i, (i + k) % count) for i in range(count)]))
    return jax.tree.map(lambda *xs: jnp.stack(xs), *got)


def per_device(
    queries, prefix_kv, tail_kv, tail_lengths, fresh_kv, out_weight, scale_in, scale_out, residual
):
    steps_n, rows_dev, width_dev = queries.shape
    heads_dev = width_dev // DH
    tp_count = lax.axis_size("tp")
    tp_rank = lax.axis_index("tp")
    sub_rank = lax.axis_index("sub")
    kv_heads = prefix_kv.shape[2] // DH
    heads_all = heads_dev * tp_count
    group = heads_all // kv_heads
    prefix_dev = prefix_kv.shape[1]
    tail_dev = tail_kv.shape[2]
    score_scale = 1.0 / math.sqrt(DH)

    if tp_count <= 8 and heads_dev % group == 0:
        got_numer, got_peak, got_mass = _partials_by_shift(
            queries, prefix_kv, tail_kv, tail_lengths, tp_count, tp_rank, group
        )
    else:
        got_numer, got_peak, got_mass = _partials_vectorized(
            queries, prefix_kv, tail_kv, tail_lengths, tp_count, tp_rank, group
        )
    return _finish(
        queries, fresh_kv, out_weight, scale_in, scale_out, residual,
        got_numer, got_peak, got_mass, tp_count, tp_rank, sub_rank, group,
    )


def _local_partial(q, keys, vals, t_keys, t_vals, t_live):
    score_scale = 1.0 / math.sqrt(DH)
    p_scores = (
        jnp.einsum("sbkgd,pkd->sbkgp", q, keys, preferred_element_type=jnp.float32) * score_scale
    )
    t_scores = (
        jnp.einsum("sbkgd,btkd->sbkgt", q, t_keys, preferred_element_type=jnp.float32)
        * score_scale
    )
    t_scores = jnp.where(t_live[None, :, None, None, :], t_scores, NEG_FILL)
    loc_peak = jnp.maximum(p_scores.max(-1), t_scores.max(-1))
    p_w = jnp.exp(p_scores - loc_peak[..., None])
    t_w = jnp.exp(t_scores - loc_peak[..., None])
    loc_mass = p_w.sum(-1) + t_w.sum(-1)
    loc_numer = jnp.einsum(
        "sbkgp,pkd->sbkgd", p_w.astype(jnp.bfloat16), vals, preferred_element_type=jnp.float32
    )
    loc_numer = loc_numer + jnp.einsum(
        "sbkgt,btkd->sbkgd", t_w.astype(jnp.bfloat16), t_vals, preferred_element_type=jnp.float32
    )
    return loc_numer, loc_peak, loc_mass


def _partials_by_shift(queries, prefix_kv, tail_kv, tail_lengths, tp_count, tp_rank, group):
    steps_n, rows_dev, width_dev = queries.shape
    heads_dev = width_dev // DH
    kv_blk = heads_dev // group
    prefix_dev = prefix_kv.shape[1]
    tail_dev = tail_kv.shape[2]
    t_pos = tp_rank * tail_dev + jnp.arange(tail_dev)
    t_live = t_pos[None, :] < tail_lengths[:, None]
    n_rows = steps_n * rows_dev * heads_dev
    n_stat = -(-2 * n_rows // DH)
    got = []
    for shift in range(tp_count):
        src = (tp_rank + shift) % tp_count
        if shift == 0:
            q = queries
        else:
            q = lax.ppermute(
                queries, "tp", [(i, (i - shift) % tp_count) for i in range(tp_count)]
            )
        col = src * (kv_blk * DH)
        keys = lax.dynamic_slice_in_dim(prefix_kv[0], col, kv_blk * DH, 1)
        vals = lax.dynamic_slice_in_dim(prefix_kv[1], col, kv_blk * DH, 1)
        t_keys = lax.dynamic_slice_in_dim(tail_kv[0], col, kv_blk * DH, 2)
        t_vals = lax.dynamic_slice_in_dim(tail_kv[1], col, kv_blk * DH, 2)
        numer, peak, mass = _local_partial(
            q.reshape(steps_n, rows_dev, kv_blk, group, DH),
            keys.reshape(prefix_dev, kv_blk, DH),
            vals.reshape(prefix_dev, kv_blk, DH),
            t_keys.reshape(rows_dev, tail_dev, kv_blk, DH),
            t_vals.reshape(rows_dev, tail_dev, kv_blk, DH),
            t_live,
        )
        stats = jnp.stack([peak.reshape(-1), mass.reshape(-1)]).reshape(-1)
        stats = jnp.pad(stats, (0, n_stat * DH - 2 * n_rows)).reshape(n_stat, DH)
        packed = jnp.concatenate([numer.reshape(n_rows, DH), stats], axis=0)
        if shift != 0:
            packed = lax.ppermute(
                packed, "tp", [(i, (i + shift) % tp_count) for i in range(tp_count)]
            )
        got.append(packed)
    got = jnp.stack(got)
    got_numer = got[:, :n_rows].reshape(tp_count, steps_n, rows_dev, heads_dev, DH)
    got_stats = got[:, n_rows:].reshape(tp_count, -1)[:, : 2 * n_rows]
    got_stats = got_stats.reshape(tp_count, 2, steps_n, rows_dev, heads_dev)
    return got_numer, got_stats[:, 0], got_stats[:, 1]


def _partials_vectorized(queries, prefix_kv, tail_kv, tail_lengths, tp_count, tp_rank, group):
    steps_n, rows_dev, width_dev = queries.shape
    heads_dev = width_dev // DH
    kv_heads = prefix_kv.shape[2] // DH
    prefix_dev = prefix_kv.shape[1]
    tail_dev = tail_kv.shape[2]
    q_blocks = _gather_blocks(queries, "tp", tp_count)
    q_all = jnp.moveaxis(q_blocks, 0, 2).reshape(steps_n, rows_dev, kv_heads, group, DH)

    t_pos = tp_rank * tail_dev + jnp.arange(tail_dev)
    t_live = t_pos[None, :] < tail_lengths[:, None]
    loc_numer, loc_peak, loc_mass = _local_partial(
        q_all,
        prefix_kv[0].reshape(prefix_dev, kv_heads, DH),
        prefix_kv[1].reshape(prefix_dev, kv_heads, DH),
        tail_kv[0].reshape(rows_dev, tail_dev, kv_heads, DH),
        tail_kv[1].reshape(rows_dev, tail_dev, kv_heads, DH),
        t_live,
    )

    def by_owner(x):
        x = x.reshape((steps_n, rows_dev, tp_count, heads_dev) + x.shape[4:])
        return jnp.moveaxis(x, 2, 0)

    stats = jnp.stack([by_owner(loc_peak), by_owner(loc_mass)], axis=1)
    got_numer, got_stats = _exchange(
        (by_owner(loc_numer), stats.reshape(tp_count, 2, -1)), "tp", tp_count
    )
    got_stats = got_stats.reshape(tp_count, 2, steps_n, rows_dev, heads_dev)
    return got_numer, got_stats[:, 0], got_stats[:, 1]


def _finish(
    queries, fresh_kv, out_weight, scale_in, scale_out, residual,
    got_numer, got_peak, got_mass, tp_count, tp_rank, sub_rank, group,
):
    steps_n, rows_dev, width_dev = queries.shape
    heads_dev = width_dev // DH
    kv_heads = fresh_kv.shape[3] // DH
    score_scale = 1.0 / math.sqrt(DH)
    own_query = queries.reshape(steps_n, rows_dev, heads_dev, DH)
    f_kv = fresh_kv.reshape(2, steps_n, rows_dev, kv_heads, DH)
    if group % heads_dev == 0:
        one_kv = lax.dynamic_index_in_dim(f_kv, tp_rank * heads_dev // group, 3, keepdims=True)
        f_kv = jnp.broadcast_to(one_kv, (2, steps_n, rows_dev, heads_dev, DH))
    else:
        kv_of_head = (tp_rank * heads_dev + jnp.arange(heads_dev)) // group
        f_kv = jnp.take(f_kv, kv_of_head, axis=3)
    f_scores = (
        jnp.einsum("sbhd,ubhd->sbhu", own_query, f_kv[0], preferred_element_type=jnp.float32)
        * score_scale
    )
    fresh_live = jnp.arange(steps_n)[None, :] <= jnp.arange(steps_n)[:, None]
    f_scores = jnp.where(fresh_live[:, None, None, :], f_scores, NEG_FILL)

    peak = jnp.maximum(got_peak.max(0), f_scores.max(-1))
    rescale = jnp.exp(got_peak - peak[None])
    f_w = jnp.exp(f_scores - peak[..., None])
    mass = (got_mass * rescale).sum(0) + f_w.sum(-1)
    numer = (got_numer * rescale[..., None]).sum(0)
    numer = numer + jnp.einsum(
        "sbhu,ubhd->sbhd", f_w.astype(jnp.bfloat16), f_kv[1], preferred_element_type=jnp.float32
    )
    attended = (numer / mass[..., None]).astype(jnp.bfloat16).reshape(steps_n, rows_dev, width_dev)

    gathered = lax.all_gather(attended, "sub", axis=1, tiled=True)
    samples = gathered.shape[1]
    local_width = out_weight.shape[1]
    head_rows_in = gathered.reshape(steps_n * samples, heads_dev, DH)
    head_weights = out_weight.reshape(heads_dev, DH, local_width)
    scale_a = jnp.repeat(jnp.exp2(-scale_in.astype(jnp.float32)), 128)
    scale_b = jnp.repeat(jnp.exp2(-scale_out.astype(jnp.float32)), 128)
    local_a = lax.dynamic_slice_in_dim(scale_a, sub_rank * local_width, local_width, 0)
    local_b = lax.dynamic_slice_in_dim(scale_b, sub_rank * local_width, local_width, 0)
    per_head_term = jnp.einsum(
        "rhd,hdf->rhf", head_rows_in, head_weights, preferred_element_type=jnp.float32
    )
    clipped = jnp.clip(per_head_term / local_a[None, None, :], -127.0, 127.0).sum(1)

    piece_cols = local_width // tp_count
    pieces = jnp.moveaxis(clipped.reshape(steps_n * samples, tp_count, piece_cols), 1, 0)
    got_pieces = _exchange(pieces, "tp", tp_count)
    summed = got_pieces.sum(0)
    piece_start = sub_rank * local_width + tp_rank * piece_cols
    piece_a = lax.dynamic_slice_in_dim(scale_a, piece_start, piece_cols, 0)
    piece_b = lax.dynamic_slice_in_dim(scale_b, piece_start, piece_cols, 0)
    levels = jnp.clip(summed * piece_a / piece_b, -127.0, 127.0).astype(jnp.bfloat16)
    level_blocks = _gather_blocks(levels, "tp", tp_count)
    all_levels = jnp.moveaxis(level_blocks, 0, 1).reshape(steps_n * samples, local_width)
    restored = all_levels.astype(jnp.float32) * local_b
    hidden = residual.reshape(steps_n * samples, local_width).astype(jnp.float32) + restored
    return hidden.astype(jnp.bfloat16).reshape(steps_n, samples, local_width)


def solution(mesh):
    return jax.shard_map(
        per_device,
        mesh=mesh,
        in_specs=(
            P(None, ("rep", "sub"), "tp"),
            P(None, ("rep", "tp"), None),
            P(None, ("rep", "sub"), "tp", None),
            P(("rep", "sub")),
            P(None, None, ("rep", "sub"), None),
            P("tp", "sub"),
            P(),
            P(),
            P(None, "rep", "sub"),
        ),
        out_specs=P(None, "rep", "sub"),
        check_vma=False,
    )
```

```python
import math

import jax
import jax.numpy as jnp
from jax import lax
from jax.experimental import pallas as pl
from jax.experimental.pallas import tpu as pltpu
from jax.sharding import PartitionSpec as P

DH = 128


NEG_FILL = -1e30


def _is_pow2(n):
    return n >= 1 and (n & (n - 1)) == 0


def _gather_blocks(x, axis_name, count):
    if count == 1:
        return x[None]
    if not _is_pow2(count):
        return lax.all_gather(x, axis_name, axis=0, tiled=False)
    me = lax.axis_index(axis_name)
    cur = x[None]
    k = 1
    while k < count:
        other = lax.ppermute(cur, axis_name, [(i, i ^ k) for i in range(count)])
        low = (me // k) % 2 == 0
        cur = jnp.where(low, jnp.concatenate([cur, other]), jnp.concatenate([other, cur]))
        k *= 2
    return cur


def _exchange(blocks, axis_name, count, direct_max=8):
    if count == 1:
        return blocks
    if count > direct_max:
        return jax.tree.map(
            lambda b: lax.all_to_all(b, axis_name, split_axis=0, concat_axis=0, tiled=True), blocks
        )
    me = lax.axis_index(axis_name)
    got = [jax.tree.map(lambda b: lax.dynamic_index_in_dim(b, me, 0, keepdims=False), blocks)]
    for k in range(1, count):
        dst = (me + k) % count
        send = jax.tree.map(lambda b: lax.dynamic_index_in_dim(b, dst, 0, keepdims=False), blocks)
        got.append(lax.ppermute(send, axis_name, [(i, (i + k) % count) for i in range(count)]))
    return jax.tree.map(lambda *xs: jnp.stack(xs), *got)


def _attend_kernel(q_ref, k_ref, v_ref, tk_ref, tv_ref, valid_ref, numer_ref, peak_ref, mass_ref):
    rows_n = q_ref.shape[1]
    samples = tk_ref.shape[1]
    per_sample = rows_n // samples
    score_scale = 1.0 / math.sqrt(DH)
    dims_nt = (((1,), (1,)), ((), ()))
    q = q_ref[0]
    p_scores = lax.dot_general(q, k_ref[0], dims_nt, preferred_element_type=jnp.float32)
    p_scores = p_scores * score_scale
    t_parts = []
    for r in range(samples):
        qr = q[r * per_sample:(r + 1) * per_sample]
        sr = lax.dot_general(qr, tk_ref[0, r], dims_nt, preferred_element_type=jnp.float32)
        sr = sr * score_scale
        t_parts.append(jnp.where(valid_ref[r:r + 1, :] > 0.0, sr, NEG_FILL))
    t_scores = jnp.concatenate(t_parts, axis=0)
    peak = jnp.maximum(
        jnp.max(p_scores, axis=1, keepdims=True), jnp.max(t_scores, axis=1, keepdims=True)
    )
    p_w = jnp.exp(p_scores - peak)
    t_w = jnp.exp(t_scores - peak)
    mass = jnp.sum(p_w, axis=1, keepdims=True) + jnp.sum(t_w, axis=1, keepdims=True)
    numer = jnp.dot(p_w.astype(jnp.bfloat16), v_ref[0], preferred_element_type=jnp.float32)
    t_w16 = t_w.astype(jnp.bfloat16)
    t_numer = [
        jnp.dot(
            t_w16[r * per_sample:(r + 1) * per_sample], tv_ref[0, r],
            preferred_element_type=jnp.float32,
        )
        for r in range(samples)
    ]
    numer_ref[0] = numer + jnp.concatenate(t_numer, axis=0)
    peak_ref[0] = jnp.broadcast_to(peak, peak_ref.shape[1:])
    mass_ref[0] = jnp.broadcast_to(mass, mass_ref.shape[1:])


def _attend_local(q_rows, prefix_kv, tail_kv, valid):
    kv_heads, rows_n, _ = q_rows.shape
    prefix_dev = prefix_kv.shape[1]
    samples, tail_dev = tail_kv.shape[1], tail_kv.shape[2]
    flops = 4 * kv_heads * rows_n * DH * (prefix_dev + tail_dev)
    bytes_in = 2 * (prefix_kv.size + tail_kv.size + q_rows.size)
    return pl.pallas_call(
        _attend_kernel,
        grid=(kv_heads,),
        in_specs=[
            pl.BlockSpec((1, rows_n, DH), lambda k: (k, 0, 0)),
            pl.BlockSpec((1, prefix_dev, DH), lambda k: (0, 0, k)),
            pl.BlockSpec((1, prefix_dev, DH), lambda k: (1, 0, k)),
            pl.BlockSpec((1, samples, tail_dev, DH), lambda k: (0, 0, 0, k)),
            pl.BlockSpec((1, samples, tail_dev, DH), lambda k: (1, 0, 0, k)),
            pl.BlockSpec((samples, tail_dev), lambda k: (0, 0)),
        ],
        out_specs=[
            pl.BlockSpec((1, rows_n, DH), lambda k: (k, 0, 0)),
            pl.BlockSpec((1, rows_n, DH), lambda k: (k, 0, 0)),
            pl.BlockSpec((1, rows_n, DH), lambda k: (k, 0, 0)),
        ],
        out_shape=[jax.ShapeDtypeStruct((kv_heads, rows_n, DH), jnp.float32)] * 3,
        cost_estimate=pl.CostEstimate(
            flops=flops,
            transcendentals=kv_heads * rows_n * (prefix_dev + tail_dev),
            bytes_accessed=bytes_in + 3 * 4 * kv_heads * rows_n * DH,
        ),
    )(q_rows, prefix_kv, prefix_kv, tail_kv, tail_kv, valid)


def per_device(
    queries, prefix_kv, tail_kv, tail_lengths, fresh_kv, out_weight, scale_in, scale_out, residual
):
    steps_n, rows_dev, width_dev = queries.shape
    heads_dev = width_dev // DH
    tp_count = lax.axis_size("tp")
    tp_rank = lax.axis_index("tp")
    sub_rank = lax.axis_index("sub")
    kv_heads = prefix_kv.shape[2] // DH
    heads_all = heads_dev * tp_count
    group = heads_all // kv_heads
    prefix_dev = prefix_kv.shape[1]
    tail_dev = tail_kv.shape[2]
    score_scale = 1.0 / math.sqrt(DH)

    q_blocks = _gather_blocks(queries, "tp", tp_count)
    q_all = jnp.moveaxis(q_blocks, 0, 2).reshape(steps_n, rows_dev, kv_heads, group, DH)
    q_rows = jnp.transpose(q_all, (2, 1, 0, 3, 4)).reshape(kv_heads, -1, DH)
    t_pos = tp_rank * tail_dev + jnp.arange(tail_dev)
    valid = (t_pos[None, :] < tail_lengths[:, None]).astype(jnp.float32)
    k_numer, k_peak, k_mass = _attend_local(q_rows, prefix_kv, tail_kv, valid)

    def by_owner(x):
        x = jnp.transpose(x, (2, 1, 0, 3) + tuple(range(4, x.ndim)))
        x = x.reshape((steps_n, rows_dev, tp_count, heads_dev) + x.shape[4:])
        return jnp.moveaxis(x, 2, 0)

    grid4 = (kv_heads, rows_dev, steps_n, group)
    o_numer = by_owner(k_numer.reshape(grid4 + (DH,))).reshape(tp_count, -1, DH)
    o_peak = by_owner(k_peak[..., 0].reshape(grid4)).reshape(tp_count, -1)
    o_mass = by_owner(k_mass[..., 0].reshape(grid4)).reshape(tp_count, -1)
    n_rows = steps_n * rows_dev * heads_dev
    n_stat = -(-2 * n_rows // DH)
    stats = jnp.concatenate([o_peak, o_mass], axis=1)
    stats = jnp.pad(stats, ((0, 0), (0, n_stat * DH - 2 * n_rows))).reshape(tp_count, n_stat, DH)
    got = _exchange(jnp.concatenate([o_numer, stats], axis=1), "tp", tp_count)
    got_numer = got[:, :n_rows].reshape(tp_count, steps_n, rows_dev, heads_dev, DH)
    got_stats = got[:, n_rows:].reshape(tp_count, -1)[:, : 2 * n_rows]
    got_stats = got_stats.reshape(tp_count, 2, steps_n, rows_dev, heads_dev)
    got_peak = got_stats[:, 0]
    got_mass = got_stats[:, 1]

    own_query = queries.reshape(steps_n, rows_dev, heads_dev, DH)
    f_kv = fresh_kv.reshape(2, steps_n, rows_dev, kv_heads, DH)
    if group % heads_dev == 0:
        one_kv = lax.dynamic_index_in_dim(f_kv, tp_rank * heads_dev // group, 3, keepdims=True)
        f_kv = jnp.broadcast_to(one_kv, (2, steps_n, rows_dev, heads_dev, DH))
    else:
        kv_of_head = (tp_rank * heads_dev + jnp.arange(heads_dev)) // group
        f_kv = jnp.take(f_kv, kv_of_head, axis=3)
    f_scores = (
        jnp.einsum("sbhd,ubhd->sbhu", own_query, f_kv[0], preferred_element_type=jnp.float32)
        * score_scale
    )
    fresh_live = jnp.arange(steps_n)[None, :] <= jnp.arange(steps_n)[:, None]
    f_scores = jnp.where(fresh_live[:, None, None, :], f_scores, NEG_FILL)

    peak = jnp.maximum(got_peak.max(0), f_scores.max(-1))
    rescale = jnp.exp(got_peak - peak[None])
    f_w = jnp.exp(f_scores - peak[..., None])
    mass = (got_mass * rescale).sum(0) + f_w.sum(-1)
    numer = (got_numer * rescale[..., None]).sum(0)
    numer = numer + jnp.einsum(
        "sbhu,ubhd->sbhd", f_w.astype(jnp.bfloat16), f_kv[1], preferred_element_type=jnp.float32
    )
    attended = (numer / mass[..., None]).astype(jnp.bfloat16).reshape(steps_n, rows_dev, width_dev)

    gathered = lax.all_gather(attended, "sub", axis=1, tiled=True)
    samples = gathered.shape[1]
    local_width = out_weight.shape[1]
    head_rows_in = gathered.reshape(steps_n * samples, heads_dev, DH)
    head_weights = out_weight.reshape(heads_dev, DH, local_width)
    scale_a = jnp.repeat(jnp.exp2(-scale_in.astype(jnp.float32)), 128)
    scale_b = jnp.repeat(jnp.exp2(-scale_out.astype(jnp.float32)), 128)
    local_a = lax.dynamic_slice_in_dim(scale_a, sub_rank * local_width, local_width, 0)
    local_b = lax.dynamic_slice_in_dim(scale_b, sub_rank * local_width, local_width, 0)
    per_head_term = jnp.einsum(
        "rhd,hdf->rhf", head_rows_in, head_weights, preferred_element_type=jnp.float32
    )
    clipped = jnp.clip(per_head_term / local_a[None, None, :], -127.0, 127.0).sum(1)

    piece_cols = local_width // tp_count
    pieces = jnp.moveaxis(clipped.reshape(steps_n * samples, tp_count, piece_cols), 1, 0)
    got_pieces = _exchange(pieces, "tp", tp_count)
    summed = got_pieces.sum(0)
    piece_start = sub_rank * local_width + tp_rank * piece_cols
    piece_a = lax.dynamic_slice_in_dim(scale_a, piece_start, piece_cols, 0)
    piece_b = lax.dynamic_slice_in_dim(scale_b, piece_start, piece_cols, 0)
    levels = jnp.clip(summed * piece_a / piece_b, -127.0, 127.0).astype(jnp.bfloat16)
    level_blocks = _gather_blocks(levels, "tp", tp_count)
    all_levels = jnp.moveaxis(level_blocks, 0, 1).reshape(steps_n * samples, local_width)
    restored = all_levels.astype(jnp.float32) * local_b
    hidden = residual.reshape(steps_n * samples, local_width).astype(jnp.float32) + restored
    return hidden.astype(jnp.bfloat16).reshape(steps_n, samples, local_width)


def solution(mesh):
    return jax.shard_map(
        per_device,
        mesh=mesh,
        in_specs=(
            P(None, ("rep", "sub"), "tp"),
            P(None, ("rep", "tp"), None),
            P(None, ("rep", "sub"), "tp", None),
            P(("rep", "sub")),
            P(None, None, ("rep", "sub"), None),
            P("tp", "sub"),
            P(),
            P(),
            P(None, "rep", "sub"),
        ),
        out_specs=P(None, "rep", "sub"),
        check_vma=False,
    )
```

```python
import math

import jax
import jax.numpy as jnp
from jax import lax
from jax.experimental import pallas as pl
from jax.experimental.pallas import tpu as pltpu
from jax.sharding import PartitionSpec as P

DH = 128


NEG_FILL = -1e30


def _is_pow2(n):
    return n >= 1 and (n & (n - 1)) == 0


def _gather_blocks(x, axis_name, count):
    if count == 1:
        return x[None]
    if not _is_pow2(count):
        return lax.all_gather(x, axis_name, axis=0, tiled=False)
    me = lax.axis_index(axis_name)
    cur = x[None]
    k = 1
    while k < count:
        other = lax.ppermute(cur, axis_name, [(i, i ^ k) for i in range(count)])
        low = (me // k) % 2 == 0
        cur = jnp.where(low, jnp.concatenate([cur, other]), jnp.concatenate([other, cur]))
        k *= 2
    return cur


def _exchange(blocks, axis_name, count, direct_max=8):
    if count == 1:
        return blocks
    if count > direct_max:
        return jax.tree.map(
            lambda b: lax.all_to_all(b, axis_name, split_axis=0, concat_axis=0, tiled=True), blocks
        )
    me = lax.axis_index(axis_name)
    got = [jax.tree.map(lambda b: lax.dynamic_index_in_dim(b, me, 0, keepdims=False), blocks)]
    for k in range(1, count):
        dst = (me + k) % count
        send = jax.tree.map(lambda b: lax.dynamic_index_in_dim(b, dst, 0, keepdims=False), blocks)
        got.append(lax.ppermute(send, axis_name, [(i, (i + k) % count) for i in range(count)]))
    return jax.tree.map(lambda *xs: jnp.stack(xs), *got)


def _attend_kernel(q_ref, k_ref, v_ref, tk_ref, tv_ref, valid_ref, numer_ref, peak_ref, mass_ref):
    rows_n = q_ref.shape[1]
    samples = tk_ref.shape[1]
    per_sample = rows_n // samples
    score_scale = 1.0 / math.sqrt(DH)
    dims_nt = (((1,), (1,)), ((), ()))
    q = q_ref[0]
    p_scores = lax.dot_general(q, k_ref[0], dims_nt, preferred_element_type=jnp.float32)
    p_scores = p_scores * score_scale
    t_parts = []
    for r in range(samples):
        qr = q[r * per_sample:(r + 1) * per_sample]
        sr = lax.dot_general(qr, tk_ref[0, r], dims_nt, preferred_element_type=jnp.float32)
        sr = sr * score_scale
        t_parts.append(jnp.where(valid_ref[r:r + 1, :] > 0.0, sr, NEG_FILL))
    t_scores = jnp.concatenate(t_parts, axis=0)
    peak = jnp.maximum(
        jnp.max(p_scores, axis=1, keepdims=True), jnp.max(t_scores, axis=1, keepdims=True)
    )
    p_w = jnp.exp(p_scores - peak)
    t_w = jnp.exp(t_scores - peak)
    mass = jnp.sum(p_w, axis=1, keepdims=True) + jnp.sum(t_w, axis=1, keepdims=True)
    numer = jnp.dot(p_w.astype(jnp.bfloat16), v_ref[0], preferred_element_type=jnp.float32)
    t_w16 = t_w.astype(jnp.bfloat16)
    t_numer = [
        jnp.dot(
            t_w16[r * per_sample:(r + 1) * per_sample], tv_ref[0, r],
            preferred_element_type=jnp.float32,
        )
        for r in range(samples)
    ]
    numer_ref[0] = numer + jnp.concatenate(t_numer, axis=0)
    peak_ref[0] = jnp.broadcast_to(peak, peak_ref.shape[1:])
    mass_ref[0] = jnp.broadcast_to(mass, mass_ref.shape[1:])


def _attend_local(q_rows, prefix_kv, tail_kv, valid):
    kv_heads, rows_n, _ = q_rows.shape
    prefix_dev = prefix_kv.shape[1]
    samples, tail_dev = tail_kv.shape[1], tail_kv.shape[2]
    flops = 4 * kv_heads * rows_n * DH * (prefix_dev + tail_dev)
    bytes_in = 2 * (prefix_kv.size + tail_kv.size + q_rows.size)
    return pl.pallas_call(
        _attend_kernel,
        grid=(kv_heads,),
        in_specs=[
            pl.BlockSpec((1, rows_n, DH), lambda k: (k, 0, 0)),
            pl.BlockSpec((1, prefix_dev, DH), lambda k: (0, 0, k)),
            pl.BlockSpec((1, prefix_dev, DH), lambda k: (1, 0, k)),
            pl.BlockSpec((1, samples, tail_dev, DH), lambda k: (0, 0, 0, k)),
            pl.BlockSpec((1, samples, tail_dev, DH), lambda k: (1, 0, 0, k)),
            pl.BlockSpec((samples, tail_dev), lambda k: (0, 0)),
        ],
        out_specs=[
            pl.BlockSpec((1, rows_n, DH), lambda k: (k, 0, 0)),
            pl.BlockSpec((1, rows_n, DH), lambda k: (k, 0, 0)),
            pl.BlockSpec((1, rows_n, DH), lambda k: (k, 0, 0)),
        ],
        out_shape=[jax.ShapeDtypeStruct((kv_heads, rows_n, DH), jnp.float32)] * 3,
        cost_estimate=pl.CostEstimate(
            flops=flops,
            transcendentals=kv_heads * rows_n * (prefix_dev + tail_dev),
            bytes_accessed=bytes_in + 3 * 4 * kv_heads * rows_n * DH,
        ),
    )(q_rows, prefix_kv, prefix_kv, tail_kv, tail_kv, valid)


def _project_kernel(blk_ref, rows_ref, w_ref, a_ref, out_ref):
    @pl.when(pl.program_id(0) == 0)
    def _():
        out_ref[...] = jnp.zeros_like(out_ref)

    inv_rows = rows_ref.shape[1] // DH
    acc = out_ref[...]
    a = a_ref[...]
    for h in range(inv_rows):
        term = jnp.dot(
            rows_ref[:, h * DH:(h + 1) * DH], w_ref[h * DH:(h + 1) * DH, :],
            preferred_element_type=jnp.float32,
        )
        acc = acc + jnp.clip(term / a, -127.0, 127.0)
    out_ref[...] = acc


def _project_block(blk, rows, out_weight, local_a, piece_cols, heads_per_step=4):
    n_rows, width = rows.shape
    chunk = heads_per_step * DH
    steps = width // chunk
    grid_spec = pltpu.PrefetchScalarGridSpec(
        num_scalar_prefetch=1,
        grid=(steps,),
        in_specs=[
            pl.BlockSpec((n_rows, chunk), lambda c, b: (0, c)),
            pl.BlockSpec((chunk, piece_cols), lambda c, b: (c, b[0])),
            pl.BlockSpec((1, piece_cols), lambda c, b: (0, b[0])),
        ],
        out_specs=pl.BlockSpec((n_rows, piece_cols), lambda c, b: (0, 0)),
    )
    return pl.pallas_call(
        _project_kernel,
        grid_spec=grid_spec,
        out_shape=jax.ShapeDtypeStruct((n_rows, piece_cols), jnp.float32),
        cost_estimate=pl.CostEstimate(
            flops=2 * n_rows * width * piece_cols,
            transcendentals=0,
            bytes_accessed=2 * width * piece_cols + 2 * rows.size + 8 * n_rows * piece_cols,
        ),
    )(jnp.reshape(blk, (1,)).astype(jnp.int32), rows, out_weight, local_a)


def per_device(
    queries, prefix_kv, tail_kv, tail_lengths, fresh_kv, out_weight, scale_in, scale_out, residual
):
    steps_n, rows_dev, width_dev = queries.shape
    heads_dev = width_dev // DH
    tp_count = lax.axis_size("tp")
    tp_rank = lax.axis_index("tp")
    sub_rank = lax.axis_index("sub")
    kv_heads = prefix_kv.shape[2] // DH
    heads_all = heads_dev * tp_count
    group = heads_all // kv_heads
    prefix_dev = prefix_kv.shape[1]
    tail_dev = tail_kv.shape[2]
    score_scale = 1.0 / math.sqrt(DH)

    q_blocks = _gather_blocks(queries, "tp", tp_count)
    q_all = jnp.moveaxis(q_blocks, 0, 2).reshape(steps_n, rows_dev, kv_heads, group, DH)
    q_rows = jnp.transpose(q_all, (2, 1, 0, 3, 4)).reshape(kv_heads, -1, DH)
    t_pos = tp_rank * tail_dev + jnp.arange(tail_dev)
    valid = (t_pos[None, :] < tail_lengths[:, None]).astype(jnp.float32)
    k_numer, k_peak, k_mass = _attend_local(q_rows, prefix_kv, tail_kv, valid)

    def by_owner(x):
        x = jnp.transpose(x, (2, 1, 0, 3) + tuple(range(4, x.ndim)))
        x = x.reshape((steps_n, rows_dev, tp_count, heads_dev) + x.shape[4:])
        return jnp.moveaxis(x, 2, 0)

    grid4 = (kv_heads, rows_dev, steps_n, group)
    o_numer = by_owner(k_numer.reshape(grid4 + (DH,))).reshape(tp_count, -1, DH)
    o_peak = by_owner(k_peak[..., 0].reshape(grid4)).reshape(tp_count, -1)
    o_mass = by_owner(k_mass[..., 0].reshape(grid4)).reshape(tp_count, -1)
    n_rows = steps_n * rows_dev * heads_dev
    n_stat = -(-2 * n_rows // DH)
    stats = jnp.concatenate([o_peak, o_mass], axis=1)
    stats = jnp.pad(stats, ((0, 0), (0, n_stat * DH - 2 * n_rows))).reshape(tp_count, n_stat, DH)
    got = _exchange(jnp.concatenate([o_numer, stats], axis=1), "tp", tp_count)
    got_numer = got[:, :n_rows].reshape(tp_count, steps_n, rows_dev, heads_dev, DH)
    got_stats = got[:, n_rows:].reshape(tp_count, -1)[:, : 2 * n_rows]
    got_stats = got_stats.reshape(tp_count, 2, steps_n, rows_dev, heads_dev)
    got_peak = got_stats[:, 0]
    got_mass = got_stats[:, 1]

    own_query = queries.reshape(steps_n, rows_dev, heads_dev, DH)
    f_kv = fresh_kv.reshape(2, steps_n, rows_dev, kv_heads, DH)
    if group % heads_dev == 0:
        one_kv = lax.dynamic_index_in_dim(f_kv, tp_rank * heads_dev // group, 3, keepdims=True)
        f_kv = jnp.broadcast_to(one_kv, (2, steps_n, rows_dev, heads_dev, DH))
    else:
        kv_of_head = (tp_rank * heads_dev + jnp.arange(heads_dev)) // group
        f_kv = jnp.take(f_kv, kv_of_head, axis=3)
    f_scores = (
        jnp.einsum("sbhd,ubhd->sbhu", own_query, f_kv[0], preferred_element_type=jnp.float32)
        * score_scale
    )
    fresh_live = jnp.arange(steps_n)[None, :] <= jnp.arange(steps_n)[:, None]
    f_scores = jnp.where(fresh_live[:, None, None, :], f_scores, NEG_FILL)

    peak = jnp.maximum(got_peak.max(0), f_scores.max(-1))
    rescale = jnp.exp(got_peak - peak[None])
    f_w = jnp.exp(f_scores - peak[..., None])
    mass = (got_mass * rescale).sum(0) + f_w.sum(-1)
    numer = (got_numer * rescale[..., None]).sum(0)
    numer = numer + jnp.einsum(
        "sbhu,ubhd->sbhd", f_w.astype(jnp.bfloat16), f_kv[1], preferred_element_type=jnp.float32
    )
    attended = (numer / mass[..., None]).astype(jnp.bfloat16).reshape(steps_n, rows_dev, width_dev)

    gathered = lax.all_gather(attended, "sub", axis=1, tiled=True)
    samples = gathered.shape[1]
    local_width = out_weight.shape[1]
    head_rows_in = gathered.reshape(steps_n * samples, heads_dev, DH)
    head_weights = out_weight.reshape(heads_dev, DH, local_width)
    scale_a = jnp.repeat(jnp.exp2(-scale_in.astype(jnp.float32)), 128)
    scale_b = jnp.repeat(jnp.exp2(-scale_out.astype(jnp.float32)), 128)
    local_a = lax.dynamic_slice_in_dim(scale_a, sub_rank * local_width, local_width, 0)
    local_b = lax.dynamic_slice_in_dim(scale_b, sub_rank * local_width, local_width, 0)
    piece_cols = local_width // tp_count
    if tp_count <= 8 and piece_cols % 128 == 0:
        rows_flat = gathered.reshape(steps_n * samples, width_dev)
        parts = []
        for shift in range(tp_count):
            blk = (tp_rank + shift) % tp_count
            part = _project_block(
                blk, rows_flat, out_weight, local_a.reshape(1, -1), piece_cols,
                heads_per_step=4 if heads_dev % 4 == 0 else 1,
            )
            if shift != 0:
                part = lax.ppermute(
                    part, "tp", [(i, (i + shift) % tp_count) for i in range(tp_count)]
                )
            parts.append(part)
        summed = sum(parts)
    else:
        per_head_term = jnp.einsum(
            "rhd,hdf->rhf", head_rows_in, head_weights, preferred_element_type=jnp.float32
        )
        clipped = jnp.clip(per_head_term / local_a[None, None, :], -127.0, 127.0).sum(1)
        pieces = jnp.moveaxis(clipped.reshape(steps_n * samples, tp_count, piece_cols), 1, 0)
        got_pieces = _exchange(pieces, "tp", tp_count)
        summed = got_pieces.sum(0)
    piece_start = sub_rank * local_width + tp_rank * piece_cols
    piece_a = lax.dynamic_slice_in_dim(scale_a, piece_start, piece_cols, 0)
    piece_b = lax.dynamic_slice_in_dim(scale_b, piece_start, piece_cols, 0)
    levels = jnp.clip(summed * piece_a / piece_b, -127.0, 127.0).astype(jnp.bfloat16)
    level_blocks = _gather_blocks(levels, "tp", tp_count)
    all_levels = jnp.moveaxis(level_blocks, 0, 1).reshape(steps_n * samples, local_width)
    restored = all_levels.astype(jnp.float32) * local_b
    hidden = residual.reshape(steps_n * samples, local_width).astype(jnp.float32) + restored
    return hidden.astype(jnp.bfloat16).reshape(steps_n, samples, local_width)


def solution(mesh):
    return jax.shard_map(
        per_device,
        mesh=mesh,
        in_specs=(
            P(None, ("rep", "sub"), "tp"),
            P(None, ("rep", "tp"), None),
            P(None, ("rep", "sub"), "tp", None),
            P(("rep", "sub")),
            P(None, None, ("rep", "sub"), None),
            P("tp", "sub"),
            P(),
            P(),
            P(None, "rep", "sub"),
        ),
        out_specs=P(None, "rep", "sub"),
        check_vma=False,
    )
```

```python
import math

import jax
import jax.numpy as jnp
from jax import lax
from jax.experimental import pallas as pl
from jax.experimental.pallas import tpu as pltpu
from jax.sharding import PartitionSpec as P

DH = 128


NEG_FILL = -1e30


def _is_pow2(n):
    return n >= 1 and (n & (n - 1)) == 0


def _gather_blocks(x, axis_name, count):
    if count == 1:
        return x[None]
    if not _is_pow2(count):
        return lax.all_gather(x, axis_name, axis=0, tiled=False)
    me = lax.axis_index(axis_name)
    if count <= 8:
        other = lax.ppermute(x, axis_name, [(i, i ^ 1) for i in range(count)])
        low = me % 2 == 0
        pair = jnp.where(low, jnp.stack([x, other]), jnp.stack([other, x]))
        pairs = [pair]
        for d in range(1, count // 2):
            pairs.append(
                lax.ppermute(pair, axis_name, [(i, (i + 2 * d) % count) for i in range(count)])
            )
        order = (me // 2 - jnp.arange(count // 2)) % (count // 2)
        placed = jnp.zeros((count // 2,) + pair.shape, pair.dtype).at[order].set(jnp.stack(pairs))
        return placed.reshape((count,) + x.shape)
    cur = x[None]
    k = 1
    while k < count:
        other = lax.ppermute(cur, axis_name, [(i, i ^ k) for i in range(count)])
        low = (me // k) % 2 == 0
        cur = jnp.where(low, jnp.concatenate([cur, other]), jnp.concatenate([other, cur]))
        k *= 2
    return cur


def _exchange(blocks, axis_name, count, direct_max=8):
    if count == 1:
        return blocks
    if count > direct_max:
        return jax.tree.map(
            lambda b: lax.all_to_all(b, axis_name, split_axis=0, concat_axis=0, tiled=True), blocks
        )
    me = lax.axis_index(axis_name)
    got = [jax.tree.map(lambda b: lax.dynamic_index_in_dim(b, me, 0, keepdims=False), blocks)]
    for k in range(1, count):
        dst = (me + k) % count
        send = jax.tree.map(lambda b: lax.dynamic_index_in_dim(b, dst, 0, keepdims=False), blocks)
        got.append(lax.ppermute(send, axis_name, [(i, (i + k) % count) for i in range(count)]))
    return jax.tree.map(lambda *xs: jnp.stack(xs), *got)


def _attend_kernel(q_ref, k_ref, v_ref, tk_ref, tv_ref, valid_ref, numer_ref, peak_ref, mass_ref):
    rows_n = q_ref.shape[1]
    samples = tk_ref.shape[1]
    per_sample = rows_n // samples
    score_scale = 1.0 / math.sqrt(DH)
    dims_nt = (((1,), (1,)), ((), ()))
    q = q_ref[0]
    p_scores = lax.dot_general(q, k_ref[0], dims_nt, preferred_element_type=jnp.float32)
    p_scores = p_scores * score_scale
    t_parts = []
    for r in range(samples):
        qr = q[r * per_sample:(r + 1) * per_sample]
        sr = lax.dot_general(qr, tk_ref[0, r], dims_nt, preferred_element_type=jnp.float32)
        sr = sr * score_scale
        t_parts.append(jnp.where(valid_ref[r:r + 1, :] > 0.0, sr, NEG_FILL))
    t_scores = jnp.concatenate(t_parts, axis=0)
    peak = jnp.maximum(
        jnp.max(p_scores, axis=1, keepdims=True), jnp.max(t_scores, axis=1, keepdims=True)
    )
    p_w = jnp.exp(p_scores - peak)
    t_w = jnp.exp(t_scores - peak)
    mass = jnp.sum(p_w, axis=1, keepdims=True) + jnp.sum(t_w, axis=1, keepdims=True)
    numer = jnp.dot(p_w.astype(jnp.bfloat16), v_ref[0], preferred_element_type=jnp.float32)
    t_w16 = t_w.astype(jnp.bfloat16)
    t_numer = [
        jnp.dot(
            t_w16[r * per_sample:(r + 1) * per_sample], tv_ref[0, r],
            preferred_element_type=jnp.float32,
        )
        for r in range(samples)
    ]
    numer_ref[0] = numer + jnp.concatenate(t_numer, axis=0)
    peak_ref[0] = jnp.broadcast_to(peak, peak_ref.shape[1:])
    mass_ref[0] = jnp.broadcast_to(mass, mass_ref.shape[1:])


def _attend_local(q_rows, prefix_kv, tail_kv, valid):
    kv_heads, rows_n, _ = q_rows.shape
    prefix_dev = prefix_kv.shape[1]
    samples, tail_dev = tail_kv.shape[1], tail_kv.shape[2]
    flops = 4 * kv_heads * rows_n * DH * (prefix_dev + tail_dev)
    bytes_in = 2 * (prefix_kv.size + tail_kv.size + q_rows.size)
    return pl.pallas_call(
        _attend_kernel,
        grid=(kv_heads,),
        in_specs=[
            pl.BlockSpec((1, rows_n, DH), lambda k: (k, 0, 0)),
            pl.BlockSpec((1, prefix_dev, DH), lambda k: (0, 0, k)),
            pl.BlockSpec((1, prefix_dev, DH), lambda k: (1, 0, k)),
            pl.BlockSpec((1, samples, tail_dev, DH), lambda k: (0, 0, 0, k)),
            pl.BlockSpec((1, samples, tail_dev, DH), lambda k: (1, 0, 0, k)),
            pl.BlockSpec((samples, tail_dev), lambda k: (0, 0)),
        ],
        out_specs=[
            pl.BlockSpec((1, rows_n, DH), lambda k: (k, 0, 0)),
            pl.BlockSpec((1, rows_n, DH), lambda k: (k, 0, 0)),
            pl.BlockSpec((1, rows_n, DH), lambda k: (k, 0, 0)),
        ],
        out_shape=[jax.ShapeDtypeStruct((kv_heads, rows_n, DH), jnp.float32)] * 3,
        cost_estimate=pl.CostEstimate(
            flops=flops,
            transcendentals=kv_heads * rows_n * (prefix_dev + tail_dev),
            bytes_accessed=bytes_in + 3 * 4 * kv_heads * rows_n * DH,
        ),
    )(q_rows, prefix_kv, prefix_kv, tail_kv, tail_kv, valid)


def per_device(
    queries, prefix_kv, tail_kv, tail_lengths, fresh_kv, out_weight, scale_in, scale_out, residual
):
    steps_n, rows_dev, width_dev = queries.shape
    heads_dev = width_dev // DH
    tp_count = lax.axis_size("tp")
    tp_rank = lax.axis_index("tp")
    sub_rank = lax.axis_index("sub")
    kv_heads = prefix_kv.shape[2] // DH
    heads_all = heads_dev * tp_count
    group = heads_all // kv_heads
    prefix_dev = prefix_kv.shape[1]
    tail_dev = tail_kv.shape[2]
    score_scale = 1.0 / math.sqrt(DH)

    q_blocks = _gather_blocks(queries, "tp", tp_count)
    q_all = jnp.moveaxis(q_blocks, 0, 2).reshape(steps_n, rows_dev, kv_heads, group, DH)
    q_rows = jnp.transpose(q_all, (2, 1, 0, 3, 4)).reshape(kv_heads, -1, DH)
    t_pos = tp_rank * tail_dev + jnp.arange(tail_dev)
    valid = (t_pos[None, :] < tail_lengths[:, None]).astype(jnp.float32)
    k_numer, k_peak, k_mass = _attend_local(q_rows, prefix_kv, tail_kv, valid)

    def by_owner(x):
        x = jnp.transpose(x, (2, 1, 0, 3) + tuple(range(4, x.ndim)))
        x = x.reshape((steps_n, rows_dev, tp_count, heads_dev) + x.shape[4:])
        return jnp.moveaxis(x, 2, 0)

    grid4 = (kv_heads, rows_dev, steps_n, group)
    o_numer = by_owner(k_numer.reshape(grid4 + (DH,))).reshape(tp_count, -1, DH)
    o_peak = by_owner(k_peak[..., 0].reshape(grid4)).reshape(tp_count, -1)
    o_mass = by_owner(k_mass[..., 0].reshape(grid4)).reshape(tp_count, -1)
    n_rows = steps_n * rows_dev * heads_dev
    n_stat = -(-2 * n_rows // DH)
    stats = jnp.concatenate([o_peak, o_mass], axis=1)
    stats = jnp.pad(stats, ((0, 0), (0, n_stat * DH - 2 * n_rows))).reshape(tp_count, n_stat, DH)
    got = _exchange(jnp.concatenate([o_numer, stats], axis=1), "tp", tp_count)
    got_numer = got[:, :n_rows].reshape(tp_count, steps_n, rows_dev, heads_dev, DH)
    got_stats = got[:, n_rows:].reshape(tp_count, -1)[:, : 2 * n_rows]
    got_stats = got_stats.reshape(tp_count, 2, steps_n, rows_dev, heads_dev)
    got_peak = got_stats[:, 0]
    got_mass = got_stats[:, 1]

    own_query = queries.reshape(steps_n, rows_dev, heads_dev, DH)
    f_kv = fresh_kv.reshape(2, steps_n, rows_dev, kv_heads, DH)
    if group % heads_dev == 0:
        one_kv = lax.dynamic_index_in_dim(f_kv, tp_rank * heads_dev // group, 3, keepdims=True)
        f_kv = jnp.broadcast_to(one_kv, (2, steps_n, rows_dev, heads_dev, DH))
    else:
        kv_of_head = (tp_rank * heads_dev + jnp.arange(heads_dev)) // group
        f_kv = jnp.take(f_kv, kv_of_head, axis=3)
    f_scores = (
        jnp.einsum("sbhd,ubhd->sbhu", own_query, f_kv[0], preferred_element_type=jnp.float32)
        * score_scale
    )
    fresh_live = jnp.arange(steps_n)[None, :] <= jnp.arange(steps_n)[:, None]
    f_scores = jnp.where(fresh_live[:, None, None, :], f_scores, NEG_FILL)

    peak = jnp.maximum(got_peak.max(0), f_scores.max(-1))
    rescale = jnp.exp(got_peak - peak[None])
    f_w = jnp.exp(f_scores - peak[..., None])
    mass = (got_mass * rescale).sum(0) + f_w.sum(-1)
    numer = (got_numer * rescale[..., None]).sum(0)
    numer = numer + jnp.einsum(
        "sbhu,ubhd->sbhd", f_w.astype(jnp.bfloat16), f_kv[1], preferred_element_type=jnp.float32
    )
    attended = (numer / mass[..., None]).astype(jnp.bfloat16).reshape(steps_n, rows_dev, width_dev)

    gathered = lax.all_gather(attended, "sub", axis=1, tiled=True)
    samples = gathered.shape[1]
    local_width = out_weight.shape[1]
    head_rows_in = gathered.reshape(steps_n * samples, heads_dev, DH)
    head_weights = out_weight.reshape(heads_dev, DH, local_width)
    scale_a = jnp.repeat(jnp.exp2(-scale_in.astype(jnp.float32)), 128)
    scale_b = jnp.repeat(jnp.exp2(-scale_out.astype(jnp.float32)), 128)
    local_a = lax.dynamic_slice_in_dim(scale_a, sub_rank * local_width, local_width, 0)
    local_b = lax.dynamic_slice_in_dim(scale_b, sub_rank * local_width, local_width, 0)
    per_head_term = jnp.einsum(
        "rhd,hdf->rhf", head_rows_in, head_weights, preferred_element_type=jnp.float32
    )
    clipped = jnp.clip(per_head_term / local_a[None, None, :], -127.0, 127.0).sum(1)

    piece_cols = local_width // tp_count
    pieces = jnp.moveaxis(clipped.reshape(steps_n * samples, tp_count, piece_cols), 1, 0)
    got_pieces = _exchange(pieces, "tp", tp_count)
    summed = got_pieces.sum(0)
    piece_start = sub_rank * local_width + tp_rank * piece_cols
    piece_a = lax.dynamic_slice_in_dim(scale_a, piece_start, piece_cols, 0)
    piece_b = lax.dynamic_slice_in_dim(scale_b, piece_start, piece_cols, 0)
    levels = jnp.clip(summed * piece_a / piece_b, -127.0, 127.0).astype(jnp.bfloat16)
    level_blocks = _gather_blocks(levels, "tp", tp_count)
    all_levels = jnp.moveaxis(level_blocks, 0, 1).reshape(steps_n * samples, local_width)
    restored = all_levels.astype(jnp.float32) * local_b
    hidden = residual.reshape(steps_n * samples, local_width).astype(jnp.float32) + restored
    return hidden.astype(jnp.bfloat16).reshape(steps_n, samples, local_width)


def solution(mesh):
    return jax.shard_map(
        per_device,
        mesh=mesh,
        in_specs=(
            P(None, ("rep", "sub"), "tp"),
            P(None, ("rep", "tp"), None),
            P(None, ("rep", "sub"), "tp", None),
            P(("rep", "sub")),
            P(None, None, ("rep", "sub"), None),
            P("tp", "sub"),
            P(),
            P(),
            P(None, "rep", "sub"),
        ),
        out_specs=P(None, "rep", "sub"),
        check_vma=False,
    )
```

```python
import math

import jax
import jax.numpy as jnp
from jax import lax
from jax.experimental import pallas as pl
from jax.experimental.pallas import tpu as pltpu
from jax.sharding import PartitionSpec as P

DH = 128


NEG_FILL = -1e30


def _is_pow2(n):
    return n >= 1 and (n & (n - 1)) == 0


def _gather_blocks(x, axis_name, count):
    if count == 1:
        return x[None]
    if not _is_pow2(count):
        return lax.all_gather(x, axis_name, axis=0, tiled=False)
    me = lax.axis_index(axis_name)
    if count <= 8:
        other = lax.ppermute(x, axis_name, [(i, i ^ 1) for i in range(count)])
        low = me % 2 == 0
        pair = jnp.where(low, jnp.stack([x, other]), jnp.stack([other, x]))
        pairs = [pair]
        for d in range(1, count // 2):
            pairs.append(
                lax.ppermute(pair, axis_name, [(i, (i + 2 * d) % count) for i in range(count)])
            )
        order = (me // 2 - jnp.arange(count // 2)) % (count // 2)
        placed = jnp.zeros((count // 2,) + pair.shape, pair.dtype).at[order].set(jnp.stack(pairs))
        return placed.reshape((count,) + x.shape)
    cur = x[None]
    k = 1
    while k < count:
        other = lax.ppermute(cur, axis_name, [(i, i ^ k) for i in range(count)])
        low = (me // k) % 2 == 0
        cur = jnp.where(low, jnp.concatenate([cur, other]), jnp.concatenate([other, cur]))
        k *= 2
    return cur


def _two_stage(blocks, axis_name, count, reduce):
    me = lax.axis_index(axis_name)
    half = count // 2
    by_parity = blocks.reshape((half, 2) + blocks.shape[1:])
    mine = lax.dynamic_index_in_dim(by_parity, me % 2, 1, keepdims=False)
    theirs = lax.dynamic_index_in_dim(by_parity, 1 - me % 2, 1, keepdims=False)
    got = lax.ppermute(theirs, axis_name, [(i, i ^ 1) for i in range(count)])
    if reduce:
        held = mine + got
    else:
        held = jnp.stack([mine, got], axis=1)
    out = [lax.dynamic_index_in_dim(held, me // 2, 0, keepdims=False)]
    for d in range(1, half):
        send = lax.dynamic_index_in_dim(held, ((me + 2 * d) % count) // 2, 0, keepdims=False)
        out.append(lax.ppermute(send, axis_name, [(i, (i + 2 * d) % count) for i in range(count)]))
    if reduce:
        return sum(out)
    return jnp.stack(out).reshape(blocks.shape)


def _exchange(blocks, axis_name, count, direct_max=8):
    if count == 1:
        return blocks
    if count > direct_max:
        return jax.tree.map(
            lambda b: lax.all_to_all(b, axis_name, split_axis=0, concat_axis=0, tiled=True), blocks
        )
    me = lax.axis_index(axis_name)
    got = [jax.tree.map(lambda b: lax.dynamic_index_in_dim(b, me, 0, keepdims=False), blocks)]
    for k in range(1, count):
        dst = (me + k) % count
        send = jax.tree.map(lambda b: lax.dynamic_index_in_dim(b, dst, 0, keepdims=False), blocks)
        got.append(lax.ppermute(send, axis_name, [(i, (i + k) % count) for i in range(count)]))
    return jax.tree.map(lambda *xs: jnp.stack(xs), *got)


def _attend_kernel(q_ref, k_ref, v_ref, tk_ref, tv_ref, valid_ref, numer_ref, peak_ref, mass_ref):
    rows_n = q_ref.shape[1]
    samples = tk_ref.shape[1]
    per_sample = rows_n // samples
    score_scale = 1.0 / math.sqrt(DH)
    dims_nt = (((1,), (1,)), ((), ()))
    q = q_ref[0]
    p_scores = lax.dot_general(q, k_ref[0], dims_nt, preferred_element_type=jnp.float32)
    p_scores = p_scores * score_scale
    t_parts = []
    for r in range(samples):
        qr = q[r * per_sample:(r + 1) * per_sample]
        sr = lax.dot_general(qr, tk_ref[0, r], dims_nt, preferred_element_type=jnp.float32)
        sr = sr * score_scale
        t_parts.append(jnp.where(valid_ref[r:r + 1, :] > 0.0, sr, NEG_FILL))
    t_scores = jnp.concatenate(t_parts, axis=0)
    peak = jnp.maximum(
        jnp.max(p_scores, axis=1, keepdims=True), jnp.max(t_scores, axis=1, keepdims=True)
    )
    p_w = jnp.exp(p_scores - peak)
    t_w = jnp.exp(t_scores - peak)
    mass = jnp.sum(p_w, axis=1, keepdims=True) + jnp.sum(t_w, axis=1, keepdims=True)
    numer = jnp.dot(p_w.astype(jnp.bfloat16), v_ref[0], preferred_element_type=jnp.float32)
    t_w16 = t_w.astype(jnp.bfloat16)
    t_numer = [
        jnp.dot(
            t_w16[r * per_sample:(r + 1) * per_sample], tv_ref[0, r],
            preferred_element_type=jnp.float32,
        )
        for r in range(samples)
    ]
    numer_ref[0] = numer + jnp.concatenate(t_numer, axis=0)
    peak_ref[0] = jnp.broadcast_to(peak, peak_ref.shape[1:])
    mass_ref[0] = jnp.broadcast_to(mass, mass_ref.shape[1:])


def _attend_local(q_rows, prefix_kv, tail_kv, valid):
    kv_heads, rows_n, _ = q_rows.shape
    prefix_dev = prefix_kv.shape[1]
    samples, tail_dev = tail_kv.shape[1], tail_kv.shape[2]
    flops = 4 * kv_heads * rows_n * DH * (prefix_dev + tail_dev)
    bytes_in = 2 * (prefix_kv.size + tail_kv.size + q_rows.size)
    return pl.pallas_call(
        _attend_kernel,
        grid=(kv_heads,),
        in_specs=[
            pl.BlockSpec((1, rows_n, DH), lambda k: (k, 0, 0)),
            pl.BlockSpec((1, prefix_dev, DH), lambda k: (0, 0, k)),
            pl.BlockSpec((1, prefix_dev, DH), lambda k: (1, 0, k)),
            pl.BlockSpec((1, samples, tail_dev, DH), lambda k: (0, 0, 0, k)),
            pl.BlockSpec((1, samples, tail_dev, DH), lambda k: (1, 0, 0, k)),
            pl.BlockSpec((samples, tail_dev), lambda k: (0, 0)),
        ],
        out_specs=[
            pl.BlockSpec((1, rows_n, DH), lambda k: (k, 0, 0)),
            pl.BlockSpec((1, rows_n, DH), lambda k: (k, 0, 0)),
            pl.BlockSpec((1, rows_n, DH), lambda k: (k, 0, 0)),
        ],
        out_shape=[jax.ShapeDtypeStruct((kv_heads, rows_n, DH), jnp.float32)] * 3,
        cost_estimate=pl.CostEstimate(
            flops=flops,
            transcendentals=kv_heads * rows_n * (prefix_dev + tail_dev),
            bytes_accessed=bytes_in + 3 * 4 * kv_heads * rows_n * DH,
        ),
    )(q_rows, prefix_kv, prefix_kv, tail_kv, tail_kv, valid)


def per_device(
    queries, prefix_kv, tail_kv, tail_lengths, fresh_kv, out_weight, scale_in, scale_out, residual
):
    steps_n, rows_dev, width_dev = queries.shape
    heads_dev = width_dev // DH
    tp_count = lax.axis_size("tp")
    tp_rank = lax.axis_index("tp")
    sub_rank = lax.axis_index("sub")
    kv_heads = prefix_kv.shape[2] // DH
    heads_all = heads_dev * tp_count
    group = heads_all // kv_heads
    prefix_dev = prefix_kv.shape[1]
    tail_dev = tail_kv.shape[2]
    score_scale = 1.0 / math.sqrt(DH)

    q_blocks = _gather_blocks(queries, "tp", tp_count)
    q_all = jnp.moveaxis(q_blocks, 0, 2).reshape(steps_n, rows_dev, kv_heads, group, DH)
    q_rows = jnp.transpose(q_all, (2, 1, 0, 3, 4)).reshape(kv_heads, -1, DH)
    t_pos = tp_rank * tail_dev + jnp.arange(tail_dev)
    valid = (t_pos[None, :] < tail_lengths[:, None]).astype(jnp.float32)
    k_numer, k_peak, k_mass = _attend_local(q_rows, prefix_kv, tail_kv, valid)

    def by_owner(x):
        x = jnp.transpose(x, (2, 1, 0, 3) + tuple(range(4, x.ndim)))
        x = x.reshape((steps_n, rows_dev, tp_count, heads_dev) + x.shape[4:])
        return jnp.moveaxis(x, 2, 0)

    grid4 = (kv_heads, rows_dev, steps_n, group)
    o_numer = by_owner(k_numer.reshape(grid4 + (DH,))).reshape(tp_count, -1, DH)
    o_peak = by_owner(k_peak[..., 0].reshape(grid4)).reshape(tp_count, -1)
    o_mass = by_owner(k_mass[..., 0].reshape(grid4)).reshape(tp_count, -1)
    n_rows = steps_n * rows_dev * heads_dev
    n_stat = -(-2 * n_rows // DH)
    stats = jnp.concatenate([o_peak, o_mass], axis=1)
    stats = jnp.pad(stats, ((0, 0), (0, n_stat * DH - 2 * n_rows))).reshape(tp_count, n_stat, DH)
    packed = jnp.concatenate([o_numer, stats], axis=1)
    if 2 <= tp_count <= 8 and tp_count % 2 == 0:
        got = _two_stage(packed, "tp", tp_count, reduce=False)
    else:
        got = _exchange(packed, "tp", tp_count)
    got_numer = got[:, :n_rows].reshape(tp_count, steps_n, rows_dev, heads_dev, DH)
    got_stats = got[:, n_rows:].reshape(tp_count, -1)[:, : 2 * n_rows]
    got_stats = got_stats.reshape(tp_count, 2, steps_n, rows_dev, heads_dev)
    got_peak = got_stats[:, 0]
    got_mass = got_stats[:, 1]

    own_query = queries.reshape(steps_n, rows_dev, heads_dev, DH)
    f_kv = fresh_kv.reshape(2, steps_n, rows_dev, kv_heads, DH)
    if group % heads_dev == 0:
        one_kv = lax.dynamic_index_in_dim(f_kv, tp_rank * heads_dev // group, 3, keepdims=True)
        f_kv = jnp.broadcast_to(one_kv, (2, steps_n, rows_dev, heads_dev, DH))
    else:
        kv_of_head = (tp_rank * heads_dev + jnp.arange(heads_dev)) // group
        f_kv = jnp.take(f_kv, kv_of_head, axis=3)
    f_scores = (
        jnp.einsum("sbhd,ubhd->sbhu", own_query, f_kv[0], preferred_element_type=jnp.float32)
        * score_scale
    )
    fresh_live = jnp.arange(steps_n)[None, :] <= jnp.arange(steps_n)[:, None]
    f_scores = jnp.where(fresh_live[:, None, None, :], f_scores, NEG_FILL)

    peak = jnp.maximum(got_peak.max(0), f_scores.max(-1))
    rescale = jnp.exp(got_peak - peak[None])
    f_w = jnp.exp(f_scores - peak[..., None])
    mass = (got_mass * rescale).sum(0) + f_w.sum(-1)
    numer = (got_numer * rescale[..., None]).sum(0)
    numer = numer + jnp.einsum(
        "sbhu,ubhd->sbhd", f_w.astype(jnp.bfloat16), f_kv[1], preferred_element_type=jnp.float32
    )
    attended = (numer / mass[..., None]).astype(jnp.bfloat16).reshape(steps_n, rows_dev, width_dev)

    gathered = lax.all_gather(attended, "sub", axis=1, tiled=True)
    samples = gathered.shape[1]
    local_width = out_weight.shape[1]
    head_rows_in = gathered.reshape(steps_n * samples, heads_dev, DH)
    head_weights = out_weight.reshape(heads_dev, DH, local_width)
    scale_a = jnp.repeat(jnp.exp2(-scale_in.astype(jnp.float32)), 128)
    scale_b = jnp.repeat(jnp.exp2(-scale_out.astype(jnp.float32)), 128)
    local_a = lax.dynamic_slice_in_dim(scale_a, sub_rank * local_width, local_width, 0)
    local_b = lax.dynamic_slice_in_dim(scale_b, sub_rank * local_width, local_width, 0)
    per_head_term = jnp.einsum(
        "rhd,hdf->rhf", head_rows_in, head_weights, preferred_element_type=jnp.float32
    )
    clipped = jnp.clip(per_head_term / local_a[None, None, :], -127.0, 127.0).sum(1)

    piece_cols = local_width // tp_count
    pieces = jnp.moveaxis(clipped.reshape(steps_n * samples, tp_count, piece_cols), 1, 0)
    if 2 <= tp_count <= 8 and tp_count % 2 == 0:
        summed = _two_stage(pieces, "tp", tp_count, reduce=True)
    else:
        summed = _exchange(pieces, "tp", tp_count).sum(0)
    piece_start = sub_rank * local_width + tp_rank * piece_cols
    piece_a = lax.dynamic_slice_in_dim(scale_a, piece_start, piece_cols, 0)
    piece_b = lax.dynamic_slice_in_dim(scale_b, piece_start, piece_cols, 0)
    levels = jnp.clip(summed * piece_a / piece_b, -127.0, 127.0).astype(jnp.bfloat16)
    level_blocks = _gather_blocks(levels, "tp", tp_count)
    all_levels = jnp.moveaxis(level_blocks, 0, 1).reshape(steps_n * samples, local_width)
    restored = all_levels.astype(jnp.float32) * local_b
    hidden = residual.reshape(steps_n * samples, local_width).astype(jnp.float32) + restored
    return hidden.astype(jnp.bfloat16).reshape(steps_n, samples, local_width)


def solution(mesh):
    return jax.shard_map(
        per_device,
        mesh=mesh,
        in_specs=(
            P(None, ("rep", "sub"), "tp"),
            P(None, ("rep", "tp"), None),
            P(None, ("rep", "sub"), "tp", None),
            P(("rep", "sub")),
            P(None, None, ("rep", "sub"), None),
            P("tp", "sub"),
            P(),
            P(),
            P(None, "rep", "sub"),
        ),
        out_specs=P(None, "rep", "sub"),
        check_vma=False,
    )
```

```python
import math

import jax
import jax.numpy as jnp
from jax import lax
from jax.experimental import pallas as pl
from jax.experimental.pallas import tpu as pltpu
from jax.sharding import PartitionSpec as P

DH = 128


NEG_FILL = -1e30


def _is_pow2(n):
    return n >= 1 and (n & (n - 1)) == 0


def _gather_blocks(x, axis_name, count):
    if count == 1:
        return x[None]
    if not _is_pow2(count):
        return lax.all_gather(x, axis_name, axis=0, tiled=False)
    me = lax.axis_index(axis_name)
    if count <= 8:
        other = lax.ppermute(x, axis_name, [(i, i ^ 1) for i in range(count)])
        low = me % 2 == 0
        pair = jnp.where(low, jnp.stack([x, other]), jnp.stack([other, x]))
        pairs = [pair]
        for d in range(1, count // 2):
            pairs.append(
                lax.ppermute(pair, axis_name, [(i, (i + 2 * d) % count) for i in range(count)])
            )
        order = (me // 2 - jnp.arange(count // 2)) % (count // 2)
        placed = jnp.zeros((count // 2,) + pair.shape, pair.dtype).at[order].set(jnp.stack(pairs))
        return placed.reshape((count,) + x.shape)
    cur = x[None]
    k = 1
    while k < count:
        other = lax.ppermute(cur, axis_name, [(i, i ^ k) for i in range(count)])
        low = (me // k) % 2 == 0
        cur = jnp.where(low, jnp.concatenate([cur, other]), jnp.concatenate([other, cur]))
        k *= 2
    return cur


def _exchange(blocks, axis_name, count, direct_max=8):
    if count == 1:
        return blocks
    if count > direct_max:
        return jax.tree.map(
            lambda b: lax.all_to_all(b, axis_name, split_axis=0, concat_axis=0, tiled=True), blocks
        )
    me = lax.axis_index(axis_name)
    got = [jax.tree.map(lambda b: lax.dynamic_index_in_dim(b, me, 0, keepdims=False), blocks)]
    for k in range(1, count):
        dst = (me + k) % count
        send = jax.tree.map(lambda b: lax.dynamic_index_in_dim(b, dst, 0, keepdims=False), blocks)
        got.append(lax.ppermute(send, axis_name, [(i, (i + k) % count) for i in range(count)]))
    return jax.tree.map(lambda *xs: jnp.stack(xs), *got)


def _attend_kernel(q_ref, k_ref, v_ref, tk_ref, tv_ref, valid_ref, numer_ref, peak_ref, mass_ref):
    heads_n, rows_n = q_ref.shape[0], q_ref.shape[1]
    samples = tk_ref.shape[1]
    per_sample = rows_n // samples
    score_scale = 1.0 / math.sqrt(DH)
    dims_nt = (((1,), (1,)), ((), ()))
    for j in range(heads_n):
        cols = slice(j * DH, (j + 1) * DH)
        q = q_ref[j]
        p_scores = lax.dot_general(q, k_ref[0, :, cols], dims_nt, preferred_element_type=jnp.float32)
        p_scores = p_scores * score_scale
        t_parts = []
        for r in range(samples):
            qr = q[r * per_sample:(r + 1) * per_sample]
            sr = lax.dot_general(
                qr, tk_ref[0, r, :, cols], dims_nt, preferred_element_type=jnp.float32
            )
            sr = sr * score_scale
            t_parts.append(jnp.where(valid_ref[r:r + 1, :] > 0.0, sr, NEG_FILL))
        t_scores = jnp.concatenate(t_parts, axis=0)
        peak = jnp.maximum(
            jnp.max(p_scores, axis=1, keepdims=True), jnp.max(t_scores, axis=1, keepdims=True)
        )
        p_w = jnp.exp(p_scores - peak)
        t_w = jnp.exp(t_scores - peak)
        mass = jnp.sum(p_w, axis=1, keepdims=True) + jnp.sum(t_w, axis=1, keepdims=True)
        numer = jnp.dot(
            p_w.astype(jnp.bfloat16), v_ref[0, :, cols], preferred_element_type=jnp.float32
        )
        t_w16 = t_w.astype(jnp.bfloat16)
        t_numer = [
            jnp.dot(
                t_w16[r * per_sample:(r + 1) * per_sample], tv_ref[0, r, :, cols],
                preferred_element_type=jnp.float32,
            )
            for r in range(samples)
        ]
        numer_ref[j] = numer + jnp.concatenate(t_numer, axis=0)
        peak_ref[j] = jnp.broadcast_to(peak, peak_ref.shape[1:])
        mass_ref[j] = jnp.broadcast_to(mass, mass_ref.shape[1:])


def _attend_local(q_rows, prefix_kv, tail_kv, valid):
    kv_heads, rows_n, _ = q_rows.shape
    prefix_dev = prefix_kv.shape[1]
    samples, tail_dev = tail_kv.shape[1], tail_kv.shape[2]
    flops = 4 * kv_heads * rows_n * DH * (prefix_dev + tail_dev)
    bytes_in = 2 * (prefix_kv.size + tail_kv.size + q_rows.size)
    per_step = 4 if kv_heads % 4 == 0 else 1
    width = per_step * DH
    return pl.pallas_call(
        _attend_kernel,
        grid=(kv_heads // per_step,),
        in_specs=[
            pl.BlockSpec((per_step, rows_n, DH), lambda k: (k, 0, 0)),
            pl.BlockSpec((1, prefix_dev, width), lambda k: (0, 0, k)),
            pl.BlockSpec((1, prefix_dev, width), lambda k: (1, 0, k)),
            pl.BlockSpec((1, samples, tail_dev, width), lambda k: (0, 0, 0, k)),
            pl.BlockSpec((1, samples, tail_dev, width), lambda k: (1, 0, 0, k)),
            pl.BlockSpec((samples, tail_dev), lambda k: (0, 0)),
        ],
        out_specs=[
            pl.BlockSpec((per_step, rows_n, DH), lambda k: (k, 0, 0)),
            pl.BlockSpec((per_step, rows_n, DH), lambda k: (k, 0, 0)),
            pl.BlockSpec((per_step, rows_n, DH), lambda k: (k, 0, 0)),
        ],
        out_shape=[jax.ShapeDtypeStruct((kv_heads, rows_n, DH), jnp.float32)] * 3,
        cost_estimate=pl.CostEstimate(
            flops=flops,
            transcendentals=kv_heads * rows_n * (prefix_dev + tail_dev),
            bytes_accessed=bytes_in + 3 * 4 * kv_heads * rows_n * DH,
        ),
        compiler_params=pltpu.CompilerParams(vmem_limit_bytes=48 * 1024 * 1024),
    )(q_rows, prefix_kv, prefix_kv, tail_kv, tail_kv, valid)


def per_device(
    queries, prefix_kv, tail_kv, tail_lengths, fresh_kv, out_weight, scale_in, scale_out, residual
):
    steps_n, rows_dev, width_dev = queries.shape
    heads_dev = width_dev // DH
    tp_count = lax.axis_size("tp")
    tp_rank = lax.axis_index("tp")
    sub_rank = lax.axis_index("sub")
    kv_heads = prefix_kv.shape[2] // DH
    heads_all = heads_dev * tp_count
    group = heads_all // kv_heads
    prefix_dev = prefix_kv.shape[1]
    tail_dev = tail_kv.shape[2]
    score_scale = 1.0 / math.sqrt(DH)

    q_blocks = _gather_blocks(queries, "tp", tp_count)
    q_all = jnp.moveaxis(q_blocks, 0, 2).reshape(steps_n, rows_dev, kv_heads, group, DH)
    q_rows = jnp.transpose(q_all, (2, 1, 0, 3, 4)).reshape(kv_heads, -1, DH)
    t_pos = tp_rank * tail_dev + jnp.arange(tail_dev)
    valid = (t_pos[None, :] < tail_lengths[:, None]).astype(jnp.float32)
    k_numer, k_peak, k_mass = _attend_local(q_rows, prefix_kv, tail_kv, valid)

    def by_owner(x):
        x = jnp.transpose(x, (2, 1, 0, 3) + tuple(range(4, x.ndim)))
        x = x.reshape((steps_n, rows_dev, tp_count, heads_dev) + x.shape[4:])
        return jnp.moveaxis(x, 2, 0)

    grid4 = (kv_heads, rows_dev, steps_n, group)
    o_numer = by_owner(k_numer.reshape(grid4 + (DH,))).reshape(tp_count, -1, DH)
    o_peak = by_owner(k_peak[..., 0].reshape(grid4)).reshape(tp_count, -1)
    o_mass = by_owner(k_mass[..., 0].reshape(grid4)).reshape(tp_count, -1)
    n_rows = steps_n * rows_dev * heads_dev
    n_stat = -(-2 * n_rows // DH)
    stats = jnp.concatenate([o_peak, o_mass], axis=1)
    stats = jnp.pad(stats, ((0, 0), (0, n_stat * DH - 2 * n_rows))).reshape(tp_count, n_stat, DH)
    got = _exchange(jnp.concatenate([o_numer, stats], axis=1), "tp", tp_count)
    got_numer = got[:, :n_rows].reshape(tp_count, steps_n, rows_dev, heads_dev, DH)
    got_stats = got[:, n_rows:].reshape(tp_count, -1)[:, : 2 * n_rows]
    got_stats = got_stats.reshape(tp_count, 2, steps_n, rows_dev, heads_dev)
    got_peak = got_stats[:, 0]
    got_mass = got_stats[:, 1]

    own_query = queries.reshape(steps_n, rows_dev, heads_dev, DH)
    f_kv = fresh_kv.reshape(2, steps_n, rows_dev, kv_heads, DH)
    if group % heads_dev == 0:
        one_kv = lax.dynamic_index_in_dim(f_kv, tp_rank * heads_dev // group, 3, keepdims=True)
        f_kv = jnp.broadcast_to(one_kv, (2, steps_n, rows_dev, heads_dev, DH))
    else:
        kv_of_head = (tp_rank * heads_dev + jnp.arange(heads_dev)) // group
        f_kv = jnp.take(f_kv, kv_of_head, axis=3)
    f_scores = (
        jnp.einsum("sbhd,ubhd->sbhu", own_query, f_kv[0], preferred_element_type=jnp.float32)
        * score_scale
    )
    fresh_live = jnp.arange(steps_n)[None, :] <= jnp.arange(steps_n)[:, None]
    f_scores = jnp.where(fresh_live[:, None, None, :], f_scores, NEG_FILL)

    peak = jnp.maximum(got_peak.max(0), f_scores.max(-1))
    rescale = jnp.exp(got_peak - peak[None])
    f_w = jnp.exp(f_scores - peak[..., None])
    mass = (got_mass * rescale).sum(0) + f_w.sum(-1)
    numer = (got_numer * rescale[..., None]).sum(0)
    numer = numer + jnp.einsum(
        "sbhu,ubhd->sbhd", f_w.astype(jnp.bfloat16), f_kv[1], preferred_element_type=jnp.float32
    )
    attended = (numer / mass[..., None]).astype(jnp.bfloat16).reshape(steps_n, rows_dev, width_dev)

    gathered = lax.all_gather(attended, "sub", axis=1, tiled=True)
    samples = gathered.shape[1]
    local_width = out_weight.shape[1]
    head_rows_in = gathered.reshape(steps_n * samples, heads_dev, DH)
    head_weights = out_weight.reshape(heads_dev, DH, local_width)
    scale_a = jnp.repeat(jnp.exp2(-scale_in.astype(jnp.float32)), 128)
    scale_b = jnp.repeat(jnp.exp2(-scale_out.astype(jnp.float32)), 128)
    local_a = lax.dynamic_slice_in_dim(scale_a, sub_rank * local_width, local_width, 0)
    local_b = lax.dynamic_slice_in_dim(scale_b, sub_rank * local_width, local_width, 0)
    per_head_term = jnp.einsum(
        "rhd,hdf->rhf", head_rows_in, head_weights, preferred_element_type=jnp.float32
    )
    clipped = jnp.clip(per_head_term / local_a[None, None, :], -127.0, 127.0).sum(1)

    piece_cols = local_width // tp_count
    pieces = jnp.moveaxis(clipped.reshape(steps_n * samples, tp_count, piece_cols), 1, 0)
    got_pieces = _exchange(pieces, "tp", tp_count)
    summed = got_pieces.sum(0)
    piece_start = sub_rank * local_width + tp_rank * piece_cols
    piece_a = lax.dynamic_slice_in_dim(scale_a, piece_start, piece_cols, 0)
    piece_b = lax.dynamic_slice_in_dim(scale_b, piece_start, piece_cols, 0)
    levels = jnp.clip(summed * piece_a / piece_b, -127.0, 127.0).astype(jnp.bfloat16)
    level_blocks = _gather_blocks(levels, "tp", tp_count)
    all_levels = jnp.moveaxis(level_blocks, 0, 1).reshape(steps_n * samples, local_width)
    restored = all_levels.astype(jnp.float32) * local_b
    hidden = residual.reshape(steps_n * samples, local_width).astype(jnp.float32) + restored
    return hidden.astype(jnp.bfloat16).reshape(steps_n, samples, local_width)


def solution(mesh):
    return jax.shard_map(
        per_device,
        mesh=mesh,
        in_specs=(
            P(None, ("rep", "sub"), "tp"),
            P(None, ("rep", "tp"), None),
            P(None, ("rep", "sub"), "tp", None),
            P(("rep", "sub")),
            P(None, None, ("rep", "sub"), None),
            P("tp", "sub"),
            P(),
            P(),
            P(None, "rep", "sub"),
        ),
        out_specs=P(None, "rep", "sub"),
        check_vma=False,
    )
```

```python
import math

import jax
import jax.numpy as jnp
from jax import lax
from jax.experimental import pallas as pl
from jax.experimental.pallas import tpu as pltpu
from jax.sharding import PartitionSpec as P

DH = 128


NEG_FILL = -1e30


def _is_pow2(n):
    return n >= 1 and (n & (n - 1)) == 0


def _gather_blocks(x, axis_name, count):
    if count == 1:
        return x[None]
    if not _is_pow2(count):
        return lax.all_gather(x, axis_name, axis=0, tiled=False)
    me = lax.axis_index(axis_name)
    if count <= 8:
        other = lax.ppermute(x, axis_name, [(i, i ^ 1) for i in range(count)])
        low = me % 2 == 0
        pair = jnp.where(low, jnp.stack([x, other]), jnp.stack([other, x]))
        pairs = [pair]
        for d in range(1, count // 2):
            pairs.append(
                lax.ppermute(pair, axis_name, [(i, (i + 2 * d) % count) for i in range(count)])
            )
        order = (me // 2 - jnp.arange(count // 2)) % (count // 2)
        placed = jnp.zeros((count // 2,) + pair.shape, pair.dtype).at[order].set(jnp.stack(pairs))
        return placed.reshape((count,) + x.shape)
    cur = x[None]
    k = 1
    while k < count:
        other = lax.ppermute(cur, axis_name, [(i, i ^ k) for i in range(count)])
        low = (me // k) % 2 == 0
        cur = jnp.where(low, jnp.concatenate([cur, other]), jnp.concatenate([other, cur]))
        k *= 2
    return cur


def _exchange(blocks, axis_name, count, direct_max=8):
    if count == 1:
        return blocks
    if count > direct_max:
        return jax.tree.map(
            lambda b: lax.all_to_all(b, axis_name, split_axis=0, concat_axis=0, tiled=True), blocks
        )
    me = lax.axis_index(axis_name)
    got = [jax.tree.map(lambda b: lax.dynamic_index_in_dim(b, me, 0, keepdims=False), blocks)]
    for k in range(count - 1, 0, -1):
        dst = (me + k) % count
        send = jax.tree.map(lambda b: lax.dynamic_index_in_dim(b, dst, 0, keepdims=False), blocks)
        got.append(lax.ppermute(send, axis_name, [(i, (i + k) % count) for i in range(count)]))
    return jax.tree.map(lambda *xs: jnp.stack(xs), *got)


def _attend_kernel(q_ref, k_ref, v_ref, tk_ref, tv_ref, valid_ref, numer_ref, peak_ref, mass_ref):
    heads_n, rows_n = q_ref.shape[0], q_ref.shape[1]
    samples = tk_ref.shape[1]
    per_sample = rows_n // samples
    score_scale = 1.0 / math.sqrt(DH)
    dims_nt = (((1,), (1,)), ((), ()))
    for j in range(heads_n):
        cols = slice(j * DH, (j + 1) * DH)
        q = q_ref[j]
        p_scores = lax.dot_general(q, k_ref[0, :, cols], dims_nt, preferred_element_type=jnp.float32)
        p_scores = p_scores * score_scale
        t_parts = []
        for r in range(samples):
            qr = q[r * per_sample:(r + 1) * per_sample]
            sr = lax.dot_general(
                qr, tk_ref[0, r, :, cols], dims_nt, preferred_element_type=jnp.float32
            )
            sr = sr * score_scale
            t_parts.append(jnp.where(valid_ref[r:r + 1, :] > 0.0, sr, NEG_FILL))
        t_scores = jnp.concatenate(t_parts, axis=0)
        peak = jnp.maximum(
            jnp.max(p_scores, axis=1, keepdims=True), jnp.max(t_scores, axis=1, keepdims=True)
        )
        p_w = jnp.exp(p_scores - peak)
        t_w = jnp.exp(t_scores - peak)
        mass = jnp.sum(p_w, axis=1, keepdims=True) + jnp.sum(t_w, axis=1, keepdims=True)
        numer = jnp.dot(
            p_w.astype(jnp.bfloat16), v_ref[0, :, cols], preferred_element_type=jnp.float32
        )
        t_w16 = t_w.astype(jnp.bfloat16)
        t_numer = [
            jnp.dot(
                t_w16[r * per_sample:(r + 1) * per_sample], tv_ref[0, r, :, cols],
                preferred_element_type=jnp.float32,
            )
            for r in range(samples)
        ]
        numer_ref[j] = numer + jnp.concatenate(t_numer, axis=0)
        peak_ref[j] = jnp.broadcast_to(peak, peak_ref.shape[1:])
        mass_ref[j] = jnp.broadcast_to(mass, mass_ref.shape[1:])


def _attend_local(q_rows, prefix_kv, tail_kv, valid):
    kv_heads, rows_n, _ = q_rows.shape
    prefix_dev = prefix_kv.shape[1]
    samples, tail_dev = tail_kv.shape[1], tail_kv.shape[2]
    flops = 4 * kv_heads * rows_n * DH * (prefix_dev + tail_dev)
    bytes_in = 2 * (prefix_kv.size + tail_kv.size + q_rows.size)
    per_step = 4 if kv_heads % 4 == 0 else 1
    width = per_step * DH
    return pl.pallas_call(
        _attend_kernel,
        grid=(kv_heads // per_step,),
        in_specs=[
            pl.BlockSpec((per_step, rows_n, DH), lambda k: (k, 0, 0)),
            pl.BlockSpec((1, prefix_dev, width), lambda k: (0, 0, k)),
            pl.BlockSpec((1, prefix_dev, width), lambda k: (1, 0, k)),
            pl.BlockSpec((1, samples, tail_dev, width), lambda k: (0, 0, 0, k)),
            pl.BlockSpec((1, samples, tail_dev, width), lambda k: (1, 0, 0, k)),
            pl.BlockSpec((samples, tail_dev), lambda k: (0, 0)),
        ],
        out_specs=[
            pl.BlockSpec((per_step, rows_n, DH), lambda k: (k, 0, 0)),
            pl.BlockSpec((per_step, rows_n, DH), lambda k: (k, 0, 0)),
            pl.BlockSpec((per_step, rows_n, DH), lambda k: (k, 0, 0)),
        ],
        out_shape=[jax.ShapeDtypeStruct((kv_heads, rows_n, DH), jnp.float32)] * 3,
        cost_estimate=pl.CostEstimate(
            flops=flops,
            transcendentals=kv_heads * rows_n * (prefix_dev + tail_dev),
            bytes_accessed=bytes_in + 3 * 4 * kv_heads * rows_n * DH,
        ),
        compiler_params=pltpu.CompilerParams(vmem_limit_bytes=48 * 1024 * 1024),
    )(q_rows, prefix_kv, prefix_kv, tail_kv, tail_kv, valid)


def per_device(
    queries, prefix_kv, tail_kv, tail_lengths, fresh_kv, out_weight, scale_in, scale_out, residual
):
    steps_n, rows_dev, width_dev = queries.shape
    heads_dev = width_dev // DH
    tp_count = lax.axis_size("tp")
    tp_rank = lax.axis_index("tp")
    sub_rank = lax.axis_index("sub")
    kv_heads = prefix_kv.shape[2] // DH
    heads_all = heads_dev * tp_count
    group = heads_all // kv_heads
    prefix_dev = prefix_kv.shape[1]
    tail_dev = tail_kv.shape[2]
    score_scale = 1.0 / math.sqrt(DH)

    q_blocks = _gather_blocks(queries, "tp", tp_count)
    q_all = jnp.moveaxis(q_blocks, 0, 2).reshape(steps_n, rows_dev, kv_heads, group, DH)
    q_rows = jnp.transpose(q_all, (2, 1, 0, 3, 4)).reshape(kv_heads, -1, DH)
    t_pos = tp_rank * tail_dev + jnp.arange(tail_dev)
    valid = (t_pos[None, :] < tail_lengths[:, None]).astype(jnp.float32)
    k_numer, k_peak, k_mass = _attend_local(q_rows, prefix_kv, tail_kv, valid)

    def by_owner(x):
        x = jnp.transpose(x, (2, 1, 0, 3) + tuple(range(4, x.ndim)))
        x = x.reshape((steps_n, rows_dev, tp_count, heads_dev) + x.shape[4:])
        return jnp.moveaxis(x, 2, 0)

    grid4 = (kv_heads, rows_dev, steps_n, group)
    o_numer = by_owner(k_numer.reshape(grid4 + (DH,))).reshape(tp_count, -1, DH)
    o_peak = by_owner(k_peak[..., 0].reshape(grid4)).reshape(tp_count, -1)
    o_mass = by_owner(k_mass[..., 0].reshape(grid4)).reshape(tp_count, -1)
    n_rows = steps_n * rows_dev * heads_dev
    n_stat = -(-2 * n_rows // DH)
    stats = jnp.concatenate([o_peak, o_mass], axis=1)
    stats = jnp.pad(stats, ((0, 0), (0, n_stat * DH - 2 * n_rows))).reshape(tp_count, n_stat, DH)
    got = _exchange(jnp.concatenate([o_numer, stats], axis=1), "tp", tp_count)
    got_numer = got[:, :n_rows].reshape(tp_count, steps_n, rows_dev, heads_dev, DH)
    got_stats = got[:, n_rows:].reshape(tp_count, -1)[:, : 2 * n_rows]
    got_stats = got_stats.reshape(tp_count, 2, steps_n, rows_dev, heads_dev)
    got_peak = got_stats[:, 0]
    got_mass = got_stats[:, 1]

    own_query = queries.reshape(steps_n, rows_dev, heads_dev, DH)
    f_kv = fresh_kv.reshape(2, steps_n, rows_dev, kv_heads, DH)
    if group % heads_dev == 0:
        one_kv = lax.dynamic_index_in_dim(f_kv, tp_rank * heads_dev // group, 3, keepdims=True)
        f_kv = jnp.broadcast_to(one_kv, (2, steps_n, rows_dev, heads_dev, DH))
    else:
        kv_of_head = (tp_rank * heads_dev + jnp.arange(heads_dev)) // group
        f_kv = jnp.take(f_kv, kv_of_head, axis=3)
    f_scores = (
        jnp.einsum("sbhd,ubhd->sbhu", own_query, f_kv[0], preferred_element_type=jnp.float32)
        * score_scale
    )
    fresh_live = jnp.arange(steps_n)[None, :] <= jnp.arange(steps_n)[:, None]
    f_scores = jnp.where(fresh_live[:, None, None, :], f_scores, NEG_FILL)

    peak = jnp.maximum(got_peak.max(0), f_scores.max(-1))
    rescale = jnp.exp(got_peak - peak[None])
    f_w = jnp.exp(f_scores - peak[..., None])
    mass = (got_mass * rescale).sum(0) + f_w.sum(-1)
    numer = (got_numer * rescale[..., None]).sum(0)
    numer = numer + jnp.einsum(
        "sbhu,ubhd->sbhd", f_w.astype(jnp.bfloat16), f_kv[1], preferred_element_type=jnp.float32
    )
    attended = (numer / mass[..., None]).astype(jnp.bfloat16).reshape(steps_n, rows_dev, width_dev)

    gathered = lax.all_gather(attended, "sub", axis=1, tiled=True)
    samples = gathered.shape[1]
    local_width = out_weight.shape[1]
    head_rows_in = gathered.reshape(steps_n * samples, heads_dev, DH)
    head_weights = out_weight.reshape(heads_dev, DH, local_width)
    scale_a = jnp.repeat(jnp.exp2(-scale_in.astype(jnp.float32)), 128)
    scale_b = jnp.repeat(jnp.exp2(-scale_out.astype(jnp.float32)), 128)
    local_a = lax.dynamic_slice_in_dim(scale_a, sub_rank * local_width, local_width, 0)
    local_b = lax.dynamic_slice_in_dim(scale_b, sub_rank * local_width, local_width, 0)
    per_head_term = jnp.einsum(
        "rhd,hdf->rhf", head_rows_in, head_weights, preferred_element_type=jnp.float32
    )
    clipped = jnp.clip(per_head_term / local_a[None, None, :], -127.0, 127.0).sum(1)

    piece_cols = local_width // tp_count
    pieces = jnp.moveaxis(clipped.reshape(steps_n * samples, tp_count, piece_cols), 1, 0)
    got_pieces = _exchange(pieces, "tp", tp_count)
    summed = got_pieces.sum(0)
    piece_start = sub_rank * local_width + tp_rank * piece_cols
    piece_a = lax.dynamic_slice_in_dim(scale_a, piece_start, piece_cols, 0)
    piece_b = lax.dynamic_slice_in_dim(scale_b, piece_start, piece_cols, 0)
    levels = jnp.clip(summed * piece_a / piece_b, -127.0, 127.0).astype(jnp.bfloat16)
    level_blocks = _gather_blocks(levels, "tp", tp_count)
    all_levels = jnp.moveaxis(level_blocks, 0, 1).reshape(steps_n * samples, local_width)
    restored = all_levels.astype(jnp.float32) * local_b
    hidden = residual.reshape(steps_n * samples, local_width).astype(jnp.float32) + restored
    return hidden.astype(jnp.bfloat16).reshape(steps_n, samples, local_width)


def solution(mesh):
    return jax.shard_map(
        per_device,
        mesh=mesh,
        in_specs=(
            P(None, ("rep", "sub"), "tp"),
            P(None, ("rep", "tp"), None),
            P(None, ("rep", "sub"), "tp", None),
            P(("rep", "sub")),
            P(None, None, ("rep", "sub"), None),
            P("tp", "sub"),
            P(),
            P(),
            P(None, "rep", "sub"),
        ),
        out_specs=P(None, "rep", "sub"),
        check_vma=False,
    )
```

```python
import math

import jax
import jax.numpy as jnp
from jax import lax
from jax.experimental import pallas as pl
from jax.experimental.pallas import tpu as pltpu
from jax.sharding import PartitionSpec as P

DH = 128


NEG_FILL = -1e30


def _is_pow2(n):
    return n >= 1 and (n & (n - 1)) == 0


def _gather_blocks(x, axis_name, count):
    if count == 1:
        return x[None]
    if not _is_pow2(count):
        return lax.all_gather(x, axis_name, axis=0, tiled=False)
    me = lax.axis_index(axis_name)
    if count <= 8:
        other = lax.ppermute(x, axis_name, [(i, i ^ 1) for i in range(count)])
        low = me % 2 == 0
        pair = jnp.where(low, jnp.stack([x, other]), jnp.stack([other, x]))
        pairs = [pair]
        for d in range(1, count // 2):
            pairs.append(
                lax.ppermute(pair, axis_name, [(i, (i + 2 * d) % count) for i in range(count)])
            )
        order = (me // 2 - jnp.arange(count // 2)) % (count // 2)
        placed = jnp.zeros((count // 2,) + pair.shape, pair.dtype).at[order].set(jnp.stack(pairs))
        return placed.reshape((count,) + x.shape)
    cur = x[None]
    k = 1
    while k < count:
        other = lax.ppermute(cur, axis_name, [(i, i ^ k) for i in range(count)])
        low = (me // k) % 2 == 0
        cur = jnp.where(low, jnp.concatenate([cur, other]), jnp.concatenate([other, cur]))
        k *= 2
    return cur


def _exchange(blocks, axis_name, count, direct_max=8):
    if count == 1:
        return blocks
    if count > direct_max:
        return jax.tree.map(
            lambda b: lax.all_to_all(b, axis_name, split_axis=0, concat_axis=0, tiled=True), blocks
        )
    me = lax.axis_index(axis_name)
    got = [jax.tree.map(lambda b: lax.dynamic_index_in_dim(b, me, 0, keepdims=False), blocks)]
    for k in range(1, count):
        dst = (me + k) % count
        send = jax.tree.map(lambda b: lax.dynamic_index_in_dim(b, dst, 0, keepdims=False), blocks)
        got.append(lax.ppermute(send, axis_name, [(i, (i + k) % count) for i in range(count)]))
    return jax.tree.map(lambda *xs: jnp.stack(xs), *got)


def _attend_kernel(q_ref, k_ref, v_ref, tk_ref, tv_ref, valid_ref, numer_ref, peak_ref, mass_ref):
    heads_n, rows_n = q_ref.shape[0], q_ref.shape[1]
    samples = tk_ref.shape[1]
    per_sample = rows_n // samples
    score_scale = 1.0 / math.sqrt(DH)
    dims_nt = (((1,), (1,)), ((), ()))
    for j in range(heads_n):
        cols = slice(j * DH, (j + 1) * DH)
        q = q_ref[j]
        p_scores = lax.dot_general(q, k_ref[0, :, cols], dims_nt, preferred_element_type=jnp.float32)
        p_scores = p_scores * score_scale
        t_parts = []
        for r in range(samples):
            qr = q[r * per_sample:(r + 1) * per_sample]
            sr = lax.dot_general(
                qr, tk_ref[0, r, :, cols], dims_nt, preferred_element_type=jnp.float32
            )
            sr = sr * score_scale
            t_parts.append(jnp.where(valid_ref[r:r + 1, :] > 0.0, sr, NEG_FILL))
        t_scores = jnp.concatenate(t_parts, axis=0)
        peak = jnp.maximum(
            jnp.max(p_scores, axis=1, keepdims=True), jnp.max(t_scores, axis=1, keepdims=True)
        )
        p_w = jnp.exp(p_scores - peak)
        t_w = jnp.exp(t_scores - peak)
        mass = jnp.sum(p_w, axis=1, keepdims=True) + jnp.sum(t_w, axis=1, keepdims=True)
        numer = jnp.dot(
            p_w.astype(jnp.bfloat16), v_ref[0, :, cols], preferred_element_type=jnp.float32
        )
        t_w16 = t_w.astype(jnp.bfloat16)
        t_numer = [
            jnp.dot(
                t_w16[r * per_sample:(r + 1) * per_sample], tv_ref[0, r, :, cols],
                preferred_element_type=jnp.float32,
            )
            for r in range(samples)
        ]
        numer_ref[j] = numer + jnp.concatenate(t_numer, axis=0)
        peak_ref[j] = jnp.broadcast_to(peak, peak_ref.shape[1:])
        mass_ref[j] = jnp.broadcast_to(mass, mass_ref.shape[1:])


def _attend_local(q_rows, prefix_kv, tail_kv, valid):
    kv_heads, rows_n, _ = q_rows.shape
    prefix_dev = prefix_kv.shape[1]
    samples, tail_dev = tail_kv.shape[1], tail_kv.shape[2]
    flops = 4 * kv_heads * rows_n * DH * (prefix_dev + tail_dev)
    bytes_in = 2 * (prefix_kv.size + tail_kv.size + q_rows.size)
    per_step = 4 if kv_heads % 4 == 0 else 1
    width = per_step * DH
    return pl.pallas_call(
        _attend_kernel,
        grid=(kv_heads // per_step,),
        in_specs=[
            pl.BlockSpec((per_step, rows_n, DH), lambda k: (k, 0, 0)),
            pl.BlockSpec((1, prefix_dev, width), lambda k: (0, 0, k)),
            pl.BlockSpec((1, prefix_dev, width), lambda k: (1, 0, k)),
            pl.BlockSpec((1, samples, tail_dev, width), lambda k: (0, 0, 0, k)),
            pl.BlockSpec((1, samples, tail_dev, width), lambda k: (1, 0, 0, k)),
            pl.BlockSpec((samples, tail_dev), lambda k: (0, 0)),
        ],
        out_specs=[
            pl.BlockSpec((per_step, rows_n, DH), lambda k: (k, 0, 0)),
            pl.BlockSpec((per_step, rows_n, DH), lambda k: (k, 0, 0)),
            pl.BlockSpec((per_step, rows_n, DH), lambda k: (k, 0, 0)),
        ],
        out_shape=[jax.ShapeDtypeStruct((kv_heads, rows_n, DH), jnp.float32)] * 3,
        cost_estimate=pl.CostEstimate(
            flops=flops,
            transcendentals=kv_heads * rows_n * (prefix_dev + tail_dev),
            bytes_accessed=bytes_in + 3 * 4 * kv_heads * rows_n * DH,
        ),
        compiler_params=pltpu.CompilerParams(vmem_limit_bytes=48 * 1024 * 1024),
    )(q_rows, prefix_kv, prefix_kv, tail_kv, tail_kv, valid)


def per_device(
    queries, prefix_kv, tail_kv, tail_lengths, fresh_kv, out_weight, scale_in, scale_out, residual
):
    steps_n, rows_dev, width_dev = queries.shape
    heads_dev = width_dev // DH
    tp_count = lax.axis_size("tp")
    tp_rank = lax.axis_index("tp")
    sub_rank = lax.axis_index("sub")
    kv_heads = prefix_kv.shape[2] // DH
    heads_all = heads_dev * tp_count
    group = heads_all // kv_heads
    prefix_dev = prefix_kv.shape[1]
    tail_dev = tail_kv.shape[2]
    score_scale = 1.0 / math.sqrt(DH)

    q_blocks = _gather_blocks(queries, "tp", tp_count)
    q_all = jnp.moveaxis(q_blocks, 0, 2).reshape(steps_n, rows_dev, kv_heads, group, DH)
    q_rows = jnp.transpose(q_all, (2, 1, 0, 3, 4)).reshape(kv_heads, -1, DH)
    t_pos = tp_rank * tail_dev + jnp.arange(tail_dev)
    valid = (t_pos[None, :] < tail_lengths[:, None]).astype(jnp.float32)
    k_numer, k_peak, k_mass = _attend_local(q_rows, prefix_kv, tail_kv, valid)

    def by_owner(x):
        x = jnp.transpose(x, (2, 1, 0, 3) + tuple(range(4, x.ndim)))
        x = x.reshape((steps_n, rows_dev, tp_count, heads_dev) + x.shape[4:])
        return jnp.moveaxis(x, 2, 0)

    grid4 = (kv_heads, rows_dev, steps_n, group)
    o_numer = by_owner(k_numer.reshape(grid4 + (DH,))).reshape(tp_count, -1, DH)
    o_peak = by_owner(k_peak[..., 0].reshape(grid4)).reshape(tp_count, -1)
    o_mass = by_owner(k_mass[..., 0].reshape(grid4)).reshape(tp_count, -1)
    n_rows = steps_n * rows_dev * heads_dev
    o_att = (o_numer / o_mass[..., None]).astype(jnp.bfloat16)
    stats = jnp.concatenate([o_peak, o_mass], axis=1)
    stats_hi = stats.astype(jnp.bfloat16)
    stats_lo = (stats - stats_hi.astype(jnp.float32)).astype(jnp.bfloat16)
    stats = jnp.concatenate([stats_hi, stats_lo], axis=1)
    n_stat = -(-4 * n_rows // (16 * DH)) * 16
    stats = jnp.pad(stats, ((0, 0), (0, n_stat * DH - 4 * n_rows))).reshape(tp_count, n_stat, DH)
    got = _exchange(jnp.concatenate([o_att, stats], axis=1), "tp", tp_count)
    got_numer = got[:, :n_rows].astype(jnp.float32)
    got_numer = got_numer.reshape(tp_count, steps_n, rows_dev, heads_dev, DH)
    got_stats = got[:, n_rows:].reshape(tp_count, -1)[:, : 4 * n_rows].astype(jnp.float32)
    got_stats = got_stats[:, : 2 * n_rows] + got_stats[:, 2 * n_rows:]
    got_stats = got_stats.reshape(tp_count, 2, steps_n, rows_dev, heads_dev)
    got_peak = got_stats[:, 0]
    got_mass = got_stats[:, 1]

    own_query = queries.reshape(steps_n, rows_dev, heads_dev, DH)
    f_kv = fresh_kv.reshape(2, steps_n, rows_dev, kv_heads, DH)
    if group % heads_dev == 0:
        one_kv = lax.dynamic_index_in_dim(f_kv, tp_rank * heads_dev // group, 3, keepdims=True)
        f_kv = jnp.broadcast_to(one_kv, (2, steps_n, rows_dev, heads_dev, DH))
    else:
        kv_of_head = (tp_rank * heads_dev + jnp.arange(heads_dev)) // group
        f_kv = jnp.take(f_kv, kv_of_head, axis=3)
    f_scores = (
        jnp.einsum("sbhd,ubhd->sbhu", own_query, f_kv[0], preferred_element_type=jnp.float32)
        * score_scale
    )
    fresh_live = jnp.arange(steps_n)[None, :] <= jnp.arange(steps_n)[:, None]
    f_scores = jnp.where(fresh_live[:, None, None, :], f_scores, NEG_FILL)

    peak = jnp.maximum(got_peak.max(0), f_scores.max(-1))
    rescale = jnp.exp(got_peak - peak[None])
    f_w = jnp.exp(f_scores - peak[..., None])
    mass = (got_mass * rescale).sum(0) + f_w.sum(-1)
    numer = (got_numer * (got_mass * rescale)[..., None]).sum(0)
    numer = numer + jnp.einsum(
        "sbhu,ubhd->sbhd", f_w.astype(jnp.bfloat16), f_kv[1], preferred_element_type=jnp.float32
    )
    attended = (numer / mass[..., None]).astype(jnp.bfloat16).reshape(steps_n, rows_dev, width_dev)

    gathered = lax.all_gather(attended, "sub", axis=1, tiled=True)
    samples = gathered.shape[1]
    local_width = out_weight.shape[1]
    head_rows_in = gathered.reshape(steps_n * samples, heads_dev, DH)
    head_weights = out_weight.reshape(heads_dev, DH, local_width)
    scale_a = jnp.repeat(jnp.exp2(-scale_in.astype(jnp.float32)), 128)
    scale_b = jnp.repeat(jnp.exp2(-scale_out.astype(jnp.float32)), 128)
    local_a = lax.dynamic_slice_in_dim(scale_a, sub_rank * local_width, local_width, 0)
    local_b = lax.dynamic_slice_in_dim(scale_b, sub_rank * local_width, local_width, 0)
    per_head_term = jnp.einsum(
        "rhd,hdf->rhf", head_rows_in, head_weights, preferred_element_type=jnp.float32
    )
    clipped = jnp.clip(per_head_term / local_a[None, None, :], -127.0, 127.0).sum(1)

    piece_cols = local_width // tp_count
    pieces = jnp.moveaxis(clipped.reshape(steps_n * samples, tp_count, piece_cols), 1, 0)
    got_pieces = _exchange(pieces, "tp", tp_count)
    summed = got_pieces.sum(0)
    piece_start = sub_rank * local_width + tp_rank * piece_cols
    piece_a = lax.dynamic_slice_in_dim(scale_a, piece_start, piece_cols, 0)
    piece_b = lax.dynamic_slice_in_dim(scale_b, piece_start, piece_cols, 0)
    levels = jnp.clip(summed * piece_a / piece_b, -127.0, 127.0).astype(jnp.bfloat16)
    level_blocks = _gather_blocks(levels, "tp", tp_count)
    all_levels = jnp.moveaxis(level_blocks, 0, 1).reshape(steps_n * samples, local_width)
    restored = all_levels.astype(jnp.float32) * local_b
    hidden = residual.reshape(steps_n * samples, local_width).astype(jnp.float32) + restored
    return hidden.astype(jnp.bfloat16).reshape(steps_n, samples, local_width)


def solution(mesh):
    return jax.shard_map(
        per_device,
        mesh=mesh,
        in_specs=(
            P(None, ("rep", "sub"), "tp"),
            P(None, ("rep", "tp"), None),
            P(None, ("rep", "sub"), "tp", None),
            P(("rep", "sub")),
            P(None, None, ("rep", "sub"), None),
            P("tp", "sub"),
            P(),
            P(),
            P(None, "rep", "sub"),
        ),
        out_specs=P(None, "rep", "sub"),
        check_vma=False,
    )
```

```python
import functools
import math

import jax
import jax.numpy as jnp
from jax import lax
from jax.experimental import pallas as pl
from jax.experimental.pallas import tpu as pltpu
from jax.sharding import PartitionSpec as P

DH = 128


NEG_FILL = -1e30


def _is_pow2(n):
    return n >= 1 and (n & (n - 1)) == 0


def _gather_blocks(x, axis_name, count):
    if count == 1:
        return x[None]
    if not _is_pow2(count):
        return lax.all_gather(x, axis_name, axis=0, tiled=False)
    me = lax.axis_index(axis_name)
    if count <= 8:
        other = lax.ppermute(x, axis_name, [(i, i ^ 1) for i in range(count)])
        low = me % 2 == 0
        pair = jnp.where(low, jnp.stack([x, other]), jnp.stack([other, x]))
        pairs = [pair]
        for d in range(1, count // 2):
            pairs.append(
                lax.ppermute(pair, axis_name, [(i, (i + 2 * d) % count) for i in range(count)])
            )
        order = (me // 2 - jnp.arange(count // 2)) % (count // 2)
        placed = jnp.zeros((count // 2,) + pair.shape, pair.dtype).at[order].set(jnp.stack(pairs))
        return placed.reshape((count,) + x.shape)
    cur = x[None]
    k = 1
    while k < count:
        other = lax.ppermute(cur, axis_name, [(i, i ^ k) for i in range(count)])
        low = (me // k) % 2 == 0
        cur = jnp.where(low, jnp.concatenate([cur, other]), jnp.concatenate([other, cur]))
        k *= 2
    return cur


def _exchange(blocks, axis_name, count, direct_max=8):
    if count == 1:
        return blocks
    if count > direct_max:
        return jax.tree.map(
            lambda b: lax.all_to_all(b, axis_name, split_axis=0, concat_axis=0, tiled=True), blocks
        )
    me = lax.axis_index(axis_name)
    got = [jax.tree.map(lambda b: lax.dynamic_index_in_dim(b, me, 0, keepdims=False), blocks)]
    for k in range(1, count):
        dst = (me + k) % count
        send = jax.tree.map(lambda b: lax.dynamic_index_in_dim(b, dst, 0, keepdims=False), blocks)
        got.append(lax.ppermute(send, axis_name, [(i, (i + k) % count) for i in range(count)]))
    return jax.tree.map(lambda *xs: jnp.stack(xs), *got)


def _attend_kernel(q_ref, k_ref, v_ref, tk_ref, tv_ref, valid_ref, numer_ref, peak_ref, mass_ref):
    heads_n, rows_n = q_ref.shape[0], q_ref.shape[1]
    samples = tk_ref.shape[1]
    per_sample = rows_n // samples
    score_scale = 1.0 / math.sqrt(DH)
    dims_nt = (((1,), (1,)), ((), ()))
    for j in range(heads_n):
        cols = slice(j * DH, (j + 1) * DH)
        q = q_ref[j]
        p_scores = lax.dot_general(q, k_ref[0, :, cols], dims_nt, preferred_element_type=jnp.float32)
        p_scores = p_scores * score_scale
        t_parts = []
        for r in range(samples):
            qr = q[r * per_sample:(r + 1) * per_sample]
            sr = lax.dot_general(
                qr, tk_ref[0, r, :, cols], dims_nt, preferred_element_type=jnp.float32
            )
            sr = sr * score_scale
            t_parts.append(jnp.where(valid_ref[r:r + 1, :] > 0.0, sr, NEG_FILL))
        t_scores = jnp.concatenate(t_parts, axis=0)
        peak = jnp.maximum(
            jnp.max(p_scores, axis=1, keepdims=True), jnp.max(t_scores, axis=1, keepdims=True)
        )
        p_w = jnp.exp(p_scores - peak)
        t_w = jnp.exp(t_scores - peak)
        mass = jnp.sum(p_w, axis=1, keepdims=True) + jnp.sum(t_w, axis=1, keepdims=True)
        numer = jnp.dot(
            p_w.astype(jnp.bfloat16), v_ref[0, :, cols], preferred_element_type=jnp.float32
        )
        t_w16 = t_w.astype(jnp.bfloat16)
        t_numer = [
            jnp.dot(
                t_w16[r * per_sample:(r + 1) * per_sample], tv_ref[0, r, :, cols],
                preferred_element_type=jnp.float32,
            )
            for r in range(samples)
        ]
        numer_ref[j] = numer + jnp.concatenate(t_numer, axis=0)
        peak_ref[j] = jnp.broadcast_to(peak, peak_ref.shape[1:])
        mass_ref[j] = jnp.broadcast_to(mass, mass_ref.shape[1:])


def _attend_local(q_rows, prefix_kv, tail_kv, valid):
    kv_heads, rows_n, _ = q_rows.shape
    prefix_dev = prefix_kv.shape[1]
    samples, tail_dev = tail_kv.shape[1], tail_kv.shape[2]
    flops = 4 * kv_heads * rows_n * DH * (prefix_dev + tail_dev)
    bytes_in = 2 * (prefix_kv.size + tail_kv.size + q_rows.size)
    per_step = 4 if kv_heads % 4 == 0 else 1
    width = per_step * DH
    return pl.pallas_call(
        _attend_kernel,
        grid=(kv_heads // per_step,),
        in_specs=[
            pl.BlockSpec((per_step, rows_n, DH), lambda k: (k, 0, 0)),
            pl.BlockSpec((1, prefix_dev, width), lambda k: (0, 0, k)),
            pl.BlockSpec((1, prefix_dev, width), lambda k: (1, 0, k)),
            pl.BlockSpec((1, samples, tail_dev, width), lambda k: (0, 0, 0, k)),
            pl.BlockSpec((1, samples, tail_dev, width), lambda k: (1, 0, 0, k)),
            pl.BlockSpec((samples, tail_dev), lambda k: (0, 0)),
        ],
        out_specs=[
            pl.BlockSpec((per_step, rows_n, DH), lambda k: (k, 0, 0)),
            pl.BlockSpec((per_step, rows_n, DH), lambda k: (k, 0, 0)),
            pl.BlockSpec((per_step, rows_n, DH), lambda k: (k, 0, 0)),
        ],
        out_shape=[jax.ShapeDtypeStruct((kv_heads, rows_n, DH), jnp.float32)] * 3,
        cost_estimate=pl.CostEstimate(
            flops=flops,
            transcendentals=kv_heads * rows_n * (prefix_dev + tail_dev),
            bytes_accessed=bytes_in + 3 * 4 * kv_heads * rows_n * DH,
        ),
        compiler_params=pltpu.CompilerParams(vmem_limit_bytes=48 * 1024 * 1024),
    )(q_rows, prefix_kv, prefix_kv, tail_kv, tail_kv, valid)


def _attend_packed_kernel(
    group, q_ref, k_ref, v_ref, tk_ref, tv_ref, valid_ref, out_ref
):
    heads_n, rows_n = q_ref.shape[0], q_ref.shape[1]
    samples, tail_dev = tk_ref.shape[1], tk_ref.shape[2]
    score_scale = 1.0 / math.sqrt(DH)
    dims_nt = (((1,), (1,)), ((), ()))
    row_sample = (lax.broadcasted_iota(jnp.int32, (rows_n, tail_dev), 0) // group) % samples
    for j in range(heads_n):
        cols = slice(j * DH, (j + 1) * DH)
        q = q_ref[j]
        p_scores = lax.dot_general(q, k_ref[0, :, cols], dims_nt, preferred_element_type=jnp.float32)
        p_scores = p_scores * score_scale
        t_scores = jnp.full((rows_n, tail_dev), NEG_FILL, jnp.float32)
        for r in range(samples):
            sr = lax.dot_general(
                q, tk_ref[0, r, :, cols], dims_nt, preferred_element_type=jnp.float32
            )
            live = (row_sample == r) & (valid_ref[r:r + 1, :] > 0.0)
            t_scores = jnp.where(live, sr * score_scale, t_scores)
        peak = jnp.maximum(
            jnp.max(p_scores, axis=1, keepdims=True), jnp.max(t_scores, axis=1, keepdims=True)
        )
        p_w = jnp.exp(p_scores - peak)
        t_w = jnp.exp(t_scores - peak)
        mass = jnp.sum(p_w, axis=1, keepdims=True) + jnp.sum(t_w, axis=1, keepdims=True)
        numer = jnp.dot(
            p_w.astype(jnp.bfloat16), v_ref[0, :, cols], preferred_element_type=jnp.float32
        )
        for r in range(samples):
            t_w16 = jnp.where(row_sample == r, t_w, 0.0).astype(jnp.bfloat16)
            numer = numer + jnp.dot(t_w16, tv_ref[0, r, :, cols], preferred_element_type=jnp.float32)
        out_ref[j, :rows_n, :] = numer
        peak_row = jnp.transpose(jnp.broadcast_to(peak, (rows_n, DH)))[0:1]
        mass_row = jnp.transpose(jnp.broadcast_to(mass, (rows_n, DH)))[0:1]
        out_ref[j, rows_n:, :] = jnp.concatenate(
            [peak_row, mass_row, jnp.zeros((6, DH), jnp.float32)], axis=0
        )


def _attend_packed(q_rows, prefix_kv, tail_kv, valid, group):
    kv_heads, rows_n, _ = q_rows.shape
    prefix_dev = prefix_kv.shape[1]
    samples, tail_dev = tail_kv.shape[1], tail_kv.shape[2]
    flops = 4 * kv_heads * rows_n * DH * (prefix_dev + samples * tail_dev)
    bytes_in = 2 * (prefix_kv.size + tail_kv.size + q_rows.size)
    per_step = 4 if kv_heads % 4 == 0 else 1
    width = per_step * DH
    return pl.pallas_call(
        functools.partial(_attend_packed_kernel, group),
        grid=(kv_heads // per_step,),
        in_specs=[
            pl.BlockSpec((per_step, rows_n, DH), lambda k: (k, 0, 0)),
            pl.BlockSpec((1, prefix_dev, width), lambda k: (0, 0, k)),
            pl.BlockSpec((1, prefix_dev, width), lambda k: (1, 0, k)),
            pl.BlockSpec((1, samples, tail_dev, width), lambda k: (0, 0, 0, k)),
            pl.BlockSpec((1, samples, tail_dev, width), lambda k: (1, 0, 0, k)),
            pl.BlockSpec((samples, tail_dev), lambda k: (0, 0)),
        ],
        out_specs=pl.BlockSpec((per_step, rows_n + 8, DH), lambda k: (k, 0, 0)),
        out_shape=jax.ShapeDtypeStruct((kv_heads, rows_n + 8, DH), jnp.float32),
        cost_estimate=pl.CostEstimate(
            flops=flops,
            transcendentals=kv_heads * rows_n * (prefix_dev + tail_dev),
            bytes_accessed=bytes_in + 4 * kv_heads * (rows_n + 8) * DH,
        ),
        compiler_params=pltpu.CompilerParams(vmem_limit_bytes=48 * 1024 * 1024),
    )(q_rows, prefix_kv, prefix_kv, tail_kv, tail_kv, valid)


def per_device(
    queries, prefix_kv, tail_kv, tail_lengths, fresh_kv, out_weight, scale_in, scale_out, residual
):
    steps_n, rows_dev, width_dev = queries.shape
    heads_dev = width_dev // DH
    tp_count = lax.axis_size("tp")
    tp_rank = lax.axis_index("tp")
    sub_rank = lax.axis_index("sub")
    kv_heads = prefix_kv.shape[2] // DH
    heads_all = heads_dev * tp_count
    group = heads_all // kv_heads
    prefix_dev = prefix_kv.shape[1]
    tail_dev = tail_kv.shape[2]
    score_scale = 1.0 / math.sqrt(DH)

    q_blocks = _gather_blocks(queries, "tp", tp_count)
    q_all = jnp.moveaxis(q_blocks, 0, 2).reshape(steps_n, rows_dev, kv_heads, group, DH)
    t_pos = tp_rank * tail_dev + jnp.arange(tail_dev)
    valid = (t_pos[None, :] < tail_lengths[:, None]).astype(jnp.float32)
    n_rows = steps_n * rows_dev * heads_dev
    if tp_count == kv_heads and heads_dev == group and n_rows == DH:
        q_rows = jnp.transpose(q_all, (2, 0, 1, 3, 4)).reshape(kv_heads, -1, DH)
        got = _exchange(_attend_packed(q_rows, prefix_kv, tail_kv, valid, group), "tp", tp_count)
        got_numer = got[:, :n_rows].reshape(tp_count, steps_n, rows_dev, heads_dev, DH)
        got_peak = got[:, n_rows].reshape(tp_count, steps_n, rows_dev, heads_dev)
        got_mass = got[:, n_rows + 1].reshape(tp_count, steps_n, rows_dev, heads_dev)
    else:

        q_rows = jnp.transpose(q_all, (2, 1, 0, 3, 4)).reshape(kv_heads, -1, DH)
        t_pos = tp_rank * tail_dev + jnp.arange(tail_dev)
        valid = (t_pos[None, :] < tail_lengths[:, None]).astype(jnp.float32)
        k_numer, k_peak, k_mass = _attend_local(q_rows, prefix_kv, tail_kv, valid)

        def by_owner(x):
            x = jnp.transpose(x, (2, 1, 0, 3) + tuple(range(4, x.ndim)))
            x = x.reshape((steps_n, rows_dev, tp_count, heads_dev) + x.shape[4:])
            return jnp.moveaxis(x, 2, 0)

        grid4 = (kv_heads, rows_dev, steps_n, group)
        o_numer = by_owner(k_numer.reshape(grid4 + (DH,))).reshape(tp_count, -1, DH)
        o_peak = by_owner(k_peak[..., 0].reshape(grid4)).reshape(tp_count, -1)
        o_mass = by_owner(k_mass[..., 0].reshape(grid4)).reshape(tp_count, -1)
        n_rows = steps_n * rows_dev * heads_dev
        n_stat = -(-2 * n_rows // DH)
        stats = jnp.concatenate([o_peak, o_mass], axis=1)
        stats = jnp.pad(stats, ((0, 0), (0, n_stat * DH - 2 * n_rows))).reshape(tp_count, n_stat, DH)
        got = _exchange(jnp.concatenate([o_numer, stats], axis=1), "tp", tp_count)
        got_numer = got[:, :n_rows].reshape(tp_count, steps_n, rows_dev, heads_dev, DH)
        got_stats = got[:, n_rows:].reshape(tp_count, -1)[:, : 2 * n_rows]
        got_stats = got_stats.reshape(tp_count, 2, steps_n, rows_dev, heads_dev)
        got_peak = got_stats[:, 0]
        got_mass = got_stats[:, 1]

    own_query = queries.reshape(steps_n, rows_dev, heads_dev, DH)
    f_kv = fresh_kv.reshape(2, steps_n, rows_dev, kv_heads, DH)
    if group % heads_dev == 0:
        one_kv = lax.dynamic_index_in_dim(f_kv, tp_rank * heads_dev // group, 3, keepdims=True)
        f_kv = jnp.broadcast_to(one_kv, (2, steps_n, rows_dev, heads_dev, DH))
    else:
        kv_of_head = (tp_rank * heads_dev + jnp.arange(heads_dev)) // group
        f_kv = jnp.take(f_kv, kv_of_head, axis=3)
    f_scores = (
        jnp.einsum("sbhd,ubhd->sbhu", own_query, f_kv[0], preferred_element_type=jnp.float32)
        * score_scale
    )
    fresh_live = jnp.arange(steps_n)[None, :] <= jnp.arange(steps_n)[:, None]
    f_scores = jnp.where(fresh_live[:, None, None, :], f_scores, NEG_FILL)

    peak = jnp.maximum(got_peak.max(0), f_scores.max(-1))
    rescale = jnp.exp(got_peak - peak[None])
    f_w = jnp.exp(f_scores - peak[..., None])
    mass = (got_mass * rescale).sum(0) + f_w.sum(-1)
    numer = (got_numer * rescale[..., None]).sum(0)
    numer = numer + jnp.einsum(
        "sbhu,ubhd->sbhd", f_w.astype(jnp.bfloat16), f_kv[1], preferred_element_type=jnp.float32
    )
    attended = (numer / mass[..., None]).astype(jnp.bfloat16).reshape(steps_n, rows_dev, width_dev)

    gathered = lax.all_gather(attended, "sub", axis=1, tiled=True)
    samples = gathered.shape[1]
    local_width = out_weight.shape[1]
    head_rows_in = gathered.reshape(steps_n * samples, heads_dev, DH)
    head_weights = out_weight.reshape(heads_dev, DH, local_width)
    scale_a = jnp.repeat(jnp.exp2(-scale_in.astype(jnp.float32)), 128)
    scale_b = jnp.repeat(jnp.exp2(-scale_out.astype(jnp.float32)), 128)
    local_a = lax.dynamic_slice_in_dim(scale_a, sub_rank * local_width, local_width, 0)
    local_b = lax.dynamic_slice_in_dim(scale_b, sub_rank * local_width, local_width, 0)
    per_head_term = jnp.einsum(
        "rhd,hdf->rhf", head_rows_in, head_weights, preferred_element_type=jnp.float32
    )
    clipped = jnp.clip(per_head_term / local_a[None, None, :], -127.0, 127.0).sum(1)

    piece_cols = local_width // tp_count
    pieces = jnp.moveaxis(clipped.reshape(steps_n * samples, tp_count, piece_cols), 1, 0)
    got_pieces = _exchange(pieces, "tp", tp_count)
    summed = got_pieces.sum(0)
    piece_start = sub_rank * local_width + tp_rank * piece_cols
    piece_a = lax.dynamic_slice_in_dim(scale_a, piece_start, piece_cols, 0)
    piece_b = lax.dynamic_slice_in_dim(scale_b, piece_start, piece_cols, 0)
    levels = jnp.clip(summed * piece_a / piece_b, -127.0, 127.0).astype(jnp.bfloat16)
    level_blocks = _gather_blocks(levels, "tp", tp_count)
    all_levels = jnp.moveaxis(level_blocks, 0, 1).reshape(steps_n * samples, local_width)
    restored = all_levels.astype(jnp.float32) * local_b
    hidden = residual.reshape(steps_n * samples, local_width).astype(jnp.float32) + restored
    return hidden.astype(jnp.bfloat16).reshape(steps_n, samples, local_width)


def solution(mesh):
    return jax.shard_map(
        per_device,
        mesh=mesh,
        in_specs=(
            P(None, ("rep", "sub"), "tp"),
            P(None, ("rep", "tp"), None),
            P(None, ("rep", "sub"), "tp", None),
            P(("rep", "sub")),
            P(None, None, ("rep", "sub"), None),
            P("tp", "sub"),
            P(),
            P(),
            P(None, "rep", "sub"),
        ),
        out_specs=P(None, "rep", "sub"),
        check_vma=False,
    )
```

```python
import functools
import math

import jax
import jax.numpy as jnp
from jax import lax
from jax.experimental import pallas as pl
from jax.experimental.pallas import tpu as pltpu
from jax.sharding import PartitionSpec as P

DH = 128


NEG_FILL = -1e30


def _is_pow2(n):
    return n >= 1 and (n & (n - 1)) == 0


def _gather_blocks(x, axis_name, count):
    if count == 1:
        return x[None]
    if not _is_pow2(count):
        return lax.all_gather(x, axis_name, axis=0, tiled=False)
    me = lax.axis_index(axis_name)
    if count <= 8:
        other = lax.ppermute(x, axis_name, [(i, i ^ 1) for i in range(count)])
        low = me % 2 == 0
        pair = jnp.where(low, jnp.stack([x, other]), jnp.stack([other, x]))
        pairs = [pair]
        for d in range(1, count // 2):
            pairs.append(
                lax.ppermute(pair, axis_name, [(i, (i + 2 * d) % count) for i in range(count)])
            )
        order = (me // 2 - jnp.arange(count // 2)) % (count // 2)
        placed = jnp.zeros((count // 2,) + pair.shape, pair.dtype).at[order].set(jnp.stack(pairs))
        return placed.reshape((count,) + x.shape)
    cur = x[None]
    k = 1
    while k < count:
        other = lax.ppermute(cur, axis_name, [(i, i ^ k) for i in range(count)])
        low = (me // k) % 2 == 0
        cur = jnp.where(low, jnp.concatenate([cur, other]), jnp.concatenate([other, cur]))
        k *= 2
    return cur


def _exchange(blocks, axis_name, count, direct_max=8):
    if count == 1:
        return blocks
    if count > direct_max:
        return jax.tree.map(
            lambda b: lax.all_to_all(b, axis_name, split_axis=0, concat_axis=0, tiled=True), blocks
        )
    me = lax.axis_index(axis_name)
    got = [jax.tree.map(lambda b: lax.dynamic_index_in_dim(b, me, 0, keepdims=False), blocks)]
    for k in range(1, count):
        dst = (me + k) % count
        send = jax.tree.map(lambda b: lax.dynamic_index_in_dim(b, dst, 0, keepdims=False), blocks)
        got.append(lax.ppermute(send, axis_name, [(i, (i + k) % count) for i in range(count)]))
    return jax.tree.map(lambda *xs: jnp.stack(xs), *got)


def _attend_kernel(q_ref, k_ref, v_ref, tk_ref, tv_ref, valid_ref, numer_ref, peak_ref, mass_ref):
    heads_n, rows_n = q_ref.shape[0], q_ref.shape[1]
    samples = tk_ref.shape[1]
    per_sample = rows_n // samples
    score_scale = 1.0 / math.sqrt(DH)
    dims_nt = (((1,), (1,)), ((), ()))
    for j in range(heads_n):
        cols = slice(j * DH, (j + 1) * DH)
        q = q_ref[j]
        p_scores = lax.dot_general(q, k_ref[0, :, cols], dims_nt, preferred_element_type=jnp.float32)
        p_scores = p_scores * score_scale
        t_parts = []
        for r in range(samples):
            qr = q[r * per_sample:(r + 1) * per_sample]
            sr = lax.dot_general(
                qr, tk_ref[0, r, :, cols], dims_nt, preferred_element_type=jnp.float32
            )
            sr = sr * score_scale
            t_parts.append(jnp.where(valid_ref[r:r + 1, :] > 0.0, sr, NEG_FILL))
        t_scores = jnp.concatenate(t_parts, axis=0)
        peak = jnp.maximum(
            jnp.max(p_scores, axis=1, keepdims=True), jnp.max(t_scores, axis=1, keepdims=True)
        )
        p_w = jnp.exp(p_scores - peak)
        t_w = jnp.exp(t_scores - peak)
        mass = jnp.sum(p_w, axis=1, keepdims=True) + jnp.sum(t_w, axis=1, keepdims=True)
        numer = jnp.dot(
            p_w.astype(jnp.bfloat16), v_ref[0, :, cols], preferred_element_type=jnp.float32
        )
        t_w16 = t_w.astype(jnp.bfloat16)
        t_numer = [
            jnp.dot(
                t_w16[r * per_sample:(r + 1) * per_sample], tv_ref[0, r, :, cols],
                preferred_element_type=jnp.float32,
            )
            for r in range(samples)
        ]
        numer_ref[j] = numer + jnp.concatenate(t_numer, axis=0)
        peak_ref[j] = jnp.broadcast_to(peak, peak_ref.shape[1:])
        mass_ref[j] = jnp.broadcast_to(mass, mass_ref.shape[1:])


def _attend_local(q_rows, prefix_kv, tail_kv, valid):
    kv_heads, rows_n, _ = q_rows.shape
    prefix_dev = prefix_kv.shape[1]
    samples, tail_dev = tail_kv.shape[1], tail_kv.shape[2]
    flops = 4 * kv_heads * rows_n * DH * (prefix_dev + tail_dev)
    bytes_in = 2 * (prefix_kv.size + tail_kv.size + q_rows.size)
    per_step = 4 if kv_heads % 4 == 0 else 1
    width = per_step * DH
    return pl.pallas_call(
        _attend_kernel,
        grid=(kv_heads // per_step,),
        in_specs=[
            pl.BlockSpec((per_step, rows_n, DH), lambda k: (k, 0, 0)),
            pl.BlockSpec((1, prefix_dev, width), lambda k: (0, 0, k)),
            pl.BlockSpec((1, prefix_dev, width), lambda k: (1, 0, k)),
            pl.BlockSpec((1, samples, tail_dev, width), lambda k: (0, 0, 0, k)),
            pl.BlockSpec((1, samples, tail_dev, width), lambda k: (1, 0, 0, k)),
            pl.BlockSpec((samples, tail_dev), lambda k: (0, 0)),
        ],
        out_specs=[
            pl.BlockSpec((per_step, rows_n, DH), lambda k: (k, 0, 0)),
            pl.BlockSpec((per_step, rows_n, DH), lambda k: (k, 0, 0)),
            pl.BlockSpec((per_step, rows_n, DH), lambda k: (k, 0, 0)),
        ],
        out_shape=[jax.ShapeDtypeStruct((kv_heads, rows_n, DH), jnp.float32)] * 3,
        cost_estimate=pl.CostEstimate(
            flops=flops,
            transcendentals=kv_heads * rows_n * (prefix_dev + tail_dev),
            bytes_accessed=bytes_in + 3 * 4 * kv_heads * rows_n * DH,
        ),
    )(q_rows, prefix_kv, prefix_kv, tail_kv, tail_kv, valid)


def _attend_packed_kernel(
    group, q_ref, k_ref, v_ref, tk_ref, tv_ref, valid_ref, out_ref
):
    heads_n, rows_n = q_ref.shape[0], q_ref.shape[1]
    samples, tail_dev = tk_ref.shape[1], tk_ref.shape[2]
    score_scale = 1.0 / math.sqrt(DH)
    dims_nt = (((1,), (1,)), ((), ()))
    row_sample = (lax.broadcasted_iota(jnp.int32, (rows_n, tail_dev), 0) // group) % samples
    for j in range(heads_n):
        cols = slice(j * DH, (j + 1) * DH)
        q = q_ref[j]
        p_scores = lax.dot_general(q, k_ref[0, :, cols], dims_nt, preferred_element_type=jnp.float32)
        p_scores = p_scores * score_scale
        t_scores = jnp.full((rows_n, tail_dev), NEG_FILL, jnp.float32)
        for r in range(samples):
            sr = lax.dot_general(
                q, tk_ref[0, r, :, cols], dims_nt, preferred_element_type=jnp.float32
            )
            live = (row_sample == r) & (valid_ref[r:r + 1, :] > 0.0)
            t_scores = jnp.where(live, sr * score_scale, t_scores)
        peak = jnp.maximum(
            jnp.max(p_scores, axis=1, keepdims=True), jnp.max(t_scores, axis=1, keepdims=True)
        )
        p_w = jnp.exp(p_scores - peak)
        t_w = jnp.exp(t_scores - peak)
        mass = jnp.sum(p_w, axis=1, keepdims=True) + jnp.sum(t_w, axis=1, keepdims=True)
        numer = jnp.dot(
            p_w.astype(jnp.bfloat16), v_ref[0, :, cols], preferred_element_type=jnp.float32
        )
        for r in range(samples):
            t_w16 = jnp.where(row_sample == r, t_w, 0.0).astype(jnp.bfloat16)
            numer = numer + jnp.dot(t_w16, tv_ref[0, r, :, cols], preferred_element_type=jnp.float32)
        out_ref[j, :rows_n, :] = numer
        peak_row = jnp.transpose(jnp.broadcast_to(peak, (rows_n, DH)))[0:1]
        mass_row = jnp.transpose(jnp.broadcast_to(mass, (rows_n, DH)))[0:1]
        out_ref[j, rows_n:, :] = jnp.concatenate(
            [peak_row, mass_row, jnp.zeros((6, DH), jnp.float32)], axis=0
        )


def _attend_packed(q_rows, prefix_kv, tail_kv, valid, group):
    kv_heads, rows_n, _ = q_rows.shape
    prefix_dev = prefix_kv.shape[1]
    samples, tail_dev = tail_kv.shape[1], tail_kv.shape[2]
    flops = 4 * kv_heads * rows_n * DH * (prefix_dev + samples * tail_dev)
    bytes_in = 2 * (prefix_kv.size + tail_kv.size + q_rows.size)
    per_step = 4 if kv_heads % 4 == 0 else 1
    width = per_step * DH
    return pl.pallas_call(
        functools.partial(_attend_packed_kernel, group),
        grid=(kv_heads // per_step,),
        in_specs=[
            pl.BlockSpec((per_step, rows_n, DH), lambda k: (k, 0, 0)),
            pl.BlockSpec((1, prefix_dev, width), lambda k: (0, 0, k)),
            pl.BlockSpec((1, prefix_dev, width), lambda k: (1, 0, k)),
            pl.BlockSpec((1, samples, tail_dev, width), lambda k: (0, 0, 0, k)),
            pl.BlockSpec((1, samples, tail_dev, width), lambda k: (1, 0, 0, k)),
            pl.BlockSpec((samples, tail_dev), lambda k: (0, 0)),
        ],
        out_specs=pl.BlockSpec((per_step, rows_n + 8, DH), lambda k: (k, 0, 0)),
        out_shape=jax.ShapeDtypeStruct((kv_heads, rows_n + 8, DH), jnp.float32),
        cost_estimate=pl.CostEstimate(
            flops=flops,
            transcendentals=kv_heads * rows_n * (prefix_dev + tail_dev),
            bytes_accessed=bytes_in + 4 * kv_heads * (rows_n + 8) * DH,
        ),
    )(q_rows, prefix_kv, prefix_kv, tail_kv, tail_kv, valid)


def per_device(
    queries, prefix_kv, tail_kv, tail_lengths, fresh_kv, out_weight, scale_in, scale_out, residual
):
    steps_n, rows_dev, width_dev = queries.shape
    heads_dev = width_dev // DH
    tp_count = lax.axis_size("tp")
    tp_rank = lax.axis_index("tp")
    sub_rank = lax.axis_index("sub")
    kv_heads = prefix_kv.shape[2] // DH
    heads_all = heads_dev * tp_count
    group = heads_all // kv_heads
    prefix_dev = prefix_kv.shape[1]
    tail_dev = tail_kv.shape[2]
    score_scale = 1.0 / math.sqrt(DH)

    q_blocks = _gather_blocks(queries, "tp", tp_count)
    q_all = jnp.moveaxis(q_blocks, 0, 2).reshape(steps_n, rows_dev, kv_heads, group, DH)
    t_pos = tp_rank * tail_dev + jnp.arange(tail_dev)
    valid = (t_pos[None, :] < tail_lengths[:, None]).astype(jnp.float32)
    n_rows = steps_n * rows_dev * heads_dev
    if tp_count == kv_heads and heads_dev == group and n_rows == DH:
        q_rows = jnp.transpose(q_all, (2, 0, 1, 3, 4)).reshape(kv_heads, -1, DH)
        got = _exchange(_attend_packed(q_rows, prefix_kv, tail_kv, valid, group), "tp", tp_count)
        got_numer = got[:, :n_rows].reshape(tp_count, steps_n, rows_dev, heads_dev, DH)
        got_peak = got[:, n_rows].reshape(tp_count, steps_n, rows_dev, heads_dev)
        got_mass = got[:, n_rows + 1].reshape(tp_count, steps_n, rows_dev, heads_dev)
    else:

        q_rows = jnp.transpose(q_all, (2, 1, 0, 3, 4)).reshape(kv_heads, -1, DH)
        t_pos = tp_rank * tail_dev + jnp.arange(tail_dev)
        valid = (t_pos[None, :] < tail_lengths[:, None]).astype(jnp.float32)
        k_numer, k_peak, k_mass = _attend_local(q_rows, prefix_kv, tail_kv, valid)

        def by_owner(x):
            x = jnp.transpose(x, (2, 1, 0, 3) + tuple(range(4, x.ndim)))
            x = x.reshape((steps_n, rows_dev, tp_count, heads_dev) + x.shape[4:])
            return jnp.moveaxis(x, 2, 0)

        grid4 = (kv_heads, rows_dev, steps_n, group)
        o_numer = by_owner(k_numer.reshape(grid4 + (DH,))).reshape(tp_count, -1, DH)
        o_peak = by_owner(k_peak[..., 0].reshape(grid4)).reshape(tp_count, -1)
        o_mass = by_owner(k_mass[..., 0].reshape(grid4)).reshape(tp_count, -1)
        n_rows = steps_n * rows_dev * heads_dev
        n_stat = -(-2 * n_rows // DH)
        stats = jnp.concatenate([o_peak, o_mass], axis=1)
        stats = jnp.pad(stats, ((0, 0), (0, n_stat * DH - 2 * n_rows))).reshape(tp_count, n_stat, DH)
        got = _exchange(jnp.concatenate([o_numer, stats], axis=1), "tp", tp_count)
        got_numer = got[:, :n_rows].reshape(tp_count, steps_n, rows_dev, heads_dev, DH)
        got_stats = got[:, n_rows:].reshape(tp_count, -1)[:, : 2 * n_rows]
        got_stats = got_stats.reshape(tp_count, 2, steps_n, rows_dev, heads_dev)
        got_peak = got_stats[:, 0]
        got_mass = got_stats[:, 1]

    own_query = queries.reshape(steps_n, rows_dev, heads_dev, DH)
    f_kv = fresh_kv.reshape(2, steps_n, rows_dev, kv_heads, DH)
    if group % heads_dev == 0:
        one_kv = lax.dynamic_index_in_dim(f_kv, tp_rank * heads_dev // group, 3, keepdims=True)
        f_kv = jnp.broadcast_to(one_kv, (2, steps_n, rows_dev, heads_dev, DH))
    else:
        kv_of_head = (tp_rank * heads_dev + jnp.arange(heads_dev)) // group
        f_kv = jnp.take(f_kv, kv_of_head, axis=3)
    f_scores = (
        jnp.einsum("sbhd,ubhd->sbhu", own_query, f_kv[0], preferred_element_type=jnp.float32)
        * score_scale
    )
    fresh_live = jnp.arange(steps_n)[None, :] <= jnp.arange(steps_n)[:, None]
    f_scores = jnp.where(fresh_live[:, None, None, :], f_scores, NEG_FILL)

    peak = jnp.maximum(got_peak.max(0), f_scores.max(-1))
    rescale = jnp.exp(got_peak - peak[None])
    f_w = jnp.exp(f_scores - peak[..., None])
    mass = (got_mass * rescale).sum(0) + f_w.sum(-1)
    numer = (got_numer * rescale[..., None]).sum(0)
    numer = numer + jnp.einsum(
        "sbhu,ubhd->sbhd", f_w.astype(jnp.bfloat16), f_kv[1], preferred_element_type=jnp.float32
    )
    attended = (numer / mass[..., None]).astype(jnp.bfloat16).reshape(steps_n, rows_dev, width_dev)

    gathered = lax.all_gather(attended, "sub", axis=1, tiled=True)
    samples = gathered.shape[1]
    local_width = out_weight.shape[1]
    head_rows_in = gathered.reshape(steps_n * samples, heads_dev, DH)
    head_weights = out_weight.reshape(heads_dev, DH, local_width)
    scale_a = jnp.repeat(jnp.exp2(-scale_in.astype(jnp.float32)), 128)
    scale_b = jnp.repeat(jnp.exp2(-scale_out.astype(jnp.float32)), 128)
    local_a = lax.dynamic_slice_in_dim(scale_a, sub_rank * local_width, local_width, 0)
    local_b = lax.dynamic_slice_in_dim(scale_b, sub_rank * local_width, local_width, 0)
    per_head_term = jnp.einsum(
        "rhd,hdf->rhf", head_rows_in, head_weights, preferred_element_type=jnp.float32
    )
    clipped = jnp.clip(per_head_term / local_a[None, None, :], -127.0, 127.0).sum(1)

    piece_cols = local_width // tp_count
    pieces = jnp.moveaxis(clipped.reshape(steps_n * samples, tp_count, piece_cols), 1, 0)
    got_pieces = _exchange(pieces, "tp", tp_count)
    summed = got_pieces.sum(0)
    piece_start = sub_rank * local_width + tp_rank * piece_cols
    piece_a = lax.dynamic_slice_in_dim(scale_a, piece_start, piece_cols, 0)
    piece_b = lax.dynamic_slice_in_dim(scale_b, piece_start, piece_cols, 0)
    levels = jnp.clip(summed * piece_a / piece_b, -127.0, 127.0).astype(jnp.bfloat16)
    level_blocks = _gather_blocks(levels, "tp", tp_count)
    all_levels = jnp.moveaxis(level_blocks, 0, 1).reshape(steps_n * samples, local_width)
    restored = all_levels.astype(jnp.float32) * local_b
    hidden = residual.reshape(steps_n * samples, local_width).astype(jnp.float32) + restored
    return hidden.astype(jnp.bfloat16).reshape(steps_n, samples, local_width)


def solution(mesh):
    return jax.shard_map(
        per_device,
        mesh=mesh,
        in_specs=(
            P(None, ("rep", "sub"), "tp"),
            P(None, ("rep", "tp"), None),
            P(None, ("rep", "sub"), "tp", None),
            P(("rep", "sub")),
            P(None, None, ("rep", "sub"), None),
            P("tp", "sub"),
            P(),
            P(),
            P(None, "rep", "sub"),
        ),
        out_specs=P(None, "rep", "sub"),
        check_vma=False,
    )
```

```python
import functools
import math

import jax
import jax.numpy as jnp
from jax import lax
from jax.experimental import pallas as pl
from jax.experimental.pallas import tpu as pltpu
from jax.sharding import PartitionSpec as P

DH = 128


NEG_FILL = -1e30


def _is_pow2(n):
    return n >= 1 and (n & (n - 1)) == 0


def _gather_blocks(x, axis_name, count):
    if count == 1:
        return x[None]
    if not _is_pow2(count):
        return lax.all_gather(x, axis_name, axis=0, tiled=False)
    me = lax.axis_index(axis_name)
    if count <= 8:
        other = lax.ppermute(x, axis_name, [(i, i ^ 1) for i in range(count)])
        low = me % 2 == 0
        pair = jnp.where(low, jnp.stack([x, other]), jnp.stack([other, x]))
        pairs = [pair]
        for d in range(1, count // 2):
            pairs.append(
                lax.ppermute(pair, axis_name, [(i, (i + 2 * d) % count) for i in range(count)])
            )
        order = (me // 2 - jnp.arange(count // 2)) % (count // 2)
        placed = jnp.zeros((count // 2,) + pair.shape, pair.dtype).at[order].set(jnp.stack(pairs))
        return placed.reshape((count,) + x.shape)
    cur = x[None]
    k = 1
    while k < count:
        other = lax.ppermute(cur, axis_name, [(i, i ^ k) for i in range(count)])
        low = (me // k) % 2 == 0
        cur = jnp.where(low, jnp.concatenate([cur, other]), jnp.concatenate([other, cur]))
        k *= 2
    return cur


def _exchange(blocks, axis_name, count, direct_max=8):
    if count == 1:
        return blocks
    if count > direct_max:
        return jax.tree.map(
            lambda b: lax.all_to_all(b, axis_name, split_axis=0, concat_axis=0, tiled=True), blocks
        )
    me = lax.axis_index(axis_name)
    got = [jax.tree.map(lambda b: lax.dynamic_index_in_dim(b, me, 0, keepdims=False), blocks)]
    for k in range(1, count):
        dst = (me + k) % count
        send = jax.tree.map(lambda b: lax.dynamic_index_in_dim(b, dst, 0, keepdims=False), blocks)
        got.append(lax.ppermute(send, axis_name, [(i, (i + k) % count) for i in range(count)]))
    return jax.tree.map(lambda *xs: jnp.stack(xs), *got)


def _attend_kernel(q_ref, k_ref, v_ref, tk_ref, tv_ref, valid_ref, numer_ref, peak_ref, mass_ref):
    heads_n, rows_n = q_ref.shape[0], q_ref.shape[1]
    samples = tk_ref.shape[1]
    per_sample = rows_n // samples
    score_scale = 1.0 / math.sqrt(DH)
    dims_nt = (((1,), (1,)), ((), ()))
    for j in range(heads_n):
        cols = slice(j * DH, (j + 1) * DH)
        q = q_ref[j]
        p_scores = lax.dot_general(q, k_ref[0, :, cols], dims_nt, preferred_element_type=jnp.float32)
        p_scores = p_scores * score_scale
        t_parts = []
        for r in range(samples):
            qr = q[r * per_sample:(r + 1) * per_sample]
            sr = lax.dot_general(
                qr, tk_ref[0, r, :, cols], dims_nt, preferred_element_type=jnp.float32
            )
            sr = sr * score_scale
            t_parts.append(jnp.where(valid_ref[r:r + 1, :] > 0.0, sr, NEG_FILL))
        t_scores = jnp.concatenate(t_parts, axis=0)
        peak = jnp.maximum(
            jnp.max(p_scores, axis=1, keepdims=True), jnp.max(t_scores, axis=1, keepdims=True)
        )
        p_w = jnp.exp(p_scores - peak)
        t_w = jnp.exp(t_scores - peak)
        mass = jnp.sum(p_w, axis=1, keepdims=True) + jnp.sum(t_w, axis=1, keepdims=True)
        numer = jnp.dot(
            p_w.astype(jnp.bfloat16), v_ref[0, :, cols], preferred_element_type=jnp.float32
        )
        t_w16 = t_w.astype(jnp.bfloat16)
        t_numer = [
            jnp.dot(
                t_w16[r * per_sample:(r + 1) * per_sample], tv_ref[0, r, :, cols],
                preferred_element_type=jnp.float32,
            )
            for r in range(samples)
        ]
        numer_ref[j] = numer + jnp.concatenate(t_numer, axis=0)
        peak_ref[j] = jnp.broadcast_to(peak, peak_ref.shape[1:])
        mass_ref[j] = jnp.broadcast_to(mass, mass_ref.shape[1:])


def _attend_local(q_rows, prefix_kv, tail_kv, valid):
    kv_heads, rows_n, _ = q_rows.shape
    prefix_dev = prefix_kv.shape[1]
    samples, tail_dev = tail_kv.shape[1], tail_kv.shape[2]
    flops = 4 * kv_heads * rows_n * DH * (prefix_dev + tail_dev)
    bytes_in = 2 * (prefix_kv.size + tail_kv.size + q_rows.size)
    per_step = 4 if kv_heads % 4 == 0 else 1
    width = per_step * DH
    return pl.pallas_call(
        _attend_kernel,
        grid=(kv_heads // per_step,),
        in_specs=[
            pl.BlockSpec((per_step, rows_n, DH), lambda k: (k, 0, 0)),
            pl.BlockSpec((1, prefix_dev, width), lambda k: (0, 0, k)),
            pl.BlockSpec((1, prefix_dev, width), lambda k: (1, 0, k)),
            pl.BlockSpec((1, samples, tail_dev, width), lambda k: (0, 0, 0, k)),
            pl.BlockSpec((1, samples, tail_dev, width), lambda k: (1, 0, 0, k)),
            pl.BlockSpec((samples, tail_dev), lambda k: (0, 0)),
        ],
        out_specs=[
            pl.BlockSpec((per_step, rows_n, DH), lambda k: (k, 0, 0)),
            pl.BlockSpec((per_step, rows_n, DH), lambda k: (k, 0, 0)),
            pl.BlockSpec((per_step, rows_n, DH), lambda k: (k, 0, 0)),
        ],
        out_shape=[jax.ShapeDtypeStruct((kv_heads, rows_n, DH), jnp.float32)] * 3,
        cost_estimate=pl.CostEstimate(
            flops=flops,
            transcendentals=kv_heads * rows_n * (prefix_dev + tail_dev),
            bytes_accessed=bytes_in + 3 * 4 * kv_heads * rows_n * DH,
        ),
        compiler_params=pltpu.CompilerParams(vmem_limit_bytes=48 * 1024 * 1024),
    )(q_rows, prefix_kv, prefix_kv, tail_kv, tail_kv, valid)


def _pairs_kernel(u_ref, q_ref, k_ref, v_ref, tko_ref, tvo_ref, tkp_ref, tvp_ref,
                  valid_o_ref, valid_p_ref, out_ref, *, group):
    heads_n, rows_n = q_ref.shape[0], q_ref.shape[1]
    per_core, tail_dev = tko_ref.shape[1], tko_ref.shape[2]
    samples = 2 * per_core
    u = u_ref[0]
    score_scale = 1.0 / math.sqrt(DH)
    dims_nt = (((1,), (1,)), ((), ()))
    row_sample = (lax.broadcasted_iota(jnp.int32, (rows_n, tail_dev), 0) // group) % samples
    sources = [(tko_ref, tvo_ref, valid_o_ref, u * per_core),
               (tkp_ref, tvp_ref, valid_p_ref, (1 - u) * per_core)]
    for j in range(heads_n):
        cols = slice(j * DH, (j + 1) * DH)
        q = q_ref[j]
        p_scores = lax.dot_general(q, k_ref[0, :, cols], dims_nt, preferred_element_type=jnp.float32)
        p_scores = p_scores * score_scale
        t_scores = jnp.full((rows_n, tail_dev), NEG_FILL, jnp.float32)
        for tk_ref, _, valid_ref, first in sources:
            for r in range(per_core):
                sr = lax.dot_general(
                    q, tk_ref[0, r, :, cols], dims_nt, preferred_element_type=jnp.float32
                )
                live = (row_sample == first + r) & (valid_ref[r:r + 1, :] > 0.0)
                t_scores = jnp.where(live, sr * score_scale, t_scores)
        peak = jnp.maximum(
            jnp.max(p_scores, axis=1, keepdims=True), jnp.max(t_scores, axis=1, keepdims=True)
        )
        p_w = jnp.exp(p_scores - peak)
        t_w = jnp.exp(t_scores - peak)
        mass = jnp.sum(p_w, axis=1, keepdims=True) + jnp.sum(t_w, axis=1, keepdims=True)
        numer = jnp.dot(
            p_w.astype(jnp.bfloat16), v_ref[0, :, cols], preferred_element_type=jnp.float32
        )
        for _, tv_ref, _, first in sources:
            for r in range(per_core):
                t_w16 = jnp.where(row_sample == first + r, t_w, 0.0).astype(jnp.bfloat16)
                numer = numer + jnp.dot(
                    t_w16, tv_ref[0, r, :, cols], preferred_element_type=jnp.float32
                )
        out_ref[j, :rows_n, :] = numer
        stat_rows = []
        for col in (peak, mass):
            for c in range(rows_n // DH):
                part = jnp.broadcast_to(col[c * DH:(c + 1) * DH], (DH, DH))
                stat_rows.append(jnp.transpose(part)[0:1])
        pad = out_ref.shape[1] - rows_n - len(stat_rows)
        out_ref[j, rows_n:, :] = jnp.concatenate(
            stat_rows + [jnp.zeros((pad, DH), jnp.float32)], axis=0
        )


def _attend_pairs(u, q_rows, prefix_kv, tail_own, tail_peer, valid_own, valid_peer, group):
    heads_n, rows_n, _ = q_rows.shape
    prefix_dev = prefix_kv.shape[1]
    per_core, tail_dev = tail_own.shape[1], tail_own.shape[2]
    width = heads_n * DH
    n_out = rows_n + 8 * (-(-(2 * rows_n // DH) // 8))
    grid_spec = pltpu.PrefetchScalarGridSpec(
        num_scalar_prefetch=1,
        grid=(1,),
        in_specs=[
            pl.BlockSpec((heads_n, rows_n, DH), lambda i, u_ref: (0, 0, 0)),
            pl.BlockSpec((1, prefix_dev, width), lambda i, u_ref: (0, 0, u_ref[0])),
            pl.BlockSpec((1, prefix_dev, width), lambda i, u_ref: (1, 0, u_ref[0])),
            pl.BlockSpec((1, per_core, tail_dev, width), lambda i, u_ref: (0, 0, 0, u_ref[0])),
            pl.BlockSpec((1, per_core, tail_dev, width), lambda i, u_ref: (1, 0, 0, u_ref[0])),
            pl.BlockSpec((1, per_core, tail_dev, width), lambda i, u_ref: (0, 0, 0, 0)),
            pl.BlockSpec((1, per_core, tail_dev, width), lambda i, u_ref: (1, 0, 0, 0)),
            pl.BlockSpec((per_core, tail_dev), lambda i, u_ref: (0, 0)),
            pl.BlockSpec((per_core, tail_dev), lambda i, u_ref: (0, 0)),
        ],
        out_specs=pl.BlockSpec((heads_n, n_out, DH), lambda i, u_ref: (0, 0, 0)),
    )
    flops = 4 * heads_n * rows_n * DH * (prefix_dev + 2 * per_core * tail_dev)
    return pl.pallas_call(
        functools.partial(_pairs_kernel, group=group),
        grid_spec=grid_spec,
        out_shape=jax.ShapeDtypeStruct((heads_n, n_out, DH), jnp.float32),
        cost_estimate=pl.CostEstimate(
            flops=flops,
            transcendentals=heads_n * rows_n * (prefix_dev + 2 * per_core * tail_dev),
            bytes_accessed=2 * (2 * prefix_dev * width + 4 * per_core * tail_dev * width
                                + q_rows.size) + 4 * heads_n * n_out * DH,
        ),
    )(jnp.reshape(u, (1,)).astype(jnp.int32), q_rows, prefix_kv, prefix_kv, tail_own, tail_own,
      tail_peer, tail_peer, valid_own, valid_peer)


def _linear(t, s):
    return t * 2 + s


def _g_pairs(k, chips):
    quarter = chips // 2
    pairs = []
    for t in range(chips):
        h, i = t // quarter, t % quarter
        pairs.append((_linear(t, h), _linear((1 - h) * quarter + (i + k) % quarter, h)))
        if k < quarter:
            pairs.append((_linear(t, 1 - h), _linear(h * quarter + (i + k) % quarter, h)))
    return pairs


def _e_pairs(k, chips):
    quarter = chips // 2
    pairs = []
    for t in range(chips):
        h, i = t // quarter, t % quarter
        for u in (0, 1):
            dst = u * quarter + (i + k) % quarter
            if h != u:
                pairs.append((_linear(t, u), _linear(dst, 1 - u)))
            elif k < quarter:
                pairs.append((_linear(t, u), _linear(dst, u)))
    return pairs


def _combine(src, rows_n):
    n = src.shape[0]
    numer = src[:, :rows_n]
    stat = src[:, rows_n:rows_n + 2 * rows_n // DH].reshape(n, 2, rows_n)
    peak, mass = stat[:, 0], stat[:, 1]
    top = peak.max(0)
    w = jnp.exp(peak - top[None])
    return (numer * w[..., None]).sum(0), top, (mass * w).sum(0)


def _attention_pairs(queries, prefix_kv, tail_kv, tail_lengths, fresh_kv, tp_count, tp_rank,
                     sub_rank, group):
    steps_n, rows_dev, width_dev = queries.shape
    quarter = tp_count // 2
    tail_dev = tail_kv.shape[2]
    u = sub_rank
    i = tp_rank % quarter
    within = tp_rank // quarter == u
    swap = [(0, 1), (1, 0)]
    peer_cols = lax.dynamic_slice_in_dim(tail_kv, (1 - u) * quarter * DH, quarter * DH, 3)
    tail_peer = lax.ppermute(peer_cols, "sub", swap)
    lengths_peer = lax.ppermute(tail_lengths, "sub", swap)
    fresh_peer = lax.ppermute(fresh_kv, "sub", swap)
    t_pos = tp_rank * tail_dev + jnp.arange(tail_dev)
    valid_own = (t_pos[None, :] < tail_lengths[:, None]).astype(jnp.float32)
    valid_peer = (t_pos[None, :] < lengths_peer[:, None]).astype(jnp.float32)

    q_both = lax.all_gather(queries, "sub", axis=1, tiled=True)
    blocks = []
    for k in range(1, quarter + 1):
        got = lax.ppermute(q_both, ("tp", "sub"), _g_pairs(k, tp_count))
        if k == quarter:
            got = jnp.where(within, q_both, got)
        blocks.append(got)
    order = (i - jnp.arange(1, quarter + 1)) % quarter
    q_heads = jnp.zeros((quarter,) + q_both.shape, q_both.dtype).at[order].set(jnp.stack(blocks))
    q_rows = q_heads.reshape(quarter, -1, DH)
    rows_n = q_rows.shape[1]
    part = _attend_pairs(u, q_rows, prefix_kv, tail_kv, tail_peer, valid_own, valid_peer, group)

    srcs = []
    for k in range(1, quarter + 1):
        send = lax.dynamic_index_in_dim(part, (i + k) % quarter, 0, keepdims=False)
        got = lax.ppermute(send, ("tp", "sub"), _e_pairs(k, tp_count))
        if k == quarter:
            own = lax.dynamic_index_in_dim(part, i, 0, keepdims=False)
            got = jnp.where(within, own, got)
        srcs.append(got)
    numer_c, peak_c, mass_c = _combine(jnp.stack(srcs), rows_n)
    n_stat = part.shape[1] - rows_n
    stats = jnp.concatenate([peak_c, mass_c]).reshape(-1, DH)
    stats = jnp.pad(stats, ((0, n_stat - stats.shape[0]), (0, 0)))
    both = lax.all_gather(jnp.concatenate([numer_c, stats]), "sub", axis=0, tiled=False)
    numer_2 = both[:, :rows_n]
    stat_2 = both[:, rows_n:rows_n + 2 * rows_n // DH].reshape(2, 2, rows_n)

    heads_dev = width_dev // DH
    score_scale = 1.0 / math.sqrt(DH)
    fresh_all = jnp.where(
        u == 0, jnp.concatenate([fresh_kv, fresh_peer], 2), jnp.concatenate([fresh_peer, fresh_kv], 2)
    )
    f_kv = lax.dynamic_slice_in_dim(fresh_all, tp_rank * DH, DH, 3)
    own_query = q_both.reshape(steps_n, 2 * rows_dev, heads_dev, DH)
    f_scores = (
        jnp.einsum("sbhd,ubd->sbhu", own_query, f_kv[0], preferred_element_type=jnp.float32)
        * score_scale
    )
    fresh_live = jnp.arange(steps_n)[None, :] <= jnp.arange(steps_n)[:, None]
    f_scores = jnp.where(fresh_live[:, None, None, :], f_scores, NEG_FILL).reshape(rows_n, steps_n)
    peak_2 = stat_2[:, 0]
    top = jnp.maximum(peak_2.max(0), f_scores.max(-1))
    w2 = jnp.exp(peak_2 - top[None])
    f_w = jnp.exp(f_scores - top[:, None])
    mass = (stat_2[:, 1] * w2).sum(0) + f_w.sum(-1)
    numer = (numer_2 * w2[..., None]).sum(0)
    f_w16 = f_w.astype(jnp.bfloat16).reshape(steps_n, 2 * rows_dev, heads_dev, steps_n)
    numer = numer + jnp.einsum(
        "sbhu,ubd->sbhd", f_w16, f_kv[1], preferred_element_type=jnp.float32
    ).reshape(rows_n, DH)
    attended = (numer / mass[:, None]).astype(jnp.bfloat16)
    return attended.reshape(steps_n, 2 * rows_dev, width_dev)


def per_device(
    queries, prefix_kv, tail_kv, tail_lengths, fresh_kv, out_weight, scale_in, scale_out, residual
):
    steps_n, rows_dev, width_dev = queries.shape
    heads_dev = width_dev // DH
    tp_count = lax.axis_size("tp")
    tp_rank = lax.axis_index("tp")
    sub_rank = lax.axis_index("sub")
    kv_heads = prefix_kv.shape[2] // DH
    heads_all = heads_dev * tp_count
    group = heads_all // kv_heads
    prefix_dev = prefix_kv.shape[1]
    tail_dev = tail_kv.shape[2]
    score_scale = 1.0 / math.sqrt(DH)

    pairs_ok = (
        tp_count == kv_heads and heads_dev == group and tp_count % 4 == 0
        and lax.axis_size("sub") == 2
    )
    if pairs_ok:
        gathered = _attention_pairs(
            queries, prefix_kv, tail_kv, tail_lengths, fresh_kv, tp_count, tp_rank, sub_rank, group
        )
        return _project(gathered, out_weight, scale_in, scale_out, residual, tp_count, tp_rank,
                        sub_rank)
    q_blocks = _gather_blocks(queries, "tp", tp_count)
    q_all = jnp.moveaxis(q_blocks, 0, 2).reshape(steps_n, rows_dev, kv_heads, group, DH)
    q_rows = jnp.transpose(q_all, (2, 1, 0, 3, 4)).reshape(kv_heads, -1, DH)
    t_pos = tp_rank * tail_dev + jnp.arange(tail_dev)
    valid = (t_pos[None, :] < tail_lengths[:, None]).astype(jnp.float32)
    k_numer, k_peak, k_mass = _attend_local(q_rows, prefix_kv, tail_kv, valid)

    def by_owner(x):
        x = jnp.transpose(x, (2, 1, 0, 3) + tuple(range(4, x.ndim)))
        x = x.reshape((steps_n, rows_dev, tp_count, heads_dev) + x.shape[4:])
        return jnp.moveaxis(x, 2, 0)

    grid4 = (kv_heads, rows_dev, steps_n, group)
    o_numer = by_owner(k_numer.reshape(grid4 + (DH,))).reshape(tp_count, -1, DH)
    o_peak = by_owner(k_peak[..., 0].reshape(grid4)).reshape(tp_count, -1)
    o_mass = by_owner(k_mass[..., 0].reshape(grid4)).reshape(tp_count, -1)
    n_rows = steps_n * rows_dev * heads_dev
    n_stat = -(-2 * n_rows // DH)
    stats = jnp.concatenate([o_peak, o_mass], axis=1)
    stats = jnp.pad(stats, ((0, 0), (0, n_stat * DH - 2 * n_rows))).reshape(tp_count, n_stat, DH)
    got = _exchange(jnp.concatenate([o_numer, stats], axis=1), "tp", tp_count)
    got_numer = got[:, :n_rows].reshape(tp_count, steps_n, rows_dev, heads_dev, DH)
    got_stats = got[:, n_rows:].reshape(tp_count, -1)[:, : 2 * n_rows]
    got_stats = got_stats.reshape(tp_count, 2, steps_n, rows_dev, heads_dev)
    got_peak = got_stats[:, 0]
    got_mass = got_stats[:, 1]

    own_query = queries.reshape(steps_n, rows_dev, heads_dev, DH)
    f_kv = fresh_kv.reshape(2, steps_n, rows_dev, kv_heads, DH)
    if group % heads_dev == 0:
        one_kv = lax.dynamic_index_in_dim(f_kv, tp_rank * heads_dev // group, 3, keepdims=True)
        f_kv = jnp.broadcast_to(one_kv, (2, steps_n, rows_dev, heads_dev, DH))
    else:
        kv_of_head = (tp_rank * heads_dev + jnp.arange(heads_dev)) // group
        f_kv = jnp.take(f_kv, kv_of_head, axis=3)
    f_scores = (
        jnp.einsum("sbhd,ubhd->sbhu", own_query, f_kv[0], preferred_element_type=jnp.float32)
        * score_scale
    )
    fresh_live = jnp.arange(steps_n)[None, :] <= jnp.arange(steps_n)[:, None]
    f_scores = jnp.where(fresh_live[:, None, None, :], f_scores, NEG_FILL)

    peak = jnp.maximum(got_peak.max(0), f_scores.max(-1))
    rescale = jnp.exp(got_peak - peak[None])
    f_w = jnp.exp(f_scores - peak[..., None])
    mass = (got_mass * rescale).sum(0) + f_w.sum(-1)
    numer = (got_numer * rescale[..., None]).sum(0)
    numer = numer + jnp.einsum(
        "sbhu,ubhd->sbhd", f_w.astype(jnp.bfloat16), f_kv[1], preferred_element_type=jnp.float32
    )
    attended = (numer / mass[..., None]).astype(jnp.bfloat16).reshape(steps_n, rows_dev, width_dev)

    gathered = lax.all_gather(attended, "sub", axis=1, tiled=True)
    return _project(gathered, out_weight, scale_in, scale_out, residual, tp_count, tp_rank,
                    sub_rank)


def _project(gathered, out_weight, scale_in, scale_out, residual, tp_count, tp_rank, sub_rank):
    steps_n, samples, width_dev = gathered.shape
    heads_dev = width_dev // DH
    local_width = out_weight.shape[1]
    head_rows_in = gathered.reshape(steps_n * samples, heads_dev, DH)
    head_weights = out_weight.reshape(heads_dev, DH, local_width)
    scale_a = jnp.repeat(jnp.exp2(-scale_in.astype(jnp.float32)), 128)
    scale_b = jnp.repeat(jnp.exp2(-scale_out.astype(jnp.float32)), 128)
    local_a = lax.dynamic_slice_in_dim(scale_a, sub_rank * local_width, local_width, 0)
    local_b = lax.dynamic_slice_in_dim(scale_b, sub_rank * local_width, local_width, 0)
    per_head_term = jnp.einsum(
        "rhd,hdf->rhf", head_rows_in, head_weights, preferred_element_type=jnp.float32
    )
    clipped = jnp.clip(per_head_term / local_a[None, None, :], -127.0, 127.0).sum(1)

    piece_cols = local_width // tp_count
    pieces = jnp.moveaxis(clipped.reshape(steps_n * samples, tp_count, piece_cols), 1, 0)
    got_pieces = _exchange(pieces, "tp", tp_count)
    summed = got_pieces.sum(0)
    piece_start = sub_rank * local_width + tp_rank * piece_cols
    piece_a = lax.dynamic_slice_in_dim(scale_a, piece_start, piece_cols, 0)
    piece_b = lax.dynamic_slice_in_dim(scale_b, piece_start, piece_cols, 0)
    levels = jnp.clip(summed * piece_a / piece_b, -127.0, 127.0).astype(jnp.bfloat16)
    level_blocks = _gather_blocks(levels, "tp", tp_count)
    all_levels = jnp.moveaxis(level_blocks, 0, 1).reshape(steps_n * samples, local_width)
    restored = all_levels.astype(jnp.float32) * local_b
    hidden = residual.reshape(steps_n * samples, local_width).astype(jnp.float32) + restored
    return hidden.astype(jnp.bfloat16).reshape(steps_n, samples, local_width)


def solution(mesh):
    return jax.shard_map(
        per_device,
        mesh=mesh,
        in_specs=(
            P(None, ("rep", "sub"), "tp"),
            P(None, ("rep", "tp"), None),
            P(None, ("rep", "sub"), "tp", None),
            P(("rep", "sub")),
            P(None, None, ("rep", "sub"), None),
            P("tp", "sub"),
            P(),
            P(),
            P(None, "rep", "sub"),
        ),
        out_specs=P(None, "rep", "sub"),
        check_vma=False,
    )
```

```python
import functools
import math

import jax
import jax.numpy as jnp
from jax import lax
from jax.experimental import pallas as pl
from jax.experimental.pallas import tpu as pltpu
from jax.sharding import PartitionSpec as P

DH = 128


NEG_FILL = -1e30


def _is_pow2(n):
    return n >= 1 and (n & (n - 1)) == 0


def _gather_blocks(x, axis_name, count):
    if count == 1:
        return x[None]
    if not _is_pow2(count):
        return lax.all_gather(x, axis_name, axis=0, tiled=False)
    me = lax.axis_index(axis_name)
    if count <= 8:
        other = lax.ppermute(x, axis_name, [(i, i ^ 1) for i in range(count)])
        low = me % 2 == 0
        pair = jnp.where(low, jnp.stack([x, other]), jnp.stack([other, x]))
        pairs = [pair]
        for d in range(1, count // 2):
            pairs.append(
                lax.ppermute(pair, axis_name, [(i, (i + 2 * d) % count) for i in range(count)])
            )
        order = (me // 2 - jnp.arange(count // 2)) % (count // 2)
        placed = jnp.zeros((count // 2,) + pair.shape, pair.dtype).at[order].set(jnp.stack(pairs))
        return placed.reshape((count,) + x.shape)
    cur = x[None]
    k = 1
    while k < count:
        other = lax.ppermute(cur, axis_name, [(i, i ^ k) for i in range(count)])
        low = (me // k) % 2 == 0
        cur = jnp.where(low, jnp.concatenate([cur, other]), jnp.concatenate([other, cur]))
        k *= 2
    return cur


def _exchange(blocks, axis_name, count, direct_max=8):
    if count == 1:
        return blocks
    if count > direct_max:
        return jax.tree.map(
            lambda b: lax.all_to_all(b, axis_name, split_axis=0, concat_axis=0, tiled=True), blocks
        )
    me = lax.axis_index(axis_name)
    got = [jax.tree.map(lambda b: lax.dynamic_index_in_dim(b, me, 0, keepdims=False), blocks)]
    for k in range(1, count):
        dst = (me + k) % count
        send = jax.tree.map(lambda b: lax.dynamic_index_in_dim(b, dst, 0, keepdims=False), blocks)
        got.append(lax.ppermute(send, axis_name, [(i, (i + k) % count) for i in range(count)]))
    return jax.tree.map(lambda *xs: jnp.stack(xs), *got)


def _attend_kernel(q_ref, k_ref, v_ref, tk_ref, tv_ref, valid_ref, numer_ref, peak_ref, mass_ref):
    heads_n, rows_n = q_ref.shape[0], q_ref.shape[1]
    samples = tk_ref.shape[1]
    per_sample = rows_n // samples
    score_scale = 1.0 / math.sqrt(DH)
    dims_nt = (((1,), (1,)), ((), ()))
    for j in range(heads_n):
        cols = slice(j * DH, (j + 1) * DH)
        q = q_ref[j]
        p_scores = lax.dot_general(q, k_ref[0, :, cols], dims_nt, preferred_element_type=jnp.float32)
        p_scores = p_scores * score_scale
        t_parts = []
        for r in range(samples):
            qr = q[r * per_sample:(r + 1) * per_sample]
            sr = lax.dot_general(
                qr, tk_ref[0, r, :, cols], dims_nt, preferred_element_type=jnp.float32
            )
            sr = sr * score_scale
            t_parts.append(jnp.where(valid_ref[r:r + 1, :] > 0.0, sr, NEG_FILL))
        t_scores = jnp.concatenate(t_parts, axis=0)
        peak = jnp.maximum(
            jnp.max(p_scores, axis=1, keepdims=True), jnp.max(t_scores, axis=1, keepdims=True)
        )
        p_w = jnp.exp(p_scores - peak)
        t_w = jnp.exp(t_scores - peak)
        mass = jnp.sum(p_w, axis=1, keepdims=True) + jnp.sum(t_w, axis=1, keepdims=True)
        numer = jnp.dot(
            p_w.astype(jnp.bfloat16), v_ref[0, :, cols], preferred_element_type=jnp.float32
        )
        t_w16 = t_w.astype(jnp.bfloat16)
        t_numer = [
            jnp.dot(
                t_w16[r * per_sample:(r + 1) * per_sample], tv_ref[0, r, :, cols],
                preferred_element_type=jnp.float32,
            )
            for r in range(samples)
        ]
        numer_ref[j] = numer + jnp.concatenate(t_numer, axis=0)
        peak_ref[j] = jnp.broadcast_to(peak, peak_ref.shape[1:])
        mass_ref[j] = jnp.broadcast_to(mass, mass_ref.shape[1:])


def _attend_local(q_rows, prefix_kv, tail_kv, valid):
    kv_heads, rows_n, _ = q_rows.shape
    prefix_dev = prefix_kv.shape[1]
    samples, tail_dev = tail_kv.shape[1], tail_kv.shape[2]
    flops = 4 * kv_heads * rows_n * DH * (prefix_dev + tail_dev)
    bytes_in = 2 * (prefix_kv.size + tail_kv.size + q_rows.size)
    per_step = 4 if kv_heads % 4 == 0 else 1
    width = per_step * DH
    return pl.pallas_call(
        _attend_kernel,
        grid=(kv_heads // per_step,),
        in_specs=[
            pl.BlockSpec((per_step, rows_n, DH), lambda k: (k, 0, 0)),
            pl.BlockSpec((1, prefix_dev, width), lambda k: (0, 0, k)),
            pl.BlockSpec((1, prefix_dev, width), lambda k: (1, 0, k)),
            pl.BlockSpec((1, samples, tail_dev, width), lambda k: (0, 0, 0, k)),
            pl.BlockSpec((1, samples, tail_dev, width), lambda k: (1, 0, 0, k)),
            pl.BlockSpec((samples, tail_dev), lambda k: (0, 0)),
        ],
        out_specs=[
            pl.BlockSpec((per_step, rows_n, DH), lambda k: (k, 0, 0)),
            pl.BlockSpec((per_step, rows_n, DH), lambda k: (k, 0, 0)),
            pl.BlockSpec((per_step, rows_n, DH), lambda k: (k, 0, 0)),
        ],
        out_shape=[jax.ShapeDtypeStruct((kv_heads, rows_n, DH), jnp.float32)] * 3,
        cost_estimate=pl.CostEstimate(
            flops=flops,
            transcendentals=kv_heads * rows_n * (prefix_dev + tail_dev),
            bytes_accessed=bytes_in + 3 * 4 * kv_heads * rows_n * DH,
        ),
        compiler_params=pltpu.CompilerParams(vmem_limit_bytes=48 * 1024 * 1024),
    )(q_rows, prefix_kv, prefix_kv, tail_kv, tail_kv, valid)


def _pairs_kernel(u_ref, q_ref, k_ref, v_ref, tko_ref, tvo_ref, tkp_ref, tvp_ref,
                  valid_o_ref, valid_p_ref, out_ref, *, group):
    heads_n, rows_n = q_ref.shape[0], q_ref.shape[1]
    per_core, tail_dev = tko_ref.shape[1], tko_ref.shape[2]
    samples = 2 * per_core
    u = u_ref[0]
    score_scale = 1.0 / math.sqrt(DH)
    dims_nt = (((1,), (1,)), ((), ()))
    row_sample = (lax.broadcasted_iota(jnp.int32, (rows_n, tail_dev), 0) // group) % samples
    sources = [(tko_ref, tvo_ref, valid_o_ref, u * per_core),
               (tkp_ref, tvp_ref, valid_p_ref, (1 - u) * per_core)]
    for j in range(heads_n):
        cols = slice(j * DH, (j + 1) * DH)
        q = q_ref[j]
        p_scores = lax.dot_general(q, k_ref[0, :, cols], dims_nt, preferred_element_type=jnp.float32)
        p_scores = p_scores * score_scale
        t_scores = jnp.full((rows_n, tail_dev), NEG_FILL, jnp.float32)
        for tk_ref, _, valid_ref, first in sources:
            for r in range(per_core):
                sr = lax.dot_general(
                    q, tk_ref[0, r, :, cols], dims_nt, preferred_element_type=jnp.float32
                )
                live = (row_sample == first + r) & (valid_ref[r:r + 1, :] > 0.0)
                t_scores = jnp.where(live, sr * score_scale, t_scores)
        peak = jnp.maximum(
            jnp.max(p_scores, axis=1, keepdims=True), jnp.max(t_scores, axis=1, keepdims=True)
        )
        p_w = jnp.exp(p_scores - peak)
        t_w = jnp.exp(t_scores - peak)
        mass = jnp.sum(p_w, axis=1, keepdims=True) + jnp.sum(t_w, axis=1, keepdims=True)
        numer = jnp.dot(
            p_w.astype(jnp.bfloat16), v_ref[0, :, cols], preferred_element_type=jnp.float32
        )
        for _, tv_ref, _, first in sources:
            for r in range(per_core):
                t_w16 = jnp.where(row_sample == first + r, t_w, 0.0).astype(jnp.bfloat16)
                numer = numer + jnp.dot(
                    t_w16, tv_ref[0, r, :, cols], preferred_element_type=jnp.float32
                )
        out_ref[j, :rows_n, :] = numer
        stat_rows = []
        for col in (peak, mass):
            for c in range(rows_n // DH):
                part = jnp.broadcast_to(col[c * DH:(c + 1) * DH], (DH, DH))
                stat_rows.append(jnp.transpose(part)[0:1])
        pad = out_ref.shape[1] - rows_n - len(stat_rows)
        out_ref[j, rows_n:, :] = jnp.concatenate(
            stat_rows + [jnp.zeros((pad, DH), jnp.float32)], axis=0
        )


def _attend_pairs(u, q_rows, prefix_kv, tail_own, tail_peer, valid_own, valid_peer, group):
    heads_n, rows_n, _ = q_rows.shape
    prefix_dev = prefix_kv.shape[1]
    per_core, tail_dev = tail_own.shape[1], tail_own.shape[2]
    width = heads_n * DH
    n_out = rows_n + 8 * (-(-(2 * rows_n // DH) // 8))
    grid_spec = pltpu.PrefetchScalarGridSpec(
        num_scalar_prefetch=1,
        grid=(1,),
        in_specs=[
            pl.BlockSpec((heads_n, rows_n, DH), lambda i, u_ref: (0, 0, 0)),
            pl.BlockSpec((1, prefix_dev, width), lambda i, u_ref: (0, 0, u_ref[0])),
            pl.BlockSpec((1, prefix_dev, width), lambda i, u_ref: (1, 0, u_ref[0])),
            pl.BlockSpec((1, per_core, tail_dev, width), lambda i, u_ref: (0, 0, 0, u_ref[0])),
            pl.BlockSpec((1, per_core, tail_dev, width), lambda i, u_ref: (1, 0, 0, u_ref[0])),
            pl.BlockSpec((1, per_core, tail_dev, width), lambda i, u_ref: (0, 0, 0, 0)),
            pl.BlockSpec((1, per_core, tail_dev, width), lambda i, u_ref: (1, 0, 0, 0)),
            pl.BlockSpec((per_core, tail_dev), lambda i, u_ref: (0, 0)),
            pl.BlockSpec((per_core, tail_dev), lambda i, u_ref: (0, 0)),
        ],
        out_specs=pl.BlockSpec((heads_n, n_out, DH), lambda i, u_ref: (0, 0, 0)),
    )
    flops = 4 * heads_n * rows_n * DH * (prefix_dev + 2 * per_core * tail_dev)
    return pl.pallas_call(
        functools.partial(_pairs_kernel, group=group),
        grid_spec=grid_spec,
        out_shape=jax.ShapeDtypeStruct((heads_n, n_out, DH), jnp.float32),
        cost_estimate=pl.CostEstimate(
            flops=flops,
            transcendentals=heads_n * rows_n * (prefix_dev + 2 * per_core * tail_dev),
            bytes_accessed=2 * (2 * prefix_dev * width + 4 * per_core * tail_dev * width
                                + q_rows.size) + 4 * heads_n * n_out * DH,
        ),
    )(jnp.reshape(u, (1,)).astype(jnp.int32), q_rows, prefix_kv, prefix_kv, tail_own, tail_own,
      tail_peer, tail_peer, valid_own, valid_peer)


def _linear(t, s):
    return t * 2 + s


def _g_pairs(k, chips):
    quarter = chips // 2
    pairs = []
    for t in range(chips):
        h, i = t // quarter, t % quarter
        pairs.append((_linear(t, h), _linear((1 - h) * quarter + (i + k) % quarter, h)))
        if k < quarter:
            pairs.append((_linear(t, 1 - h), _linear(h * quarter + (i + k) % quarter, h)))
    return pairs


def _e_pairs(k, chips):
    quarter = chips // 2
    pairs = []
    for t in range(chips):
        h, i = t // quarter, t % quarter
        for u in (0, 1):
            dst = u * quarter + (i + k) % quarter
            if h != u:
                pairs.append((_linear(t, u), _linear(dst, 1 - u)))
            elif k < quarter:
                pairs.append((_linear(t, u), _linear(dst, u)))
    return pairs


def _combine(src, rows_n):
    n = src.shape[0]
    numer = src[:, :rows_n]
    stat = src[:, rows_n:rows_n + 2 * rows_n // DH].reshape(n, 2, rows_n)
    peak, mass = stat[:, 0], stat[:, 1]
    top = peak.max(0)
    w = jnp.exp(peak - top[None])
    return (numer * w[..., None]).sum(0), top, (mass * w).sum(0)


def _attention_pairs(queries, prefix_kv, tail_kv, tail_lengths, fresh_kv, tp_count, tp_rank,
                     sub_rank, group):
    steps_n, rows_dev, width_dev = queries.shape
    quarter = tp_count // 2
    tail_dev = tail_kv.shape[2]
    u = sub_rank
    i = tp_rank % quarter
    within = tp_rank // quarter == u
    swap = [(0, 1), (1, 0)]
    t_pos = tp_rank * tail_dev + jnp.arange(tail_dev)
    valid_own = (t_pos[None, :] < tail_lengths[:, None]).astype(jnp.float32)
    peer_cols = lax.dynamic_slice_in_dim(tail_kv, (1 - u) * quarter * DH, quarter * DH, 3)
    lane = quarter * DH
    parcel = jnp.concatenate([
        peer_cols.reshape(-1, lane),
        fresh_kv.reshape(-1, lane),
        jnp.pad(valid_own.astype(jnp.bfloat16).reshape(-1), (0, -valid_own.size % lane)).reshape(-1, lane),
    ])
    parcel = lax.ppermute(parcel, "sub", swap)
    n_tail = peer_cols.size // lane
    n_fresh = fresh_kv.size // lane
    tail_peer = parcel[:n_tail].reshape(peer_cols.shape)
    fresh_peer = parcel[n_tail:n_tail + n_fresh].reshape(fresh_kv.shape)
    valid_peer = parcel[n_tail + n_fresh:].reshape(-1)[: valid_own.size]
    valid_peer = valid_peer.reshape(valid_own.shape).astype(jnp.float32)

    q_both = lax.all_gather(queries, "sub", axis=1, tiled=True)
    blocks = []
    for k in range(1, quarter + 1):
        got = lax.ppermute(q_both, ("tp", "sub"), _g_pairs(k, tp_count))
        if k == quarter:
            got = jnp.where(within, q_both, got)
        blocks.append(got)
    order = (i - jnp.arange(1, quarter + 1)) % quarter
    q_heads = jnp.zeros((quarter,) + q_both.shape, q_both.dtype).at[order].set(jnp.stack(blocks))
    q_rows = q_heads.reshape(quarter, -1, DH)
    rows_n = q_rows.shape[1]
    part = _attend_pairs(u, q_rows, prefix_kv, tail_kv, tail_peer, valid_own, valid_peer, group)

    srcs = []
    for k in range(1, quarter + 1):
        send = lax.dynamic_index_in_dim(part, (i + k) % quarter, 0, keepdims=False)
        got = lax.ppermute(send, ("tp", "sub"), _e_pairs(k, tp_count))
        if k == quarter:
            own = lax.dynamic_index_in_dim(part, i, 0, keepdims=False)
            got = jnp.where(within, own, got)
        srcs.append(got)
    numer_c, peak_c, mass_c = _combine(jnp.stack(srcs), rows_n)
    n_stat = part.shape[1] - rows_n
    stats = jnp.concatenate([peak_c, mass_c]).reshape(-1, DH)
    stats = jnp.pad(stats, ((0, n_stat - stats.shape[0]), (0, 0)))
    mine = jnp.concatenate([numer_c, stats])
    theirs = lax.ppermute(mine, "sub", swap)
    both = jnp.where(u == 0, jnp.stack([mine, theirs]), jnp.stack([theirs, mine]))
    numer_2 = both[:, :rows_n]
    stat_2 = both[:, rows_n:rows_n + 2 * rows_n // DH].reshape(2, 2, rows_n)

    heads_dev = width_dev // DH
    score_scale = 1.0 / math.sqrt(DH)
    fresh_all = jnp.where(
        u == 0, jnp.concatenate([fresh_kv, fresh_peer], 2), jnp.concatenate([fresh_peer, fresh_kv], 2)
    )
    f_kv = lax.dynamic_slice_in_dim(fresh_all, tp_rank * DH, DH, 3)
    own_query = q_both.reshape(steps_n, 2 * rows_dev, heads_dev, DH)
    f_scores = (
        jnp.einsum("sbhd,ubd->sbhu", own_query, f_kv[0], preferred_element_type=jnp.float32)
        * score_scale
    )
    fresh_live = jnp.arange(steps_n)[None, :] <= jnp.arange(steps_n)[:, None]
    f_scores = jnp.where(fresh_live[:, None, None, :], f_scores, NEG_FILL).reshape(rows_n, steps_n)
    peak_2 = stat_2[:, 0]
    top = jnp.maximum(peak_2.max(0), f_scores.max(-1))
    w2 = jnp.exp(peak_2 - top[None])
    f_w = jnp.exp(f_scores - top[:, None])
    mass = (stat_2[:, 1] * w2).sum(0) + f_w.sum(-1)
    numer = (numer_2 * w2[..., None]).sum(0)
    f_w16 = f_w.astype(jnp.bfloat16).reshape(steps_n, 2 * rows_dev, heads_dev, steps_n)
    numer = numer + jnp.einsum(
        "sbhu,ubd->sbhd", f_w16, f_kv[1], preferred_element_type=jnp.float32
    ).reshape(rows_n, DH)
    attended = (numer / mass[:, None]).astype(jnp.bfloat16)
    return attended.reshape(steps_n, 2 * rows_dev, width_dev)


def per_device(
    queries, prefix_kv, tail_kv, tail_lengths, fresh_kv, out_weight, scale_in, scale_out, residual
):
    steps_n, rows_dev, width_dev = queries.shape
    heads_dev = width_dev // DH
    tp_count = lax.axis_size("tp")
    tp_rank = lax.axis_index("tp")
    sub_rank = lax.axis_index("sub")
    kv_heads = prefix_kv.shape[2] // DH
    heads_all = heads_dev * tp_count
    group = heads_all // kv_heads
    prefix_dev = prefix_kv.shape[1]
    tail_dev = tail_kv.shape[2]
    score_scale = 1.0 / math.sqrt(DH)

    pairs_ok = (
        tp_count == kv_heads and heads_dev == group and tp_count % 4 == 0
        and lax.axis_size("sub") == 2
    )
    if pairs_ok:
        gathered = _attention_pairs(
            queries, prefix_kv, tail_kv, tail_lengths, fresh_kv, tp_count, tp_rank, sub_rank, group
        )
        return _project(gathered, out_weight, scale_in, scale_out, residual, tp_count, tp_rank,
                        sub_rank)
    q_blocks = _gather_blocks(queries, "tp", tp_count)
    q_all = jnp.moveaxis(q_blocks, 0, 2).reshape(steps_n, rows_dev, kv_heads, group, DH)
    q_rows = jnp.transpose(q_all, (2, 1, 0, 3, 4)).reshape(kv_heads, -1, DH)
    t_pos = tp_rank * tail_dev + jnp.arange(tail_dev)
    valid = (t_pos[None, :] < tail_lengths[:, None]).astype(jnp.float32)
    k_numer, k_peak, k_mass = _attend_local(q_rows, prefix_kv, tail_kv, valid)

    def by_owner(x):
        x = jnp.transpose(x, (2, 1, 0, 3) + tuple(range(4, x.ndim)))
        x = x.reshape((steps_n, rows_dev, tp_count, heads_dev) + x.shape[4:])
        return jnp.moveaxis(x, 2, 0)

    grid4 = (kv_heads, rows_dev, steps_n, group)
    o_numer = by_owner(k_numer.reshape(grid4 + (DH,))).reshape(tp_count, -1, DH)
    o_peak = by_owner(k_peak[..., 0].reshape(grid4)).reshape(tp_count, -1)
    o_mass = by_owner(k_mass[..., 0].reshape(grid4)).reshape(tp_count, -1)
    n_rows = steps_n * rows_dev * heads_dev
    n_stat = -(-2 * n_rows // DH)
    stats = jnp.concatenate([o_peak, o_mass], axis=1)
    stats = jnp.pad(stats, ((0, 0), (0, n_stat * DH - 2 * n_rows))).reshape(tp_count, n_stat, DH)
    got = _exchange(jnp.concatenate([o_numer, stats], axis=1), "tp", tp_count)
    got_numer = got[:, :n_rows].reshape(tp_count, steps_n, rows_dev, heads_dev, DH)
    got_stats = got[:, n_rows:].reshape(tp_count, -1)[:, : 2 * n_rows]
    got_stats = got_stats.reshape(tp_count, 2, steps_n, rows_dev, heads_dev)
    got_peak = got_stats[:, 0]
    got_mass = got_stats[:, 1]

    own_query = queries.reshape(steps_n, rows_dev, heads_dev, DH)
    f_kv = fresh_kv.reshape(2, steps_n, rows_dev, kv_heads, DH)
    if group % heads_dev == 0:
        one_kv = lax.dynamic_index_in_dim(f_kv, tp_rank * heads_dev // group, 3, keepdims=True)
        f_kv = jnp.broadcast_to(one_kv, (2, steps_n, rows_dev, heads_dev, DH))
    else:
        kv_of_head = (tp_rank * heads_dev + jnp.arange(heads_dev)) // group
        f_kv = jnp.take(f_kv, kv_of_head, axis=3)
    f_scores = (
        jnp.einsum("sbhd,ubhd->sbhu", own_query, f_kv[0], preferred_element_type=jnp.float32)
        * score_scale
    )
    fresh_live = jnp.arange(steps_n)[None, :] <= jnp.arange(steps_n)[:, None]
    f_scores = jnp.where(fresh_live[:, None, None, :], f_scores, NEG_FILL)

    peak = jnp.maximum(got_peak.max(0), f_scores.max(-1))
    rescale = jnp.exp(got_peak - peak[None])
    f_w = jnp.exp(f_scores - peak[..., None])
    mass = (got_mass * rescale).sum(0) + f_w.sum(-1)
    numer = (got_numer * rescale[..., None]).sum(0)
    numer = numer + jnp.einsum(
        "sbhu,ubhd->sbhd", f_w.astype(jnp.bfloat16), f_kv[1], preferred_element_type=jnp.float32
    )
    attended = (numer / mass[..., None]).astype(jnp.bfloat16).reshape(steps_n, rows_dev, width_dev)

    gathered = lax.all_gather(attended, "sub", axis=1, tiled=True)
    return _project(gathered, out_weight, scale_in, scale_out, residual, tp_count, tp_rank,
                    sub_rank)


def _project(gathered, out_weight, scale_in, scale_out, residual, tp_count, tp_rank, sub_rank):
    steps_n, samples, width_dev = gathered.shape
    heads_dev = width_dev // DH
    local_width = out_weight.shape[1]
    head_rows_in = gathered.reshape(steps_n * samples, heads_dev, DH)
    head_weights = out_weight.reshape(heads_dev, DH, local_width)
    scale_a = jnp.repeat(jnp.exp2(-scale_in.astype(jnp.float32)), 128)
    scale_b = jnp.repeat(jnp.exp2(-scale_out.astype(jnp.float32)), 128)
    local_a = lax.dynamic_slice_in_dim(scale_a, sub_rank * local_width, local_width, 0)
    local_b = lax.dynamic_slice_in_dim(scale_b, sub_rank * local_width, local_width, 0)
    per_head_term = jnp.einsum(
        "rhd,hdf->rhf", head_rows_in, head_weights, preferred_element_type=jnp.float32
    )
    clipped = jnp.clip(per_head_term / local_a[None, None, :], -127.0, 127.0).sum(1)

    piece_cols = local_width // tp_count
    pieces = jnp.moveaxis(clipped.reshape(steps_n * samples, tp_count, piece_cols), 1, 0)
    got_pieces = _exchange(pieces, "tp", tp_count)
    summed = got_pieces.sum(0)
    piece_start = sub_rank * local_width + tp_rank * piece_cols
    piece_a = lax.dynamic_slice_in_dim(scale_a, piece_start, piece_cols, 0)
    piece_b = lax.dynamic_slice_in_dim(scale_b, piece_start, piece_cols, 0)
    levels = jnp.clip(summed * piece_a / piece_b, -127.0, 127.0).astype(jnp.bfloat16)
    level_blocks = _gather_blocks(levels, "tp", tp_count)
    all_levels = jnp.moveaxis(level_blocks, 0, 1).reshape(steps_n * samples, local_width)
    restored = all_levels.astype(jnp.float32) * local_b
    hidden = residual.reshape(steps_n * samples, local_width).astype(jnp.float32) + restored
    return hidden.astype(jnp.bfloat16).reshape(steps_n, samples, local_width)


def solution(mesh):
    return jax.shard_map(
        per_device,
        mesh=mesh,
        in_specs=(
            P(None, ("rep", "sub"), "tp"),
            P(None, ("rep", "tp"), None),
            P(None, ("rep", "sub"), "tp", None),
            P(("rep", "sub")),
            P(None, None, ("rep", "sub"), None),
            P("tp", "sub"),
            P(),
            P(),
            P(None, "rep", "sub"),
        ),
        out_specs=P(None, "rep", "sub"),
        check_vma=False,
    )
```

```python
import math

import jax
import jax.numpy as jnp
from jax import lax
from jax.experimental import pallas as pl
from jax.experimental.pallas import tpu as pltpu
from jax.sharding import PartitionSpec as P

DH = 128


NEG_FILL = -1e30


def _is_pow2(n):
    return n >= 1 and (n & (n - 1)) == 0


def _gather_blocks(x, axis_name, count):
    if count == 1:
        return x[None]
    if not _is_pow2(count):
        return lax.all_gather(x, axis_name, axis=0, tiled=False)
    me = lax.axis_index(axis_name)
    if count <= 8:
        half = count // 2
        got = [x]
        for d in range(1, half):
            got.append(lax.ppermute(x, axis_name, [(i, (i + 2 * d) % count) for i in range(count)]))
        order = (me // 2 - jnp.arange(half)) % half
        mine = jnp.zeros((half,) + x.shape, x.dtype).at[order].set(jnp.stack(got))
        other = lax.ppermute(mine, axis_name, [(i, i ^ 1) for i in range(count)])
        low = me % 2 == 0
        pairs = jnp.where(low, jnp.stack([mine, other], 1), jnp.stack([other, mine], 1))
        return pairs.reshape((count,) + x.shape)
    cur = x[None]
    k = 1
    while k < count:
        other = lax.ppermute(cur, axis_name, [(i, i ^ k) for i in range(count)])
        low = (me // k) % 2 == 0
        cur = jnp.where(low, jnp.concatenate([cur, other]), jnp.concatenate([other, cur]))
        k *= 2
    return cur


def _exchange(blocks, axis_name, count, direct_max=8):
    if count == 1:
        return blocks
    if count > direct_max:
        return jax.tree.map(
            lambda b: lax.all_to_all(b, axis_name, split_axis=0, concat_axis=0, tiled=True), blocks
        )
    me = lax.axis_index(axis_name)
    got = [jax.tree.map(lambda b: lax.dynamic_index_in_dim(b, me, 0, keepdims=False), blocks)]
    for k in range(1, count):
        dst = (me + k) % count
        send = jax.tree.map(lambda b: lax.dynamic_index_in_dim(b, dst, 0, keepdims=False), blocks)
        got.append(lax.ppermute(send, axis_name, [(i, (i + k) % count) for i in range(count)]))
    return jax.tree.map(lambda *xs: jnp.stack(xs), *got)


def _attend_kernel(q_ref, k_ref, v_ref, tk_ref, tv_ref, valid_ref, numer_ref, peak_ref, mass_ref):
    heads_n, rows_n = q_ref.shape[0], q_ref.shape[1]
    samples = tk_ref.shape[1]
    per_sample = rows_n // samples
    score_scale = 1.0 / math.sqrt(DH)
    dims_nt = (((1,), (1,)), ((), ()))
    for j in range(heads_n):
        cols = slice(j * DH, (j + 1) * DH)
        q = q_ref[j]
        p_scores = lax.dot_general(q, k_ref[0, :, cols], dims_nt, preferred_element_type=jnp.float32)
        p_scores = p_scores * score_scale
        t_parts = []
        for r in range(samples):
            qr = q[r * per_sample:(r + 1) * per_sample]
            sr = lax.dot_general(
                qr, tk_ref[0, r, :, cols], dims_nt, preferred_element_type=jnp.float32
            )
            sr = sr * score_scale
            t_parts.append(jnp.where(valid_ref[r:r + 1, :] > 0.0, sr, NEG_FILL))
        t_scores = jnp.concatenate(t_parts, axis=0)
        peak = jnp.maximum(
            jnp.max(p_scores, axis=1, keepdims=True), jnp.max(t_scores, axis=1, keepdims=True)
        )
        p_w = jnp.exp(p_scores - peak)
        t_w = jnp.exp(t_scores - peak)
        mass = jnp.sum(p_w, axis=1, keepdims=True) + jnp.sum(t_w, axis=1, keepdims=True)
        numer = jnp.dot(
            p_w.astype(jnp.bfloat16), v_ref[0, :, cols], preferred_element_type=jnp.float32
        )
        t_w16 = t_w.astype(jnp.bfloat16)
        t_numer = [
            jnp.dot(
                t_w16[r * per_sample:(r + 1) * per_sample], tv_ref[0, r, :, cols],
                preferred_element_type=jnp.float32,
            )
            for r in range(samples)
        ]
        numer_ref[j] = numer + jnp.concatenate(t_numer, axis=0)
        peak_ref[j] = jnp.broadcast_to(peak, peak_ref.shape[1:])
        mass_ref[j] = jnp.broadcast_to(mass, mass_ref.shape[1:])


def _attend_local(q_rows, prefix_kv, tail_kv, valid):
    kv_heads, rows_n, _ = q_rows.shape
    prefix_dev = prefix_kv.shape[1]
    samples, tail_dev = tail_kv.shape[1], tail_kv.shape[2]
    flops = 4 * kv_heads * rows_n * DH * (prefix_dev + tail_dev)
    bytes_in = 2 * (prefix_kv.size + tail_kv.size + q_rows.size)
    per_step = 4 if kv_heads % 4 == 0 else 1
    width = per_step * DH
    return pl.pallas_call(
        _attend_kernel,
        grid=(kv_heads // per_step,),
        in_specs=[
            pl.BlockSpec((per_step, rows_n, DH), lambda k: (k, 0, 0)),
            pl.BlockSpec((1, prefix_dev, width), lambda k: (0, 0, k)),
            pl.BlockSpec((1, prefix_dev, width), lambda k: (1, 0, k)),
            pl.BlockSpec((1, samples, tail_dev, width), lambda k: (0, 0, 0, k)),
            pl.BlockSpec((1, samples, tail_dev, width), lambda k: (1, 0, 0, k)),
            pl.BlockSpec((samples, tail_dev), lambda k: (0, 0)),
        ],
        out_specs=[
            pl.BlockSpec((per_step, rows_n, DH), lambda k: (k, 0, 0)),
            pl.BlockSpec((per_step, rows_n, DH), lambda k: (k, 0, 0)),
            pl.BlockSpec((per_step, rows_n, DH), lambda k: (k, 0, 0)),
        ],
        out_shape=[jax.ShapeDtypeStruct((kv_heads, rows_n, DH), jnp.float32)] * 3,
        cost_estimate=pl.CostEstimate(
            flops=flops,
            transcendentals=kv_heads * rows_n * (prefix_dev + tail_dev),
            bytes_accessed=bytes_in + 3 * 4 * kv_heads * rows_n * DH,
        ),
        compiler_params=pltpu.CompilerParams(vmem_limit_bytes=48 * 1024 * 1024),
    )(q_rows, prefix_kv, prefix_kv, tail_kv, tail_kv, valid)


def per_device(
    queries, prefix_kv, tail_kv, tail_lengths, fresh_kv, out_weight, scale_in, scale_out, residual
):
    steps_n, rows_dev, width_dev = queries.shape
    heads_dev = width_dev // DH
    tp_count = lax.axis_size("tp")
    tp_rank = lax.axis_index("tp")
    sub_rank = lax.axis_index("sub")
    kv_heads = prefix_kv.shape[2] // DH
    heads_all = heads_dev * tp_count
    group = heads_all // kv_heads
    prefix_dev = prefix_kv.shape[1]
    tail_dev = tail_kv.shape[2]
    score_scale = 1.0 / math.sqrt(DH)

    q_blocks = _gather_blocks(queries, "tp", tp_count)
    q_all = jnp.moveaxis(q_blocks, 0, 2).reshape(steps_n, rows_dev, kv_heads, group, DH)
    q_rows = jnp.transpose(q_all, (2, 1, 0, 3, 4)).reshape(kv_heads, -1, DH)
    t_pos = tp_rank * tail_dev + jnp.arange(tail_dev)
    valid = (t_pos[None, :] < tail_lengths[:, None]).astype(jnp.float32)
    k_numer, k_peak, k_mass = _attend_local(q_rows, prefix_kv, tail_kv, valid)

    def by_owner(x):
        x = jnp.transpose(x, (2, 1, 0, 3) + tuple(range(4, x.ndim)))
        x = x.reshape((steps_n, rows_dev, tp_count, heads_dev) + x.shape[4:])
        return jnp.moveaxis(x, 2, 0)

    grid4 = (kv_heads, rows_dev, steps_n, group)
    o_numer = by_owner(k_numer.reshape(grid4 + (DH,))).reshape(tp_count, -1, DH)
    o_peak = by_owner(k_peak[..., 0].reshape(grid4)).reshape(tp_count, -1)
    o_mass = by_owner(k_mass[..., 0].reshape(grid4)).reshape(tp_count, -1)
    n_rows = steps_n * rows_dev * heads_dev
    n_stat = -(-2 * n_rows // DH)
    stats = jnp.concatenate([o_peak, o_mass], axis=1)
    stats = jnp.pad(stats, ((0, 0), (0, n_stat * DH - 2 * n_rows))).reshape(tp_count, n_stat, DH)
    got = _exchange(jnp.concatenate([o_numer, stats], axis=1), "tp", tp_count)
    got_numer = got[:, :n_rows].reshape(tp_count, steps_n, rows_dev, heads_dev, DH)
    got_stats = got[:, n_rows:].reshape(tp_count, -1)[:, : 2 * n_rows]
    got_stats = got_stats.reshape(tp_count, 2, steps_n, rows_dev, heads_dev)
    got_peak = got_stats[:, 0]
    got_mass = got_stats[:, 1]

    own_query = queries.reshape(steps_n, rows_dev, heads_dev, DH)
    f_kv = fresh_kv.reshape(2, steps_n, rows_dev, kv_heads, DH)
    if group % heads_dev == 0:
        one_kv = lax.dynamic_index_in_dim(f_kv, tp_rank * heads_dev // group, 3, keepdims=True)
        f_kv = jnp.broadcast_to(one_kv, (2, steps_n, rows_dev, heads_dev, DH))
    else:
        kv_of_head = (tp_rank * heads_dev + jnp.arange(heads_dev)) // group
        f_kv = jnp.take(f_kv, kv_of_head, axis=3)
    f_scores = (
        jnp.einsum("sbhd,ubhd->sbhu", own_query, f_kv[0], preferred_element_type=jnp.float32)
        * score_scale
    )
    fresh_live = jnp.arange(steps_n)[None, :] <= jnp.arange(steps_n)[:, None]
    f_scores = jnp.where(fresh_live[:, None, None, :], f_scores, NEG_FILL)

    peak = jnp.maximum(got_peak.max(0), f_scores.max(-1))
    rescale = jnp.exp(got_peak - peak[None])
    f_w = jnp.exp(f_scores - peak[..., None])
    mass = (got_mass * rescale).sum(0) + f_w.sum(-1)
    numer = (got_numer * rescale[..., None]).sum(0)
    numer = numer + jnp.einsum(
        "sbhu,ubhd->sbhd", f_w.astype(jnp.bfloat16), f_kv[1], preferred_element_type=jnp.float32
    )
    attended = (numer / mass[..., None]).astype(jnp.bfloat16).reshape(steps_n, rows_dev, width_dev)

    gathered = lax.all_gather(attended, "sub", axis=1, tiled=True)
    samples = gathered.shape[1]
    local_width = out_weight.shape[1]
    head_rows_in = gathered.reshape(steps_n * samples, heads_dev, DH)
    head_weights = out_weight.reshape(heads_dev, DH, local_width)
    scale_a = jnp.repeat(jnp.exp2(-scale_in.astype(jnp.float32)), 128)
    scale_b = jnp.repeat(jnp.exp2(-scale_out.astype(jnp.float32)), 128)
    local_a = lax.dynamic_slice_in_dim(scale_a, sub_rank * local_width, local_width, 0)
    local_b = lax.dynamic_slice_in_dim(scale_b, sub_rank * local_width, local_width, 0)
    per_head_term = jnp.einsum(
        "rhd,hdf->rhf", head_rows_in, head_weights, preferred_element_type=jnp.float32
    )
    clipped = jnp.clip(per_head_term / local_a[None, None, :], -127.0, 127.0).sum(1)

    piece_cols = local_width // tp_count
    pieces = jnp.moveaxis(clipped.reshape(steps_n * samples, tp_count, piece_cols), 1, 0)
    got_pieces = _exchange(pieces, "tp", tp_count)
    summed = got_pieces.sum(0)
    piece_start = sub_rank * local_width + tp_rank * piece_cols
    piece_a = lax.dynamic_slice_in_dim(scale_a, piece_start, piece_cols, 0)
    piece_b = lax.dynamic_slice_in_dim(scale_b, piece_start, piece_cols, 0)
    levels = jnp.clip(summed * piece_a / piece_b, -127.0, 127.0).astype(jnp.bfloat16)
    level_blocks = _gather_blocks(levels, "tp", tp_count)
    all_levels = jnp.moveaxis(level_blocks, 0, 1).reshape(steps_n * samples, local_width)
    restored = all_levels.astype(jnp.float32) * local_b
    hidden = residual.reshape(steps_n * samples, local_width).astype(jnp.float32) + restored
    return hidden.astype(jnp.bfloat16).reshape(steps_n, samples, local_width)


def solution(mesh):
    return jax.shard_map(
        per_device,
        mesh=mesh,
        in_specs=(
            P(None, ("rep", "sub"), "tp"),
            P(None, ("rep", "tp"), None),
            P(None, ("rep", "sub"), "tp", None),
            P(("rep", "sub")),
            P(None, None, ("rep", "sub"), None),
            P("tp", "sub"),
            P(),
            P(),
            P(None, "rep", "sub"),
        ),
        out_specs=P(None, "rep", "sub"),
        check_vma=False,
    )
```

```python
import math

import jax
import jax.numpy as jnp
from jax import lax
from jax.experimental import pallas as pl
from jax.experimental.pallas import tpu as pltpu
from jax.sharding import PartitionSpec as P

DH = 128


NEG_FILL = -1e30


def _is_pow2(n):
    return n >= 1 and (n & (n - 1)) == 0


def _gather_blocks(x, axis_name, count):
    if count == 1:
        return x[None]
    if not _is_pow2(count):
        return lax.all_gather(x, axis_name, axis=0, tiled=False)
    me = lax.axis_index(axis_name)
    if count <= 8:
        other = lax.ppermute(x, axis_name, [(i, i ^ 1) for i in range(count)])
        low = me % 2 == 0
        pair = jnp.where(low, jnp.stack([x, other]), jnp.stack([other, x]))
        pairs = [pair]
        for d in range(1, count // 2):
            pairs.append(
                lax.ppermute(pair, axis_name, [(i, (i + 2 * d) % count) for i in range(count)])
            )
        order = (me // 2 - jnp.arange(count // 2)) % (count // 2)
        placed = jnp.zeros((count // 2,) + pair.shape, pair.dtype).at[order].set(jnp.stack(pairs))
        return placed.reshape((count,) + x.shape)
    cur = x[None]
    k = 1
    while k < count:
        other = lax.ppermute(cur, axis_name, [(i, i ^ k) for i in range(count)])
        low = (me // k) % 2 == 0
        cur = jnp.where(low, jnp.concatenate([cur, other]), jnp.concatenate([other, cur]))
        k *= 2
    return cur


def _exchange(blocks, axis_name, count, direct_max=8):
    if count == 1:
        return blocks
    if count > direct_max:
        return jax.tree.map(
            lambda b: lax.all_to_all(b, axis_name, split_axis=0, concat_axis=0, tiled=True), blocks
        )
    me = lax.axis_index(axis_name)
    got = [jax.tree.map(lambda b: lax.dynamic_index_in_dim(b, me, 0, keepdims=False), blocks)]
    for k in range(1, count):
        if _is_pow2(count):
            dst = me ^ k
            perm = [(i, i ^ k) for i in range(count)]
        else:
            dst = (me + k) % count
            perm = [(i, (i + k) % count) for i in range(count)]
        send = jax.tree.map(lambda b: lax.dynamic_index_in_dim(b, dst, 0, keepdims=False), blocks)
        got.append(lax.ppermute(send, axis_name, perm))
    return jax.tree.map(lambda *xs: jnp.stack(xs), *got)


def _attend_kernel(q_ref, k_ref, v_ref, tk_ref, tv_ref, valid_ref, numer_ref, peak_ref, mass_ref):
    heads_n, rows_n = q_ref.shape[0], q_ref.shape[1]
    samples = tk_ref.shape[1]
    per_sample = rows_n // samples
    score_scale = 1.0 / math.sqrt(DH)
    dims_nt = (((1,), (1,)), ((), ()))
    for j in range(heads_n):
        cols = slice(j * DH, (j + 1) * DH)
        q = q_ref[j]
        p_scores = lax.dot_general(q, k_ref[0, :, cols], dims_nt, preferred_element_type=jnp.float32)
        p_scores = p_scores * score_scale
        t_parts = []
        for r in range(samples):
            qr = q[r * per_sample:(r + 1) * per_sample]
            sr = lax.dot_general(
                qr, tk_ref[0, r, :, cols], dims_nt, preferred_element_type=jnp.float32
            )
            sr = sr * score_scale
            t_parts.append(jnp.where(valid_ref[r:r + 1, :] > 0.0, sr, NEG_FILL))
        t_scores = jnp.concatenate(t_parts, axis=0)
        peak = jnp.maximum(
            jnp.max(p_scores, axis=1, keepdims=True), jnp.max(t_scores, axis=1, keepdims=True)
        )
        p_w = jnp.exp(p_scores - peak)
        t_w = jnp.exp(t_scores - peak)
        mass = jnp.sum(p_w, axis=1, keepdims=True) + jnp.sum(t_w, axis=1, keepdims=True)
        numer = jnp.dot(
            p_w.astype(jnp.bfloat16), v_ref[0, :, cols], preferred_element_type=jnp.float32
        )
        t_w16 = t_w.astype(jnp.bfloat16)
        t_numer = [
            jnp.dot(
                t_w16[r * per_sample:(r + 1) * per_sample], tv_ref[0, r, :, cols],
                preferred_element_type=jnp.float32,
            )
            for r in range(samples)
        ]
        numer_ref[j] = numer + jnp.concatenate(t_numer, axis=0)
        peak_ref[j] = jnp.broadcast_to(peak, peak_ref.shape[1:])
        mass_ref[j] = jnp.broadcast_to(mass, mass_ref.shape[1:])


def _attend_local(q_rows, prefix_kv, tail_kv, valid):
    kv_heads, rows_n, _ = q_rows.shape
    prefix_dev = prefix_kv.shape[1]
    samples, tail_dev = tail_kv.shape[1], tail_kv.shape[2]
    flops = 4 * kv_heads * rows_n * DH * (prefix_dev + tail_dev)
    bytes_in = 2 * (prefix_kv.size + tail_kv.size + q_rows.size)
    per_step = 4 if kv_heads % 4 == 0 else 1
    width = per_step * DH
    return pl.pallas_call(
        _attend_kernel,
        grid=(kv_heads // per_step,),
        in_specs=[
            pl.BlockSpec((per_step, rows_n, DH), lambda k: (k, 0, 0)),
            pl.BlockSpec((1, prefix_dev, width), lambda k: (0, 0, k)),
            pl.BlockSpec((1, prefix_dev, width), lambda k: (1, 0, k)),
            pl.BlockSpec((1, samples, tail_dev, width), lambda k: (0, 0, 0, k)),
            pl.BlockSpec((1, samples, tail_dev, width), lambda k: (1, 0, 0, k)),
            pl.BlockSpec((samples, tail_dev), lambda k: (0, 0)),
        ],
        out_specs=[
            pl.BlockSpec((per_step, rows_n, DH), lambda k: (k, 0, 0)),
            pl.BlockSpec((per_step, rows_n, DH), lambda k: (k, 0, 0)),
            pl.BlockSpec((per_step, rows_n, DH), lambda k: (k, 0, 0)),
        ],
        out_shape=[jax.ShapeDtypeStruct((kv_heads, rows_n, DH), jnp.float32)] * 3,
        cost_estimate=pl.CostEstimate(
            flops=flops,
            transcendentals=kv_heads * rows_n * (prefix_dev + tail_dev),
            bytes_accessed=bytes_in + 3 * 4 * kv_heads * rows_n * DH,
        ),
        compiler_params=pltpu.CompilerParams(vmem_limit_bytes=48 * 1024 * 1024),
    )(q_rows, prefix_kv, prefix_kv, tail_kv, tail_kv, valid)


def per_device(
    queries, prefix_kv, tail_kv, tail_lengths, fresh_kv, out_weight, scale_in, scale_out, residual
):
    steps_n, rows_dev, width_dev = queries.shape
    heads_dev = width_dev // DH
    tp_count = lax.axis_size("tp")
    tp_rank = lax.axis_index("tp")
    sub_rank = lax.axis_index("sub")
    kv_heads = prefix_kv.shape[2] // DH
    heads_all = heads_dev * tp_count
    group = heads_all // kv_heads
    prefix_dev = prefix_kv.shape[1]
    tail_dev = tail_kv.shape[2]
    score_scale = 1.0 / math.sqrt(DH)

    q_blocks = _gather_blocks(queries, "tp", tp_count)
    q_all = jnp.moveaxis(q_blocks, 0, 2).reshape(steps_n, rows_dev, kv_heads, group, DH)
    q_rows = jnp.transpose(q_all, (2, 1, 0, 3, 4)).reshape(kv_heads, -1, DH)
    t_pos = tp_rank * tail_dev + jnp.arange(tail_dev)
    valid = (t_pos[None, :] < tail_lengths[:, None]).astype(jnp.float32)
    k_numer, k_peak, k_mass = _attend_local(q_rows, prefix_kv, tail_kv, valid)

    def by_owner(x):
        x = jnp.transpose(x, (2, 1, 0, 3) + tuple(range(4, x.ndim)))
        x = x.reshape((steps_n, rows_dev, tp_count, heads_dev) + x.shape[4:])
        return jnp.moveaxis(x, 2, 0)

    grid4 = (kv_heads, rows_dev, steps_n, group)
    o_numer = by_owner(k_numer.reshape(grid4 + (DH,))).reshape(tp_count, -1, DH)
    o_peak = by_owner(k_peak[..., 0].reshape(grid4)).reshape(tp_count, -1)
    o_mass = by_owner(k_mass[..., 0].reshape(grid4)).reshape(tp_count, -1)
    n_rows = steps_n * rows_dev * heads_dev
    n_stat = -(-2 * n_rows // DH)
    stats = jnp.concatenate([o_peak, o_mass], axis=1)
    stats = jnp.pad(stats, ((0, 0), (0, n_stat * DH - 2 * n_rows))).reshape(tp_count, n_stat, DH)
    got = _exchange(jnp.concatenate([o_numer, stats], axis=1), "tp", tp_count)
    got_numer = got[:, :n_rows].reshape(tp_count, steps_n, rows_dev, heads_dev, DH)
    got_stats = got[:, n_rows:].reshape(tp_count, -1)[:, : 2 * n_rows]
    got_stats = got_stats.reshape(tp_count, 2, steps_n, rows_dev, heads_dev)
    got_peak = got_stats[:, 0]
    got_mass = got_stats[:, 1]

    own_query = queries.reshape(steps_n, rows_dev, heads_dev, DH)
    f_kv = fresh_kv.reshape(2, steps_n, rows_dev, kv_heads, DH)
    if group % heads_dev == 0:
        one_kv = lax.dynamic_index_in_dim(f_kv, tp_rank * heads_dev // group, 3, keepdims=True)
        f_kv = jnp.broadcast_to(one_kv, (2, steps_n, rows_dev, heads_dev, DH))
    else:
        kv_of_head = (tp_rank * heads_dev + jnp.arange(heads_dev)) // group
        f_kv = jnp.take(f_kv, kv_of_head, axis=3)
    f_scores = (
        jnp.einsum("sbhd,ubhd->sbhu", own_query, f_kv[0], preferred_element_type=jnp.float32)
        * score_scale
    )
    fresh_live = jnp.arange(steps_n)[None, :] <= jnp.arange(steps_n)[:, None]
    f_scores = jnp.where(fresh_live[:, None, None, :], f_scores, NEG_FILL)

    peak = jnp.maximum(got_peak.max(0), f_scores.max(-1))
    rescale = jnp.exp(got_peak - peak[None])
    f_w = jnp.exp(f_scores - peak[..., None])
    mass = (got_mass * rescale).sum(0) + f_w.sum(-1)
    numer = (got_numer * rescale[..., None]).sum(0)
    numer = numer + jnp.einsum(
        "sbhu,ubhd->sbhd", f_w.astype(jnp.bfloat16), f_kv[1], preferred_element_type=jnp.float32
    )
    attended = (numer / mass[..., None]).astype(jnp.bfloat16).reshape(steps_n, rows_dev, width_dev)

    gathered = lax.all_gather(attended, "sub", axis=1, tiled=True)
    samples = gathered.shape[1]
    local_width = out_weight.shape[1]
    head_rows_in = gathered.reshape(steps_n * samples, heads_dev, DH)
    head_weights = out_weight.reshape(heads_dev, DH, local_width)
    scale_a = jnp.repeat(jnp.exp2(-scale_in.astype(jnp.float32)), 128)
    scale_b = jnp.repeat(jnp.exp2(-scale_out.astype(jnp.float32)), 128)
    local_a = lax.dynamic_slice_in_dim(scale_a, sub_rank * local_width, local_width, 0)
    local_b = lax.dynamic_slice_in_dim(scale_b, sub_rank * local_width, local_width, 0)
    per_head_term = jnp.einsum(
        "rhd,hdf->rhf", head_rows_in, head_weights, preferred_element_type=jnp.float32
    )
    clipped = jnp.clip(per_head_term / local_a[None, None, :], -127.0, 127.0).sum(1)

    piece_cols = local_width // tp_count
    pieces = jnp.moveaxis(clipped.reshape(steps_n * samples, tp_count, piece_cols), 1, 0)
    got_pieces = _exchange(pieces, "tp", tp_count)
    summed = got_pieces.sum(0)
    piece_start = sub_rank * local_width + tp_rank * piece_cols
    piece_a = lax.dynamic_slice_in_dim(scale_a, piece_start, piece_cols, 0)
    piece_b = lax.dynamic_slice_in_dim(scale_b, piece_start, piece_cols, 0)
    levels = jnp.clip(summed * piece_a / piece_b, -127.0, 127.0).astype(jnp.bfloat16)
    level_blocks = _gather_blocks(levels, "tp", tp_count)
    all_levels = jnp.moveaxis(level_blocks, 0, 1).reshape(steps_n * samples, local_width)
    restored = all_levels.astype(jnp.float32) * local_b
    hidden = residual.reshape(steps_n * samples, local_width).astype(jnp.float32) + restored
    return hidden.astype(jnp.bfloat16).reshape(steps_n, samples, local_width)


def solution(mesh):
    return jax.shard_map(
        per_device,
        mesh=mesh,
        in_specs=(
            P(None, ("rep", "sub"), "tp"),
            P(None, ("rep", "tp"), None),
            P(None, ("rep", "sub"), "tp", None),
            P(("rep", "sub")),
            P(None, None, ("rep", "sub"), None),
            P("tp", "sub"),
            P(),
            P(),
            P(None, "rep", "sub"),
        ),
        out_specs=P(None, "rep", "sub"),
        check_vma=False,
    )
```

```python
import functools
import math

import jax
import jax.numpy as jnp
from jax import lax
from jax.experimental import pallas as pl
from jax.experimental.pallas import tpu as pltpu
from jax.sharding import PartitionSpec as P

DH = 128


NEG_FILL = -1e30


def _is_pow2(n):
    return n >= 1 and (n & (n - 1)) == 0


def _gather_blocks(x, axis_name, count):
    if count == 1:
        return x[None]
    if not _is_pow2(count):
        return lax.all_gather(x, axis_name, axis=0, tiled=False)
    me = lax.axis_index(axis_name)
    if count <= 8:
        other = lax.ppermute(x, axis_name, [(i, i ^ 1) for i in range(count)])
        low = me % 2 == 0
        pair = jnp.where(low, jnp.stack([x, other]), jnp.stack([other, x]))
        pairs = [pair]
        for d in range(1, count // 2):
            pairs.append(
                lax.ppermute(pair, axis_name, [(i, (i + 2 * d) % count) for i in range(count)])
            )
        order = (me // 2 - jnp.arange(count // 2)) % (count // 2)
        placed = jnp.zeros((count // 2,) + pair.shape, pair.dtype).at[order].set(jnp.stack(pairs))
        return placed.reshape((count,) + x.shape)
    cur = x[None]
    k = 1
    while k < count:
        other = lax.ppermute(cur, axis_name, [(i, i ^ k) for i in range(count)])
        low = (me // k) % 2 == 0
        cur = jnp.where(low, jnp.concatenate([cur, other]), jnp.concatenate([other, cur]))
        k *= 2
    return cur


def _exchange(blocks, axis_name, count, direct_max=8):
    if count == 1:
        return blocks
    if count > direct_max:
        return jax.tree.map(
            lambda b: lax.all_to_all(b, axis_name, split_axis=0, concat_axis=0, tiled=True), blocks
        )
    me = lax.axis_index(axis_name)
    got = [jax.tree.map(lambda b: lax.dynamic_index_in_dim(b, me, 0, keepdims=False), blocks)]
    for k in range(1, count):
        dst = (me + k) % count
        send = jax.tree.map(lambda b: lax.dynamic_index_in_dim(b, dst, 0, keepdims=False), blocks)
        got.append(lax.ppermute(send, axis_name, [(i, (i + k) % count) for i in range(count)]))
    return jax.tree.map(lambda *xs: jnp.stack(xs), *got)


def _attend_kernel(q_ref, k_ref, v_ref, tk_ref, tv_ref, valid_ref, numer_ref, peak_ref, mass_ref):
    heads_n, rows_n = q_ref.shape[0], q_ref.shape[1]
    samples = tk_ref.shape[1]
    per_sample = rows_n // samples
    score_scale = 1.0 / math.sqrt(DH)
    dims_nt = (((1,), (1,)), ((), ()))
    for j in range(heads_n):
        cols = slice(j * DH, (j + 1) * DH)
        q = q_ref[j]
        p_scores = lax.dot_general(q, k_ref[0, :, cols], dims_nt, preferred_element_type=jnp.float32)
        p_scores = p_scores * score_scale
        t_parts = []
        for r in range(samples):
            qr = q[r * per_sample:(r + 1) * per_sample]
            sr = lax.dot_general(
                qr, tk_ref[0, r, :, cols], dims_nt, preferred_element_type=jnp.float32
            )
            sr = sr * score_scale
            t_parts.append(jnp.where(valid_ref[r:r + 1, :] > 0.0, sr, NEG_FILL))
        t_scores = jnp.concatenate(t_parts, axis=0)
        peak = jnp.maximum(
            jnp.max(p_scores, axis=1, keepdims=True), jnp.max(t_scores, axis=1, keepdims=True)
        )
        p_w = jnp.exp(p_scores - peak)
        t_w = jnp.exp(t_scores - peak)
        mass = jnp.sum(p_w, axis=1, keepdims=True) + jnp.sum(t_w, axis=1, keepdims=True)
        numer = jnp.dot(
            p_w.astype(jnp.bfloat16), v_ref[0, :, cols], preferred_element_type=jnp.float32
        )
        t_w16 = t_w.astype(jnp.bfloat16)
        t_numer = [
            jnp.dot(
                t_w16[r * per_sample:(r + 1) * per_sample], tv_ref[0, r, :, cols],
                preferred_element_type=jnp.float32,
            )
            for r in range(samples)
        ]
        numer_ref[j] = numer + jnp.concatenate(t_numer, axis=0)
        peak_ref[j] = jnp.broadcast_to(peak, peak_ref.shape[1:])
        mass_ref[j] = jnp.broadcast_to(mass, mass_ref.shape[1:])


def _attend_local(q_rows, prefix_kv, tail_kv, valid):
    kv_heads, rows_n, _ = q_rows.shape
    prefix_dev = prefix_kv.shape[1]
    samples, tail_dev = tail_kv.shape[1], tail_kv.shape[2]
    flops = 4 * kv_heads * rows_n * DH * (prefix_dev + tail_dev)
    bytes_in = 2 * (prefix_kv.size + tail_kv.size + q_rows.size)
    per_step = 4 if kv_heads % 4 == 0 else 1
    width = per_step * DH
    return pl.pallas_call(
        _attend_kernel,
        grid=(kv_heads // per_step,),
        in_specs=[
            pl.BlockSpec((per_step, rows_n, DH), lambda k: (k, 0, 0)),
            pl.BlockSpec((1, prefix_dev, width), lambda k: (0, 0, k)),
            pl.BlockSpec((1, prefix_dev, width), lambda k: (1, 0, k)),
            pl.BlockSpec((1, samples, tail_dev, width), lambda k: (0, 0, 0, k)),
            pl.BlockSpec((1, samples, tail_dev, width), lambda k: (1, 0, 0, k)),
            pl.BlockSpec((samples, tail_dev), lambda k: (0, 0)),
        ],
        out_specs=[
            pl.BlockSpec((per_step, rows_n, DH), lambda k: (k, 0, 0)),
            pl.BlockSpec((per_step, rows_n, DH), lambda k: (k, 0, 0)),
            pl.BlockSpec((per_step, rows_n, DH), lambda k: (k, 0, 0)),
        ],
        out_shape=[jax.ShapeDtypeStruct((kv_heads, rows_n, DH), jnp.float32)] * 3,
        cost_estimate=pl.CostEstimate(
            flops=flops,
            transcendentals=kv_heads * rows_n * (prefix_dev + tail_dev),
            bytes_accessed=bytes_in + 3 * 4 * kv_heads * rows_n * DH,
        ),
        compiler_params=pltpu.CompilerParams(vmem_limit_bytes=48 * 1024 * 1024),
    )(q_rows, prefix_kv, prefix_kv, tail_kv, tail_kv, valid)


def _attend_packed_kernel(
    group, q_ref, k_ref, v_ref, tk_ref, tv_ref, valid_ref, out_ref
):
    heads_n, rows_n = q_ref.shape[0], q_ref.shape[1]
    samples, tail_dev = tk_ref.shape[1], tk_ref.shape[2]
    score_scale = 1.0 / math.sqrt(DH)
    dims_nt = (((1,), (1,)), ((), ()))
    row_sample = (lax.broadcasted_iota(jnp.int32, (rows_n, tail_dev), 0) // group) % samples
    for j in range(heads_n):
        cols = slice(j * DH, (j + 1) * DH)
        q = q_ref[j]
        p_scores = lax.dot_general(q, k_ref[0, :, cols], dims_nt, preferred_element_type=jnp.float32)
        p_scores = p_scores * score_scale
        t_scores = jnp.full((rows_n, tail_dev), NEG_FILL, jnp.float32)
        for r in range(samples):
            sr = lax.dot_general(
                q, tk_ref[0, r, :, cols], dims_nt, preferred_element_type=jnp.float32
            )
            live = (row_sample == r) & (valid_ref[r:r + 1, :] > 0.0)
            t_scores = jnp.where(live, sr * score_scale, t_scores)
        peak = jnp.maximum(
            jnp.max(p_scores, axis=1, keepdims=True), jnp.max(t_scores, axis=1, keepdims=True)
        )
        p_w = jnp.exp(p_scores - peak)
        t_w = jnp.exp(t_scores - peak)
        mass = jnp.sum(p_w, axis=1, keepdims=True) + jnp.sum(t_w, axis=1, keepdims=True)
        numer = jnp.dot(
            p_w.astype(jnp.bfloat16), v_ref[0, :, cols], preferred_element_type=jnp.float32
        )
        for r in range(samples):
            t_w16 = jnp.where(row_sample == r, t_w, 0.0).astype(jnp.bfloat16)
            numer = numer + jnp.dot(t_w16, tv_ref[0, r, :, cols], preferred_element_type=jnp.float32)
        out_ref[j, :rows_n, :] = numer
        peak_row = jnp.transpose(jnp.broadcast_to(peak, (rows_n, DH)))[0:1]
        mass_row = jnp.transpose(jnp.broadcast_to(mass, (rows_n, DH)))[0:1]
        out_ref[j, rows_n:, :] = jnp.concatenate(
            [peak_row, mass_row, jnp.zeros((6, DH), jnp.float32)], axis=0
        )


def _attend_packed(q_rows, prefix_kv, tail_kv, valid, group):
    kv_heads, rows_n, _ = q_rows.shape
    prefix_dev = prefix_kv.shape[1]
    samples, tail_dev = tail_kv.shape[1], tail_kv.shape[2]
    flops = 4 * kv_heads * rows_n * DH * (prefix_dev + samples * tail_dev)
    bytes_in = 2 * (prefix_kv.size + tail_kv.size + q_rows.size)
    per_step = 4 if kv_heads % 4 == 0 else 1
    width = per_step * DH
    return pl.pallas_call(
        functools.partial(_attend_packed_kernel, group),
        grid=(kv_heads // per_step,),
        in_specs=[
            pl.BlockSpec((per_step, rows_n, DH), lambda k: (k, 0, 0)),
            pl.BlockSpec((1, prefix_dev, width), lambda k: (0, 0, k)),
            pl.BlockSpec((1, prefix_dev, width), lambda k: (1, 0, k)),
            pl.BlockSpec((1, samples, tail_dev, width), lambda k: (0, 0, 0, k)),
            pl.BlockSpec((1, samples, tail_dev, width), lambda k: (1, 0, 0, k)),
            pl.BlockSpec((samples, tail_dev), lambda k: (0, 0)),
        ],
        out_specs=pl.BlockSpec((per_step, rows_n + 8, DH), lambda k: (k, 0, 0)),
        out_shape=jax.ShapeDtypeStruct((kv_heads, rows_n + 8, DH), jnp.float32),
        cost_estimate=pl.CostEstimate(
            flops=flops,
            transcendentals=kv_heads * rows_n * (prefix_dev + tail_dev),
            bytes_accessed=bytes_in + 4 * kv_heads * (rows_n + 8) * DH,
        ),
        compiler_params=pltpu.CompilerParams(vmem_limit_bytes=48 * 1024 * 1024),
    )(q_rows, prefix_kv, prefix_kv, tail_kv, tail_kv, valid)


def _attend_packed_pairs(blk, q_rows, prefix_kv, tail_kv, valid, group):
    heads_n, rows_n, _ = q_rows.shape
    prefix_dev = prefix_kv.shape[1]
    samples, tail_dev = tail_kv.shape[1], tail_kv.shape[2]
    flops = 4 * heads_n * rows_n * DH * (prefix_dev + samples * tail_dev)
    width = 2 * DH
    grid_spec = pltpu.PrefetchScalarGridSpec(
        num_scalar_prefetch=1,
        grid=(heads_n // 2,),
        in_specs=[
            pl.BlockSpec((2, rows_n, DH), lambda g, b: (g, 0, 0)),
            pl.BlockSpec((1, prefix_dev, width), lambda g, b: (0, 0, b[g])),
            pl.BlockSpec((1, prefix_dev, width), lambda g, b: (1, 0, b[g])),
            pl.BlockSpec((1, samples, tail_dev, width), lambda g, b: (0, 0, 0, b[g])),
            pl.BlockSpec((1, samples, tail_dev, width), lambda g, b: (1, 0, 0, b[g])),
            pl.BlockSpec((samples, tail_dev), lambda g, b: (0, 0)),
        ],
        out_specs=pl.BlockSpec((2, rows_n + 8, DH), lambda g, b: (g, 0, 0)),
    )
    return pl.pallas_call(
        lambda b_ref, *refs: _attend_packed_kernel(group, *refs),
        grid_spec=grid_spec,
        out_shape=jax.ShapeDtypeStruct((heads_n, rows_n + 8, DH), jnp.float32),
        cost_estimate=pl.CostEstimate(
            flops=flops,
            transcendentals=heads_n * rows_n * (prefix_dev + tail_dev),
            bytes_accessed=2 * (2 * prefix_dev + 2 * samples * tail_dev) * heads_n * DH
            + 2 * q_rows.size + 4 * heads_n * (rows_n + 8) * DH,
        ),
        compiler_params=pltpu.CompilerParams(vmem_limit_bytes=48 * 1024 * 1024),
    )(blk.astype(jnp.int32), q_rows, prefix_kv, prefix_kv, tail_kv, tail_kv, valid)


def per_device(
    queries, prefix_kv, tail_kv, tail_lengths, fresh_kv, out_weight, scale_in, scale_out, residual
):
    steps_n, rows_dev, width_dev = queries.shape
    heads_dev = width_dev // DH
    tp_count = lax.axis_size("tp")
    tp_rank = lax.axis_index("tp")
    sub_rank = lax.axis_index("sub")
    kv_heads = prefix_kv.shape[2] // DH
    heads_all = heads_dev * tp_count
    group = heads_all // kv_heads
    prefix_dev = prefix_kv.shape[1]
    tail_dev = tail_kv.shape[2]
    score_scale = 1.0 / math.sqrt(DH)

    n_rows = steps_n * rows_dev * heads_dev
    pairs_ok = (tp_count == kv_heads and heads_dev == group and n_rows == DH
                and tp_count in (4, 8))
    if pairs_ok:
        t_pos = tp_rank * tail_dev + jnp.arange(tail_dev)
        valid = (t_pos[None, :] < tail_lengths[:, None]).astype(jnp.float32)
        half = tp_count // 2
        mine = tp_rank // 2
        other = lax.ppermute(queries, "tp", [(i, i ^ 1) for i in range(tp_count)])
        pair = jnp.where(tp_rank % 2 == 0, jnp.stack([queries, other]), jnp.stack([other, queries]))
        far = [
            lax.ppermute(pair, "tp", [(i, (i + 2 * d) % tp_count) for i in range(tp_count)])
            for d in range(1, half)
        ]
        out_near = _attend_packed_pairs(
            jnp.reshape(mine, (1,)), pair.reshape(2, -1, DH), prefix_kv, tail_kv, valid, group
        )
        far_blk = (mine - jnp.arange(1, half)) % half
        out_far = _attend_packed_pairs(
            far_blk, jnp.stack(far).reshape(2 * (half - 1), -1, DH), prefix_kv, tail_kv, valid,
            group,
        )
        outs = jnp.concatenate([out_near, out_far])

        def position(head):
            d = (mine - head // 2) % half
            return jnp.where(d == 0, head % 2, 2 * d + head % 2)

        got = [lax.dynamic_index_in_dim(outs, position(tp_rank), 0, keepdims=False)]
        for k in range(1, tp_count):
            send = lax.dynamic_index_in_dim(outs, position((tp_rank + k) % tp_count), 0, keepdims=False)
            got.append(lax.ppermute(send, "tp", [(i, (i + k) % tp_count) for i in range(tp_count)]))
        got = jnp.stack(got)
        got_numer = got[:, :n_rows].reshape(tp_count, steps_n, rows_dev, heads_dev, DH)
        got_peak = got[:, n_rows].reshape(tp_count, steps_n, rows_dev, heads_dev)
        got_mass = got[:, n_rows + 1].reshape(tp_count, steps_n, rows_dev, heads_dev)
        q_blocks = None
    else:
        q_blocks = _gather_blocks(queries, "tp", tp_count)
    if not pairs_ok:
        q_all = jnp.moveaxis(q_blocks, 0, 2).reshape(steps_n, rows_dev, kv_heads, group, DH)
        t_pos = tp_rank * tail_dev + jnp.arange(tail_dev)
        valid = (t_pos[None, :] < tail_lengths[:, None]).astype(jnp.float32)
        n_rows = steps_n * rows_dev * heads_dev
        if tp_count == kv_heads and heads_dev == group and n_rows == DH:
            q_rows = jnp.transpose(q_all, (2, 0, 1, 3, 4)).reshape(kv_heads, -1, DH)
            got = _exchange(_attend_packed(q_rows, prefix_kv, tail_kv, valid, group), "tp", tp_count)
            got_numer = got[:, :n_rows].reshape(tp_count, steps_n, rows_dev, heads_dev, DH)
            got_peak = got[:, n_rows].reshape(tp_count, steps_n, rows_dev, heads_dev)
            got_mass = got[:, n_rows + 1].reshape(tp_count, steps_n, rows_dev, heads_dev)
        else:

            q_rows = jnp.transpose(q_all, (2, 1, 0, 3, 4)).reshape(kv_heads, -1, DH)
            t_pos = tp_rank * tail_dev + jnp.arange(tail_dev)
            valid = (t_pos[None, :] < tail_lengths[:, None]).astype(jnp.float32)
            k_numer, k_peak, k_mass = _attend_local(q_rows, prefix_kv, tail_kv, valid)

            def by_owner(x):
                x = jnp.transpose(x, (2, 1, 0, 3) + tuple(range(4, x.ndim)))
                x = x.reshape((steps_n, rows_dev, tp_count, heads_dev) + x.shape[4:])
                return jnp.moveaxis(x, 2, 0)

            grid4 = (kv_heads, rows_dev, steps_n, group)
            o_numer = by_owner(k_numer.reshape(grid4 + (DH,))).reshape(tp_count, -1, DH)
            o_peak = by_owner(k_peak[..., 0].reshape(grid4)).reshape(tp_count, -1)
            o_mass = by_owner(k_mass[..., 0].reshape(grid4)).reshape(tp_count, -1)
            n_rows = steps_n * rows_dev * heads_dev
            n_stat = -(-2 * n_rows // DH)
            stats = jnp.concatenate([o_peak, o_mass], axis=1)
            stats = jnp.pad(stats, ((0, 0), (0, n_stat * DH - 2 * n_rows))).reshape(tp_count, n_stat, DH)
            got = _exchange(jnp.concatenate([o_numer, stats], axis=1), "tp", tp_count)
            got_numer = got[:, :n_rows].reshape(tp_count, steps_n, rows_dev, heads_dev, DH)
            got_stats = got[:, n_rows:].reshape(tp_count, -1)[:, : 2 * n_rows]
            got_stats = got_stats.reshape(tp_count, 2, steps_n, rows_dev, heads_dev)
            got_peak = got_stats[:, 0]
            got_mass = got_stats[:, 1]

    own_query = queries.reshape(steps_n, rows_dev, heads_dev, DH)
    f_kv = fresh_kv.reshape(2, steps_n, rows_dev, kv_heads, DH)
    if group % heads_dev == 0:
        one_kv = lax.dynamic_index_in_dim(f_kv, tp_rank * heads_dev // group, 3, keepdims=True)
        f_kv = jnp.broadcast_to(one_kv, (2, steps_n, rows_dev, heads_dev, DH))
    else:
        kv_of_head = (tp_rank * heads_dev + jnp.arange(heads_dev)) // group
        f_kv = jnp.take(f_kv, kv_of_head, axis=3)
    f_scores = (
        jnp.einsum("sbhd,ubhd->sbhu", own_query, f_kv[0], preferred_element_type=jnp.float32)
        * score_scale
    )
    fresh_live = jnp.arange(steps_n)[None, :] <= jnp.arange(steps_n)[:, None]
    f_scores = jnp.where(fresh_live[:, None, None, :], f_scores, NEG_FILL)

    peak = jnp.maximum(got_peak.max(0), f_scores.max(-1))
    rescale = jnp.exp(got_peak - peak[None])
    f_w = jnp.exp(f_scores - peak[..., None])
    mass = (got_mass * rescale).sum(0) + f_w.sum(-1)
    numer = (got_numer * rescale[..., None]).sum(0)
    numer = numer + jnp.einsum(
        "sbhu,ubhd->sbhd", f_w.astype(jnp.bfloat16), f_kv[1], preferred_element_type=jnp.float32
    )
    attended = (numer / mass[..., None]).astype(jnp.bfloat16).reshape(steps_n, rows_dev, width_dev)

    gathered = lax.all_gather(attended, "sub", axis=1, tiled=True)
    samples = gathered.shape[1]
    local_width = out_weight.shape[1]
    head_rows_in = gathered.reshape(steps_n * samples, heads_dev, DH)
    head_weights = out_weight.reshape(heads_dev, DH, local_width)
    scale_a = jnp.repeat(jnp.exp2(-scale_in.astype(jnp.float32)), 128)
    scale_b = jnp.repeat(jnp.exp2(-scale_out.astype(jnp.float32)), 128)
    local_a = lax.dynamic_slice_in_dim(scale_a, sub_rank * local_width, local_width, 0)
    local_b = lax.dynamic_slice_in_dim(scale_b, sub_rank * local_width, local_width, 0)
    per_head_term = jnp.einsum(
        "rhd,hdf->rhf", head_rows_in, head_weights, preferred_element_type=jnp.float32
    )
    clipped = jnp.clip(per_head_term / local_a[None, None, :], -127.0, 127.0).sum(1)

    piece_cols = local_width // tp_count
    pieces = jnp.moveaxis(clipped.reshape(steps_n * samples, tp_count, piece_cols), 1, 0)
    got_pieces = _exchange(pieces, "tp", tp_count)
    summed = got_pieces.sum(0)
    piece_start = sub_rank * local_width + tp_rank * piece_cols
    piece_a = lax.dynamic_slice_in_dim(scale_a, piece_start, piece_cols, 0)
    piece_b = lax.dynamic_slice_in_dim(scale_b, piece_start, piece_cols, 0)
    levels = jnp.clip(summed * piece_a / piece_b, -127.0, 127.0).astype(jnp.bfloat16)
    level_blocks = _gather_blocks(levels, "tp", tp_count)
    all_levels = jnp.moveaxis(level_blocks, 0, 1).reshape(steps_n * samples, local_width)
    restored = all_levels.astype(jnp.float32) * local_b
    hidden = residual.reshape(steps_n * samples, local_width).astype(jnp.float32) + restored
    return hidden.astype(jnp.bfloat16).reshape(steps_n, samples, local_width)


def solution(mesh):
    return jax.shard_map(
        per_device,
        mesh=mesh,
        in_specs=(
            P(None, ("rep", "sub"), "tp"),
            P(None, ("rep", "tp"), None),
            P(None, ("rep", "sub"), "tp", None),
            P(("rep", "sub")),
            P(None, None, ("rep", "sub"), None),
            P("tp", "sub"),
            P(),
            P(),
            P(None, "rep", "sub"),
        ),
        out_specs=P(None, "rep", "sub"),
        check_vma=False,
    )
```

```python
import functools
import math

import jax
import jax.numpy as jnp
from jax import lax
from jax.experimental import pallas as pl
from jax.experimental.pallas import tpu as pltpu
from jax.sharding import PartitionSpec as P

DH = 128


NEG_FILL = -1e30


def _is_pow2(n):
    return n >= 1 and (n & (n - 1)) == 0


def _gather_blocks(x, axis_name, count):
    if count == 1:
        return x[None]
    if not _is_pow2(count):
        return lax.all_gather(x, axis_name, axis=0, tiled=False)
    me = lax.axis_index(axis_name)
    if count <= 8:
        other = lax.ppermute(x, axis_name, [(i, i ^ 1) for i in range(count)])
        low = me % 2 == 0
        pair = jnp.where(low, jnp.stack([x, other]), jnp.stack([other, x]))
        pairs = [pair]
        for d in range(1, count // 2):
            pairs.append(
                lax.ppermute(pair, axis_name, [(i, (i + 2 * d) % count) for i in range(count)])
            )
        order = (me // 2 - jnp.arange(count // 2)) % (count // 2)
        placed = jnp.zeros((count // 2,) + pair.shape, pair.dtype).at[order].set(jnp.stack(pairs))
        return placed.reshape((count,) + x.shape)
    cur = x[None]
    k = 1
    while k < count:
        other = lax.ppermute(cur, axis_name, [(i, i ^ k) for i in range(count)])
        low = (me // k) % 2 == 0
        cur = jnp.where(low, jnp.concatenate([cur, other]), jnp.concatenate([other, cur]))
        k *= 2
    return cur


def _exchange(blocks, axis_name, count, direct_max=8):
    if count == 1:
        return blocks
    if count > direct_max:
        return jax.tree.map(
            lambda b: lax.all_to_all(b, axis_name, split_axis=0, concat_axis=0, tiled=True), blocks
        )
    me = lax.axis_index(axis_name)
    got = [jax.tree.map(lambda b: lax.dynamic_index_in_dim(b, me, 0, keepdims=False), blocks)]
    for k in range(1, count):
        dst = (me + k) % count
        send = jax.tree.map(lambda b: lax.dynamic_index_in_dim(b, dst, 0, keepdims=False), blocks)
        got.append(lax.ppermute(send, axis_name, [(i, (i + k) % count) for i in range(count)]))
    return jax.tree.map(lambda *xs: jnp.stack(xs), *got)


def _attend_kernel(q_ref, k_ref, v_ref, tk_ref, tv_ref, valid_ref, numer_ref, peak_ref, mass_ref):
    heads_n, rows_n = q_ref.shape[0], q_ref.shape[1]
    samples = tk_ref.shape[1]
    per_sample = rows_n // samples
    score_scale = 1.0 / math.sqrt(DH)
    dims_nt = (((1,), (1,)), ((), ()))
    for j in range(heads_n):
        cols = slice(j * DH, (j + 1) * DH)
        q = q_ref[j]
        p_scores = lax.dot_general(q, k_ref[0, :, cols], dims_nt, preferred_element_type=jnp.float32)
        p_scores = p_scores * score_scale
        t_parts = []
        for r in range(samples):
            qr = q[r * per_sample:(r + 1) * per_sample]
            sr = lax.dot_general(
                qr, tk_ref[0, r, :, cols], dims_nt, preferred_element_type=jnp.float32
            )
            sr = sr * score_scale
            t_parts.append(jnp.where(valid_ref[r:r + 1, :] > 0.0, sr, NEG_FILL))
        t_scores = jnp.concatenate(t_parts, axis=0)
        peak = jnp.maximum(
            jnp.max(p_scores, axis=1, keepdims=True), jnp.max(t_scores, axis=1, keepdims=True)
        )
        p_w = jnp.exp(p_scores - peak)
        t_w = jnp.exp(t_scores - peak)
        mass = jnp.sum(p_w, axis=1, keepdims=True) + jnp.sum(t_w, axis=1, keepdims=True)
        numer = jnp.dot(
            p_w.astype(jnp.bfloat16), v_ref[0, :, cols], preferred_element_type=jnp.float32
        )
        t_w16 = t_w.astype(jnp.bfloat16)
        t_numer = [
            jnp.dot(
                t_w16[r * per_sample:(r + 1) * per_sample], tv_ref[0, r, :, cols],
                preferred_element_type=jnp.float32,
            )
            for r in range(samples)
        ]
        numer_ref[j] = numer + jnp.concatenate(t_numer, axis=0)
        peak_ref[j] = jnp.broadcast_to(peak, peak_ref.shape[1:])
        mass_ref[j] = jnp.broadcast_to(mass, mass_ref.shape[1:])


def _attend_local(q_rows, prefix_kv, tail_kv, valid):
    kv_heads, rows_n, _ = q_rows.shape
    prefix_dev = prefix_kv.shape[1]
    samples, tail_dev = tail_kv.shape[1], tail_kv.shape[2]
    flops = 4 * kv_heads * rows_n * DH * (prefix_dev + tail_dev)
    bytes_in = 2 * (prefix_kv.size + tail_kv.size + q_rows.size)
    per_step = 4 if kv_heads % 4 == 0 else 1
    width = per_step * DH
    return pl.pallas_call(
        _attend_kernel,
        grid=(kv_heads // per_step,),
        in_specs=[
            pl.BlockSpec((per_step, rows_n, DH), lambda k: (k, 0, 0)),
            pl.BlockSpec((1, prefix_dev, width), lambda k: (0, 0, k)),
            pl.BlockSpec((1, prefix_dev, width), lambda k: (1, 0, k)),
            pl.BlockSpec((1, samples, tail_dev, width), lambda k: (0, 0, 0, k)),
            pl.BlockSpec((1, samples, tail_dev, width), lambda k: (1, 0, 0, k)),
            pl.BlockSpec((samples, tail_dev), lambda k: (0, 0)),
        ],
        out_specs=[
            pl.BlockSpec((per_step, rows_n, DH), lambda k: (k, 0, 0)),
            pl.BlockSpec((per_step, rows_n, DH), lambda k: (k, 0, 0)),
            pl.BlockSpec((per_step, rows_n, DH), lambda k: (k, 0, 0)),
        ],
        out_shape=[jax.ShapeDtypeStruct((kv_heads, rows_n, DH), jnp.float32)] * 3,
        cost_estimate=pl.CostEstimate(
            flops=flops,
            transcendentals=kv_heads * rows_n * (prefix_dev + tail_dev),
            bytes_accessed=bytes_in + 3 * 4 * kv_heads * rows_n * DH,
        ),
        compiler_params=pltpu.CompilerParams(vmem_limit_bytes=48 * 1024 * 1024),
    )(q_rows, prefix_kv, prefix_kv, tail_kv, tail_kv, valid)


def _attend_packed_kernel(
    group, q_ref, k_ref, v_ref, tk_ref, tv_ref, valid_ref, out_ref
):
    heads_n, rows_n = q_ref.shape[0], q_ref.shape[1]
    samples, tail_dev = tk_ref.shape[1], tk_ref.shape[2]
    score_scale = 1.0 / math.sqrt(DH)
    dims_nt = (((1,), (1,)), ((), ()))
    row_sample = (lax.broadcasted_iota(jnp.int32, (rows_n, tail_dev), 0) // group) % samples
    for j in range(heads_n):
        cols = slice(j * DH, (j + 1) * DH)
        q = q_ref[j]
        p_scores = lax.dot_general(q, k_ref[0, :, cols], dims_nt, preferred_element_type=jnp.float32)
        p_scores = p_scores * score_scale
        t_scores = jnp.full((rows_n, tail_dev), NEG_FILL, jnp.float32)
        for r in range(samples):
            sr = lax.dot_general(
                q, tk_ref[0, r, :, cols], dims_nt, preferred_element_type=jnp.float32
            )
            live = (row_sample == r) & (valid_ref[r:r + 1, :] > 0.0)
            t_scores = jnp.where(live, sr * score_scale, t_scores)
        peak = jnp.maximum(
            jnp.max(p_scores, axis=1, keepdims=True), jnp.max(t_scores, axis=1, keepdims=True)
        )
        p_w = jnp.exp(p_scores - peak)
        t_w = jnp.exp(t_scores - peak)
        mass = jnp.sum(p_w, axis=1, keepdims=True) + jnp.sum(t_w, axis=1, keepdims=True)
        numer = jnp.dot(
            p_w.astype(jnp.bfloat16), v_ref[0, :, cols], preferred_element_type=jnp.float32
        )
        for r in range(samples):
            t_w16 = jnp.where(row_sample == r, t_w, 0.0).astype(jnp.bfloat16)
            numer = numer + jnp.dot(t_w16, tv_ref[0, r, :, cols], preferred_element_type=jnp.float32)
        out_ref[j, :rows_n, :] = numer
        peak_row = jnp.transpose(jnp.broadcast_to(peak, (rows_n, DH)))[0:1]
        mass_row = jnp.transpose(jnp.broadcast_to(mass, (rows_n, DH)))[0:1]
        out_ref[j, rows_n:, :] = jnp.concatenate(
            [peak_row, mass_row, jnp.zeros((6, DH), jnp.float32)], axis=0
        )


def _attend_packed(q_rows, prefix_kv, tail_kv, valid, group):
    kv_heads, rows_n, _ = q_rows.shape
    prefix_dev = prefix_kv.shape[1]
    samples, tail_dev = tail_kv.shape[1], tail_kv.shape[2]
    flops = 4 * kv_heads * rows_n * DH * (prefix_dev + samples * tail_dev)
    bytes_in = 2 * (prefix_kv.size + tail_kv.size + q_rows.size)
    per_step = 4 if kv_heads % 4 == 0 else 1
    width = per_step * DH
    return pl.pallas_call(
        functools.partial(_attend_packed_kernel, group),
        grid=(kv_heads // per_step,),
        in_specs=[
            pl.BlockSpec((per_step, rows_n, DH), lambda k: (k, 0, 0)),
            pl.BlockSpec((1, prefix_dev, width), lambda k: (0, 0, k)),
            pl.BlockSpec((1, prefix_dev, width), lambda k: (1, 0, k)),
            pl.BlockSpec((1, samples, tail_dev, width), lambda k: (0, 0, 0, k)),
            pl.BlockSpec((1, samples, tail_dev, width), lambda k: (1, 0, 0, k)),
            pl.BlockSpec((samples, tail_dev), lambda k: (0, 0)),
        ],
        out_specs=pl.BlockSpec((per_step, rows_n + 8, DH), lambda k: (k, 0, 0)),
        out_shape=jax.ShapeDtypeStruct((kv_heads, rows_n + 8, DH), jnp.float32),
        cost_estimate=pl.CostEstimate(
            flops=flops,
            transcendentals=kv_heads * rows_n * (prefix_dev + tail_dev),
            bytes_accessed=bytes_in + 4 * kv_heads * (rows_n + 8) * DH,
        ),
        compiler_params=pltpu.CompilerParams(vmem_limit_bytes=48 * 1024 * 1024),
    )(q_rows, prefix_kv, prefix_kv, tail_kv, tail_kv, valid)


def _attend_packed_pairs(blk, q_rows, prefix_kv, tail_kv, valid, group):
    heads_n, rows_n, _ = q_rows.shape
    prefix_dev = prefix_kv.shape[1]
    samples, tail_dev = tail_kv.shape[1], tail_kv.shape[2]
    flops = 4 * heads_n * rows_n * DH * (prefix_dev + samples * tail_dev)
    width = 2 * DH
    grid_spec = pltpu.PrefetchScalarGridSpec(
        num_scalar_prefetch=1,
        grid=(heads_n // 2,),
        in_specs=[
            pl.BlockSpec((2, rows_n, DH), lambda g, b: (g, 0, 0)),
            pl.BlockSpec((1, prefix_dev, width), lambda g, b: (0, 0, b[g])),
            pl.BlockSpec((1, prefix_dev, width), lambda g, b: (1, 0, b[g])),
            pl.BlockSpec((1, samples, tail_dev, width), lambda g, b: (0, 0, 0, b[g])),
            pl.BlockSpec((1, samples, tail_dev, width), lambda g, b: (1, 0, 0, b[g])),
            pl.BlockSpec((samples, tail_dev), lambda g, b: (0, 0)),
        ],
        out_specs=pl.BlockSpec((2, rows_n + 8, DH), lambda g, b: (g, 0, 0)),
    )
    return pl.pallas_call(
        lambda b_ref, *refs: _attend_packed_kernel(group, *refs),
        grid_spec=grid_spec,
        out_shape=jax.ShapeDtypeStruct((heads_n, rows_n + 8, DH), jnp.float32),
        cost_estimate=pl.CostEstimate(
            flops=flops,
            transcendentals=heads_n * rows_n * (prefix_dev + tail_dev),
            bytes_accessed=2 * (2 * prefix_dev + 2 * samples * tail_dev) * heads_n * DH
            + 2 * q_rows.size + 4 * heads_n * (rows_n + 8) * DH,
        ),
        compiler_params=pltpu.CompilerParams(vmem_limit_bytes=48 * 1024 * 1024),
    )(blk.astype(jnp.int32), q_rows, prefix_kv, prefix_kv, tail_kv, tail_kv, valid)


def per_device(
    queries, prefix_kv, tail_kv, tail_lengths, fresh_kv, out_weight, scale_in, scale_out, residual
):
    steps_n, rows_dev, width_dev = queries.shape
    heads_dev = width_dev // DH
    tp_count = lax.axis_size("tp")
    tp_rank = lax.axis_index("tp")
    sub_rank = lax.axis_index("sub")
    kv_heads = prefix_kv.shape[2] // DH
    heads_all = heads_dev * tp_count
    group = heads_all // kv_heads
    prefix_dev = prefix_kv.shape[1]
    tail_dev = tail_kv.shape[2]
    score_scale = 1.0 / math.sqrt(DH)

    n_rows = steps_n * rows_dev * heads_dev
    pairs_ok = (tp_count == kv_heads and heads_dev == group and n_rows == DH
                and tp_count in (4, 8))
    if pairs_ok:
        t_pos = tp_rank * tail_dev + jnp.arange(tail_dev)
        valid = (t_pos[None, :] < tail_lengths[:, None]).astype(jnp.float32)
        half = tp_count // 2
        mine = tp_rank // 2
        other = lax.ppermute(queries, "tp", [(i, i ^ 1) for i in range(tp_count)])
        pair = jnp.where(tp_rank % 2 == 0, jnp.stack([queries, other]), jnp.stack([other, queries]))
        far = [
            lax.ppermute(pair, "tp", [(i, (i + 2 * d) % tp_count) for i in range(tp_count)])
            for d in range(1, half)
        ]
        out_near = _attend_packed_pairs(
            jnp.reshape(mine, (1,)), pair.reshape(2, -1, DH), prefix_kv, tail_kv, valid, group
        )
        far_blk = (mine - jnp.arange(1, half)) % half
        out_far = _attend_packed_pairs(
            far_blk, jnp.stack(far).reshape(2 * (half - 1), -1, DH), prefix_kv, tail_kv, valid,
            group,
        )
        outs = jnp.concatenate([out_near, out_far])

        def position(head):
            d = (mine - head // 2) % half
            return jnp.where(d == 0, head % 2, 2 * d + head % 2)

        got = [
            lax.dynamic_index_in_dim(out_near, tp_rank % 2, 0, keepdims=False),
            lax.ppermute(
                lax.dynamic_index_in_dim(out_near, 1 - tp_rank % 2, 0, keepdims=False),
                "tp", [(i, i ^ 1) for i in range(tp_count)],
            ),
        ]
        for d in range(1, half):
            for flip in (0, 1):
                dst = ((mine + d) % half) * 2 + (tp_rank % 2 ^ flip)
                perm = [(i, ((i // 2 + d) % half) * 2 + (i % 2 ^ flip)) for i in range(tp_count)]
                send = lax.dynamic_index_in_dim(outs, position(dst), 0, keepdims=False)
                got.append(lax.ppermute(send, "tp", perm))
        got = jnp.stack(got)
        got_numer = got[:, :n_rows].reshape(tp_count, steps_n, rows_dev, heads_dev, DH)
        got_peak = got[:, n_rows].reshape(tp_count, steps_n, rows_dev, heads_dev)
        got_mass = got[:, n_rows + 1].reshape(tp_count, steps_n, rows_dev, heads_dev)
        q_blocks = None
    else:
        q_blocks = _gather_blocks(queries, "tp", tp_count)
    if not pairs_ok:
        q_all = jnp.moveaxis(q_blocks, 0, 2).reshape(steps_n, rows_dev, kv_heads, group, DH)
        t_pos = tp_rank * tail_dev + jnp.arange(tail_dev)
        valid = (t_pos[None, :] < tail_lengths[:, None]).astype(jnp.float32)
        n_rows = steps_n * rows_dev * heads_dev
        if tp_count == kv_heads and heads_dev == group and n_rows == DH:
            q_rows = jnp.transpose(q_all, (2, 0, 1, 3, 4)).reshape(kv_heads, -1, DH)
            got = _exchange(_attend_packed(q_rows, prefix_kv, tail_kv, valid, group), "tp", tp_count)
            got_numer = got[:, :n_rows].reshape(tp_count, steps_n, rows_dev, heads_dev, DH)
            got_peak = got[:, n_rows].reshape(tp_count, steps_n, rows_dev, heads_dev)
            got_mass = got[:, n_rows + 1].reshape(tp_count, steps_n, rows_dev, heads_dev)
        else:

            q_rows = jnp.transpose(q_all, (2, 1, 0, 3, 4)).reshape(kv_heads, -1, DH)
            t_pos = tp_rank * tail_dev + jnp.arange(tail_dev)
            valid = (t_pos[None, :] < tail_lengths[:, None]).astype(jnp.float32)
            k_numer, k_peak, k_mass = _attend_local(q_rows, prefix_kv, tail_kv, valid)

            def by_owner(x):
                x = jnp.transpose(x, (2, 1, 0, 3) + tuple(range(4, x.ndim)))
                x = x.reshape((steps_n, rows_dev, tp_count, heads_dev) + x.shape[4:])
                return jnp.moveaxis(x, 2, 0)

            grid4 = (kv_heads, rows_dev, steps_n, group)
            o_numer = by_owner(k_numer.reshape(grid4 + (DH,))).reshape(tp_count, -1, DH)
            o_peak = by_owner(k_peak[..., 0].reshape(grid4)).reshape(tp_count, -1)
            o_mass = by_owner(k_mass[..., 0].reshape(grid4)).reshape(tp_count, -1)
            n_rows = steps_n * rows_dev * heads_dev
            n_stat = -(-2 * n_rows // DH)
            stats = jnp.concatenate([o_peak, o_mass], axis=1)
            stats = jnp.pad(stats, ((0, 0), (0, n_stat * DH - 2 * n_rows))).reshape(tp_count, n_stat, DH)
            got = _exchange(jnp.concatenate([o_numer, stats], axis=1), "tp", tp_count)
            got_numer = got[:, :n_rows].reshape(tp_count, steps_n, rows_dev, heads_dev, DH)
            got_stats = got[:, n_rows:].reshape(tp_count, -1)[:, : 2 * n_rows]
            got_stats = got_stats.reshape(tp_count, 2, steps_n, rows_dev, heads_dev)
            got_peak = got_stats[:, 0]
            got_mass = got_stats[:, 1]

    own_query = queries.reshape(steps_n, rows_dev, heads_dev, DH)
    f_kv = fresh_kv.reshape(2, steps_n, rows_dev, kv_heads, DH)
    if group % heads_dev == 0:
        one_kv = lax.dynamic_index_in_dim(f_kv, tp_rank * heads_dev // group, 3, keepdims=True)
        f_kv = jnp.broadcast_to(one_kv, (2, steps_n, rows_dev, heads_dev, DH))
    else:
        kv_of_head = (tp_rank * heads_dev + jnp.arange(heads_dev)) // group
        f_kv = jnp.take(f_kv, kv_of_head, axis=3)
    f_scores = (
        jnp.einsum("sbhd,ubhd->sbhu", own_query, f_kv[0], preferred_element_type=jnp.float32)
        * score_scale
    )
    fresh_live = jnp.arange(steps_n)[None, :] <= jnp.arange(steps_n)[:, None]
    f_scores = jnp.where(fresh_live[:, None, None, :], f_scores, NEG_FILL)

    peak = jnp.maximum(got_peak.max(0), f_scores.max(-1))
    rescale = jnp.exp(got_peak - peak[None])
    f_w = jnp.exp(f_scores - peak[..., None])
    mass = (got_mass * rescale).sum(0) + f_w.sum(-1)
    numer = (got_numer * rescale[..., None]).sum(0)
    numer = numer + jnp.einsum(
        "sbhu,ubhd->sbhd", f_w.astype(jnp.bfloat16), f_kv[1], preferred_element_type=jnp.float32
    )
    attended = (numer / mass[..., None]).astype(jnp.bfloat16).reshape(steps_n, rows_dev, width_dev)

    gathered = lax.all_gather(attended, "sub", axis=1, tiled=True)
    samples = gathered.shape[1]
    local_width = out_weight.shape[1]
    head_rows_in = gathered.reshape(steps_n * samples, heads_dev, DH)
    head_weights = out_weight.reshape(heads_dev, DH, local_width)
    scale_a = jnp.repeat(jnp.exp2(-scale_in.astype(jnp.float32)), 128)
    scale_b = jnp.repeat(jnp.exp2(-scale_out.astype(jnp.float32)), 128)
    local_a = lax.dynamic_slice_in_dim(scale_a, sub_rank * local_width, local_width, 0)
    local_b = lax.dynamic_slice_in_dim(scale_b, sub_rank * local_width, local_width, 0)
    per_head_term = jnp.einsum(
        "rhd,hdf->rhf", head_rows_in, head_weights, preferred_element_type=jnp.float32
    )
    clipped = jnp.clip(per_head_term / local_a[None, None, :], -127.0, 127.0).sum(1)

    piece_cols = local_width // tp_count
    pieces = jnp.moveaxis(clipped.reshape(steps_n * samples, tp_count, piece_cols), 1, 0)
    got_pieces = _exchange(pieces, "tp", tp_count)
    summed = got_pieces.sum(0)
    piece_start = sub_rank * local_width + tp_rank * piece_cols
    piece_a = lax.dynamic_slice_in_dim(scale_a, piece_start, piece_cols, 0)
    piece_b = lax.dynamic_slice_in_dim(scale_b, piece_start, piece_cols, 0)
    levels = jnp.clip(summed * piece_a / piece_b, -127.0, 127.0).astype(jnp.bfloat16)
    level_blocks = _gather_blocks(levels, "tp", tp_count)
    all_levels = jnp.moveaxis(level_blocks, 0, 1).reshape(steps_n * samples, local_width)
    restored = all_levels.astype(jnp.float32) * local_b
    hidden = residual.reshape(steps_n * samples, local_width).astype(jnp.float32) + restored
    return hidden.astype(jnp.bfloat16).reshape(steps_n, samples, local_width)


def solution(mesh):
    return jax.shard_map(
        per_device,
        mesh=mesh,
        in_specs=(
            P(None, ("rep", "sub"), "tp"),
            P(None, ("rep", "tp"), None),
            P(None, ("rep", "sub"), "tp", None),
            P(("rep", "sub")),
            P(None, None, ("rep", "sub"), None),
            P("tp", "sub"),
            P(),
            P(),
            P(None, "rep", "sub"),
        ),
        out_specs=P(None, "rep", "sub"),
        check_vma=False,
    )
```

```python
import functools
import math

import jax
import jax.numpy as jnp
from jax import lax
from jax.experimental import pallas as pl
from jax.experimental.pallas import tpu as pltpu
from jax.sharding import PartitionSpec as P

DH = 128


NEG_FILL = -1e30


def _is_pow2(n):
    return n >= 1 and (n & (n - 1)) == 0


def _gather_blocks(x, axis_name, count):
    if count == 1:
        return x[None]
    if not _is_pow2(count):
        return lax.all_gather(x, axis_name, axis=0, tiled=False)
    me = lax.axis_index(axis_name)
    if count <= 8:
        other = lax.ppermute(x, axis_name, [(i, i ^ 1) for i in range(count)])
        low = me % 2 == 0
        pair = jnp.where(low, jnp.stack([x, other]), jnp.stack([other, x]))
        pairs = [pair]
        for d in range(1, count // 2):
            pairs.append(
                lax.ppermute(pair, axis_name, [(i, (i + 2 * d) % count) for i in range(count)])
            )
        order = (me // 2 - jnp.arange(count // 2)) % (count // 2)
        placed = jnp.zeros((count // 2,) + pair.shape, pair.dtype).at[order].set(jnp.stack(pairs))
        return placed.reshape((count,) + x.shape)
    cur = x[None]
    k = 1
    while k < count:
        other = lax.ppermute(cur, axis_name, [(i, i ^ k) for i in range(count)])
        low = (me // k) % 2 == 0
        cur = jnp.where(low, jnp.concatenate([cur, other]), jnp.concatenate([other, cur]))
        k *= 2
    return cur


def _exchange(blocks, axis_name, count, direct_max=8):
    if count == 1:
        return blocks
    if count > direct_max:
        return jax.tree.map(
            lambda b: lax.all_to_all(b, axis_name, split_axis=0, concat_axis=0, tiled=True), blocks
        )
    me = lax.axis_index(axis_name)
    got = [jax.tree.map(lambda b: lax.dynamic_index_in_dim(b, me, 0, keepdims=False), blocks)]
    for k in range(1, count):
        dst = (me + k) % count
        send = jax.tree.map(lambda b: lax.dynamic_index_in_dim(b, dst, 0, keepdims=False), blocks)
        got.append(lax.ppermute(send, axis_name, [(i, (i + k) % count) for i in range(count)]))
    return jax.tree.map(lambda *xs: jnp.stack(xs), *got)


def _attend_kernel(q_ref, k_ref, v_ref, tk_ref, tv_ref, valid_ref, numer_ref, peak_ref, mass_ref):
    heads_n, rows_n = q_ref.shape[0], q_ref.shape[1]
    samples = tk_ref.shape[1]
    per_sample = rows_n // samples
    score_scale = 1.0 / math.sqrt(DH)
    dims_nt = (((1,), (1,)), ((), ()))
    for j in range(heads_n):
        cols = slice(j * DH, (j + 1) * DH)
        q = q_ref[j]
        p_scores = lax.dot_general(q, k_ref[0, :, cols], dims_nt, preferred_element_type=jnp.float32)
        p_scores = p_scores * score_scale
        t_parts = []
        for r in range(samples):
            qr = q[r * per_sample:(r + 1) * per_sample]
            sr = lax.dot_general(
                qr, tk_ref[0, r, :, cols], dims_nt, preferred_element_type=jnp.float32
            )
            sr = sr * score_scale
            t_parts.append(jnp.where(valid_ref[r:r + 1, :] > 0.0, sr, NEG_FILL))
        t_scores = jnp.concatenate(t_parts, axis=0)
        peak = jnp.maximum(
            jnp.max(p_scores, axis=1, keepdims=True), jnp.max(t_scores, axis=1, keepdims=True)
        )
        p_w = jnp.exp(p_scores - peak)
        t_w = jnp.exp(t_scores - peak)
        mass = jnp.sum(p_w, axis=1, keepdims=True) + jnp.sum(t_w, axis=1, keepdims=True)
        numer = jnp.dot(
            p_w.astype(jnp.bfloat16), v_ref[0, :, cols], preferred_element_type=jnp.float32
        )
        t_w16 = t_w.astype(jnp.bfloat16)
        t_numer = [
            jnp.dot(
                t_w16[r * per_sample:(r + 1) * per_sample], tv_ref[0, r, :, cols],
                preferred_element_type=jnp.float32,
            )
            for r in range(samples)
        ]
        numer_ref[j] = numer + jnp.concatenate(t_numer, axis=0)
        peak_ref[j] = jnp.broadcast_to(peak, peak_ref.shape[1:])
        mass_ref[j] = jnp.broadcast_to(mass, mass_ref.shape[1:])


def _attend_local(q_rows, prefix_kv, tail_kv, valid):
    kv_heads, rows_n, _ = q_rows.shape
    prefix_dev = prefix_kv.shape[1]
    samples, tail_dev = tail_kv.shape[1], tail_kv.shape[2]
    flops = 4 * kv_heads * rows_n * DH * (prefix_dev + tail_dev)
    bytes_in = 2 * (prefix_kv.size + tail_kv.size + q_rows.size)
    per_step = 4 if kv_heads % 4 == 0 else 1
    width = per_step * DH
    return pl.pallas_call(
        _attend_kernel,
        grid=(kv_heads // per_step,),
        in_specs=[
            pl.BlockSpec((per_step, rows_n, DH), lambda k: (k, 0, 0)),
            pl.BlockSpec((1, prefix_dev, width), lambda k: (0, 0, k)),
            pl.BlockSpec((1, prefix_dev, width), lambda k: (1, 0, k)),
            pl.BlockSpec((1, samples, tail_dev, width), lambda k: (0, 0, 0, k)),
            pl.BlockSpec((1, samples, tail_dev, width), lambda k: (1, 0, 0, k)),
            pl.BlockSpec((samples, tail_dev), lambda k: (0, 0)),
        ],
        out_specs=[
            pl.BlockSpec((per_step, rows_n, DH), lambda k: (k, 0, 0)),
            pl.BlockSpec((per_step, rows_n, DH), lambda k: (k, 0, 0)),
            pl.BlockSpec((per_step, rows_n, DH), lambda k: (k, 0, 0)),
        ],
        out_shape=[jax.ShapeDtypeStruct((kv_heads, rows_n, DH), jnp.float32)] * 3,
        cost_estimate=pl.CostEstimate(
            flops=flops,
            transcendentals=kv_heads * rows_n * (prefix_dev + tail_dev),
            bytes_accessed=bytes_in + 3 * 4 * kv_heads * rows_n * DH,
        ),
        compiler_params=pltpu.CompilerParams(vmem_limit_bytes=48 * 1024 * 1024),
    )(q_rows, prefix_kv, prefix_kv, tail_kv, tail_kv, valid)


def _attend_packed_kernel(
    group, q_ref, k_ref, v_ref, tk_ref, tv_ref, valid_ref, out_ref
):
    heads_n, rows_n = q_ref.shape[0], q_ref.shape[1]
    samples, tail_dev = tk_ref.shape[1], tk_ref.shape[2]
    score_scale = 1.0 / math.sqrt(DH)
    dims_nt = (((1,), (1,)), ((), ()))
    row_sample = (lax.broadcasted_iota(jnp.int32, (rows_n, tail_dev), 0) // group) % samples
    for j in range(heads_n):
        cols = slice(j * DH, (j + 1) * DH)
        q = q_ref[j]
        p_scores = lax.dot_general(q, k_ref[0, :, cols], dims_nt, preferred_element_type=jnp.float32)
        p_scores = p_scores * score_scale
        t_scores = jnp.full((rows_n, tail_dev), NEG_FILL, jnp.float32)
        for r in range(samples):
            sr = lax.dot_general(
                q, tk_ref[0, r, :, cols], dims_nt, preferred_element_type=jnp.float32
            )
            live = (row_sample == r) & (valid_ref[r:r + 1, :] > 0.0)
            t_scores = jnp.where(live, sr * score_scale, t_scores)
        peak = jnp.maximum(
            jnp.max(p_scores, axis=1, keepdims=True), jnp.max(t_scores, axis=1, keepdims=True)
        )
        p_w = jnp.exp(p_scores - peak)
        t_w = jnp.exp(t_scores - peak)
        mass = jnp.sum(p_w, axis=1, keepdims=True) + jnp.sum(t_w, axis=1, keepdims=True)
        numer = jnp.dot(
            p_w.astype(jnp.bfloat16), v_ref[0, :, cols], preferred_element_type=jnp.float32
        )
        for r in range(samples):
            t_w16 = jnp.where(row_sample == r, t_w, 0.0).astype(jnp.bfloat16)
            numer = numer + jnp.dot(t_w16, tv_ref[0, r, :, cols], preferred_element_type=jnp.float32)
        out_ref[j, :rows_n, :] = numer
        peak_row = jnp.transpose(jnp.broadcast_to(peak, (rows_n, DH)))[0:1]
        mass_row = jnp.transpose(jnp.broadcast_to(mass, (rows_n, DH)))[0:1]
        out_ref[j, rows_n:, :] = jnp.concatenate(
            [peak_row, mass_row, jnp.zeros((6, DH), jnp.float32)], axis=0
        )


def _attend_packed(q_rows, prefix_kv, tail_kv, valid, group):
    kv_heads, rows_n, _ = q_rows.shape
    prefix_dev = prefix_kv.shape[1]
    samples, tail_dev = tail_kv.shape[1], tail_kv.shape[2]
    flops = 4 * kv_heads * rows_n * DH * (prefix_dev + samples * tail_dev)
    bytes_in = 2 * (prefix_kv.size + tail_kv.size + q_rows.size)
    per_step = 4 if kv_heads % 4 == 0 else 1
    width = per_step * DH
    return pl.pallas_call(
        functools.partial(_attend_packed_kernel, group),
        grid=(kv_heads // per_step,),
        in_specs=[
            pl.BlockSpec((per_step, rows_n, DH), lambda k: (k, 0, 0)),
            pl.BlockSpec((1, prefix_dev, width), lambda k: (0, 0, k)),
            pl.BlockSpec((1, prefix_dev, width), lambda k: (1, 0, k)),
            pl.BlockSpec((1, samples, tail_dev, width), lambda k: (0, 0, 0, k)),
            pl.BlockSpec((1, samples, tail_dev, width), lambda k: (1, 0, 0, k)),
            pl.BlockSpec((samples, tail_dev), lambda k: (0, 0)),
        ],
        out_specs=pl.BlockSpec((per_step, rows_n + 8, DH), lambda k: (k, 0, 0)),
        out_shape=jax.ShapeDtypeStruct((kv_heads, rows_n + 8, DH), jnp.float32),
        cost_estimate=pl.CostEstimate(
            flops=flops,
            transcendentals=kv_heads * rows_n * (prefix_dev + tail_dev),
            bytes_accessed=bytes_in + 4 * kv_heads * (rows_n + 8) * DH,
        ),
        compiler_params=pltpu.CompilerParams(vmem_limit_bytes=48 * 1024 * 1024),
    )(q_rows, prefix_kv, prefix_kv, tail_kv, tail_kv, valid)


def _attend_packed_pairs(blk, q_rows, prefix_kv, tail_kv, valid, group):
    heads_n, rows_n, _ = q_rows.shape
    prefix_dev = prefix_kv.shape[1]
    samples, tail_dev = tail_kv.shape[1], tail_kv.shape[2]
    flops = 4 * heads_n * rows_n * DH * (prefix_dev + samples * tail_dev)
    width = 2 * DH
    grid_spec = pltpu.PrefetchScalarGridSpec(
        num_scalar_prefetch=1,
        grid=(heads_n // 2,),
        in_specs=[
            pl.BlockSpec((2, rows_n, DH), lambda g, b: (g, 0, 0)),
            pl.BlockSpec((1, prefix_dev, width), lambda g, b: (0, 0, b[g])),
            pl.BlockSpec((1, prefix_dev, width), lambda g, b: (1, 0, b[g])),
            pl.BlockSpec((1, samples, tail_dev, width), lambda g, b: (0, 0, 0, b[g])),
            pl.BlockSpec((1, samples, tail_dev, width), lambda g, b: (1, 0, 0, b[g])),
            pl.BlockSpec((samples, tail_dev), lambda g, b: (0, 0)),
        ],
        out_specs=pl.BlockSpec((2, rows_n + 8, DH), lambda g, b: (g, 0, 0)),
    )
    return pl.pallas_call(
        lambda b_ref, *refs: _attend_packed_kernel(group, *refs),
        grid_spec=grid_spec,
        out_shape=jax.ShapeDtypeStruct((heads_n, rows_n + 8, DH), jnp.float32),
        cost_estimate=pl.CostEstimate(
            flops=flops,
            transcendentals=heads_n * rows_n * (prefix_dev + tail_dev),
            bytes_accessed=2 * (2 * prefix_dev + 2 * samples * tail_dev) * heads_n * DH
            + 2 * q_rows.size + 4 * heads_n * (rows_n + 8) * DH,
        ),
        compiler_params=pltpu.CompilerParams(vmem_limit_bytes=48 * 1024 * 1024),
    )(blk.astype(jnp.int32), q_rows, prefix_kv, prefix_kv, tail_kv, tail_kv, valid)


def per_device(
    queries, prefix_kv, tail_kv, tail_lengths, fresh_kv, out_weight, scale_in, scale_out, residual
):
    steps_n, rows_dev, width_dev = queries.shape
    heads_dev = width_dev // DH
    tp_count = lax.axis_size("tp")
    tp_rank = lax.axis_index("tp")
    sub_rank = lax.axis_index("sub")
    kv_heads = prefix_kv.shape[2] // DH
    heads_all = heads_dev * tp_count
    group = heads_all // kv_heads
    prefix_dev = prefix_kv.shape[1]
    tail_dev = tail_kv.shape[2]
    score_scale = 1.0 / math.sqrt(DH)

    n_rows = steps_n * rows_dev * heads_dev
    pairs_ok = (tp_count == kv_heads and heads_dev == group and n_rows == DH
                and tp_count in (4, 8))
    if pairs_ok:
        t_pos = tp_rank * tail_dev + jnp.arange(tail_dev)
        valid = (t_pos[None, :] < tail_lengths[:, None]).astype(jnp.float32)
        half = tp_count // 2
        mine = tp_rank // 2
        other = lax.ppermute(queries, "tp", [(i, i ^ 1) for i in range(tp_count)])
        pair = jnp.where(tp_rank % 2 == 0, jnp.stack([queries, other]), jnp.stack([other, queries]))
        far = [
            lax.ppermute(pair, "tp", [(i, (i + 2 * d) % tp_count) for i in range(tp_count)])
            for d in range(1, half)
        ]
        out_near = _attend_packed_pairs(
            jnp.reshape(mine, (1,)), pair.reshape(2, -1, DH), prefix_kv, tail_kv, valid, group
        )
        got = [
            lax.dynamic_index_in_dim(out_near, tp_rank % 2, 0, keepdims=False),
            lax.ppermute(
                lax.dynamic_index_in_dim(out_near, 1 - tp_rank % 2, 0, keepdims=False),
                "tp", [(i, i ^ 1) for i in range(tp_count)],
            ),
        ]
        for d in range(1, half):
            out_d = _attend_packed_pairs(
                jnp.reshape((mine - d) % half, (1,)), far[d - 1].reshape(2, -1, DH),
                prefix_kv, tail_kv, valid, group,
            )
            for flip in (0, 1):
                perm = [(i, ((i // 2 - d) % half) * 2 + (i % 2 ^ flip)) for i in range(tp_count)]
                send = lax.dynamic_index_in_dim(out_d, tp_rank % 2 ^ flip, 0, keepdims=False)
                got.append(lax.ppermute(send, "tp", perm))
        got = jnp.stack(got)
        got_numer = got[:, :n_rows].reshape(tp_count, steps_n, rows_dev, heads_dev, DH)
        got_peak = got[:, n_rows].reshape(tp_count, steps_n, rows_dev, heads_dev)
        got_mass = got[:, n_rows + 1].reshape(tp_count, steps_n, rows_dev, heads_dev)
        q_blocks = None
    else:
        q_blocks = _gather_blocks(queries, "tp", tp_count)
    if not pairs_ok:
        q_all = jnp.moveaxis(q_blocks, 0, 2).reshape(steps_n, rows_dev, kv_heads, group, DH)
        t_pos = tp_rank * tail_dev + jnp.arange(tail_dev)
        valid = (t_pos[None, :] < tail_lengths[:, None]).astype(jnp.float32)
        n_rows = steps_n * rows_dev * heads_dev
        if tp_count == kv_heads and heads_dev == group and n_rows == DH:
            q_rows = jnp.transpose(q_all, (2, 0, 1, 3, 4)).reshape(kv_heads, -1, DH)
            got = _exchange(_attend_packed(q_rows, prefix_kv, tail_kv, valid, group), "tp", tp_count)
            got_numer = got[:, :n_rows].reshape(tp_count, steps_n, rows_dev, heads_dev, DH)
            got_peak = got[:, n_rows].reshape(tp_count, steps_n, rows_dev, heads_dev)
            got_mass = got[:, n_rows + 1].reshape(tp_count, steps_n, rows_dev, heads_dev)
        else:

            q_rows = jnp.transpose(q_all, (2, 1, 0, 3, 4)).reshape(kv_heads, -1, DH)
            t_pos = tp_rank * tail_dev + jnp.arange(tail_dev)
            valid = (t_pos[None, :] < tail_lengths[:, None]).astype(jnp.float32)
            k_numer, k_peak, k_mass = _attend_local(q_rows, prefix_kv, tail_kv, valid)

            def by_owner(x):
                x = jnp.transpose(x, (2, 1, 0, 3) + tuple(range(4, x.ndim)))
                x = x.reshape((steps_n, rows_dev, tp_count, heads_dev) + x.shape[4:])
                return jnp.moveaxis(x, 2, 0)

            grid4 = (kv_heads, rows_dev, steps_n, group)
            o_numer = by_owner(k_numer.reshape(grid4 + (DH,))).reshape(tp_count, -1, DH)
            o_peak = by_owner(k_peak[..., 0].reshape(grid4)).reshape(tp_count, -1)
            o_mass = by_owner(k_mass[..., 0].reshape(grid4)).reshape(tp_count, -1)
            n_rows = steps_n * rows_dev * heads_dev
            n_stat = -(-2 * n_rows // DH)
            stats = jnp.concatenate([o_peak, o_mass], axis=1)
            stats = jnp.pad(stats, ((0, 0), (0, n_stat * DH - 2 * n_rows))).reshape(tp_count, n_stat, DH)
            got = _exchange(jnp.concatenate([o_numer, stats], axis=1), "tp", tp_count)
            got_numer = got[:, :n_rows].reshape(tp_count, steps_n, rows_dev, heads_dev, DH)
            got_stats = got[:, n_rows:].reshape(tp_count, -1)[:, : 2 * n_rows]
            got_stats = got_stats.reshape(tp_count, 2, steps_n, rows_dev, heads_dev)
            got_peak = got_stats[:, 0]
            got_mass = got_stats[:, 1]

    own_query = queries.reshape(steps_n, rows_dev, heads_dev, DH)
    f_kv = fresh_kv.reshape(2, steps_n, rows_dev, kv_heads, DH)
    if group % heads_dev == 0:
        one_kv = lax.dynamic_index_in_dim(f_kv, tp_rank * heads_dev // group, 3, keepdims=True)
        f_kv = jnp.broadcast_to(one_kv, (2, steps_n, rows_dev, heads_dev, DH))
    else:
        kv_of_head = (tp_rank * heads_dev + jnp.arange(heads_dev)) // group
        f_kv = jnp.take(f_kv, kv_of_head, axis=3)
    f_scores = (
        jnp.einsum("sbhd,ubhd->sbhu", own_query, f_kv[0], preferred_element_type=jnp.float32)
        * score_scale
    )
    fresh_live = jnp.arange(steps_n)[None, :] <= jnp.arange(steps_n)[:, None]
    f_scores = jnp.where(fresh_live[:, None, None, :], f_scores, NEG_FILL)

    peak = jnp.maximum(got_peak.max(0), f_scores.max(-1))
    rescale = jnp.exp(got_peak - peak[None])
    f_w = jnp.exp(f_scores - peak[..., None])
    mass = (got_mass * rescale).sum(0) + f_w.sum(-1)
    numer = (got_numer * rescale[..., None]).sum(0)
    numer = numer + jnp.einsum(
        "sbhu,ubhd->sbhd", f_w.astype(jnp.bfloat16), f_kv[1], preferred_element_type=jnp.float32
    )
    attended = (numer / mass[..., None]).astype(jnp.bfloat16).reshape(steps_n, rows_dev, width_dev)

    gathered = lax.all_gather(attended, "sub", axis=1, tiled=True)
    samples = gathered.shape[1]
    local_width = out_weight.shape[1]
    head_rows_in = gathered.reshape(steps_n * samples, heads_dev, DH)
    head_weights = out_weight.reshape(heads_dev, DH, local_width)
    scale_a = jnp.repeat(jnp.exp2(-scale_in.astype(jnp.float32)), 128)
    scale_b = jnp.repeat(jnp.exp2(-scale_out.astype(jnp.float32)), 128)
    local_a = lax.dynamic_slice_in_dim(scale_a, sub_rank * local_width, local_width, 0)
    local_b = lax.dynamic_slice_in_dim(scale_b, sub_rank * local_width, local_width, 0)
    per_head_term = jnp.einsum(
        "rhd,hdf->rhf", head_rows_in, head_weights, preferred_element_type=jnp.float32
    )
    clipped = jnp.clip(per_head_term / local_a[None, None, :], -127.0, 127.0).sum(1)

    piece_cols = local_width // tp_count
    pieces = jnp.moveaxis(clipped.reshape(steps_n * samples, tp_count, piece_cols), 1, 0)
    got_pieces = _exchange(pieces, "tp", tp_count)
    summed = got_pieces.sum(0)
    piece_start = sub_rank * local_width + tp_rank * piece_cols
    piece_a = lax.dynamic_slice_in_dim(scale_a, piece_start, piece_cols, 0)
    piece_b = lax.dynamic_slice_in_dim(scale_b, piece_start, piece_cols, 0)
    levels = jnp.clip(summed * piece_a / piece_b, -127.0, 127.0).astype(jnp.bfloat16)
    level_blocks = _gather_blocks(levels, "tp", tp_count)
    all_levels = jnp.moveaxis(level_blocks, 0, 1).reshape(steps_n * samples, local_width)
    restored = all_levels.astype(jnp.float32) * local_b
    hidden = residual.reshape(steps_n * samples, local_width).astype(jnp.float32) + restored
    return hidden.astype(jnp.bfloat16).reshape(steps_n, samples, local_width)


def solution(mesh):
    return jax.shard_map(
        per_device,
        mesh=mesh,
        in_specs=(
            P(None, ("rep", "sub"), "tp"),
            P(None, ("rep", "tp"), None),
            P(None, ("rep", "sub"), "tp", None),
            P(("rep", "sub")),
            P(None, None, ("rep", "sub"), None),
            P("tp", "sub"),
            P(),
            P(),
            P(None, "rep", "sub"),
        ),
        out_specs=P(None, "rep", "sub"),
        check_vma=False,
    )
```

```python
import functools
import math

import jax
import jax.numpy as jnp
from jax import lax
from jax.experimental import pallas as pl
from jax.experimental.pallas import tpu as pltpu
from jax.sharding import PartitionSpec as P

DH = 128


NEG_FILL = -1e30


def _is_pow2(n):
    return n >= 1 and (n & (n - 1)) == 0


def _gather_blocks(x, axis_name, count):
    if count == 1:
        return x[None]
    if not _is_pow2(count):
        return lax.all_gather(x, axis_name, axis=0, tiled=False)
    me = lax.axis_index(axis_name)
    if count <= 8:
        other = lax.ppermute(x, axis_name, [(i, i ^ 1) for i in range(count)])
        low = me % 2 == 0
        pair = jnp.where(low, jnp.stack([x, other]), jnp.stack([other, x]))
        pairs = [pair]
        for d in range(1, count // 2):
            pairs.append(
                lax.ppermute(pair, axis_name, [(i, (i + 2 * d) % count) for i in range(count)])
            )
        order = (me // 2 - jnp.arange(count // 2)) % (count // 2)
        placed = jnp.zeros((count // 2,) + pair.shape, pair.dtype).at[order].set(jnp.stack(pairs))
        return placed.reshape((count,) + x.shape)
    cur = x[None]
    k = 1
    while k < count:
        other = lax.ppermute(cur, axis_name, [(i, i ^ k) for i in range(count)])
        low = (me // k) % 2 == 0
        cur = jnp.where(low, jnp.concatenate([cur, other]), jnp.concatenate([other, cur]))
        k *= 2
    return cur


def _exchange(blocks, axis_name, count, direct_max=8):
    if count == 1:
        return blocks
    if count > direct_max:
        return jax.tree.map(
            lambda b: lax.all_to_all(b, axis_name, split_axis=0, concat_axis=0, tiled=True), blocks
        )
    me = lax.axis_index(axis_name)
    got = [jax.tree.map(lambda b: lax.dynamic_index_in_dim(b, me, 0, keepdims=False), blocks)]
    if count in (4, 8):
        half = count // 2
        moves = [(me ^ 1, [(i, i ^ 1) for i in range(count)])]
        for d in range(1, half):
            for flip in (0, 1):
                moves.append((
                    ((me // 2 + d) % half) * 2 + (me % 2 ^ flip),
                    [(i, ((i // 2 + d) % half) * 2 + (i % 2 ^ flip)) for i in range(count)],
                ))
    else:
        moves = [((me + k) % count, [(i, (i + k) % count) for i in range(count)])
                 for k in range(1, count)]
    for dst, perm in moves:
        send = jax.tree.map(lambda b: lax.dynamic_index_in_dim(b, dst, 0, keepdims=False), blocks)
        got.append(lax.ppermute(send, axis_name, perm))
    return jax.tree.map(lambda *xs: jnp.stack(xs), *got)


def _attend_kernel(q_ref, k_ref, v_ref, tk_ref, tv_ref, valid_ref, numer_ref, peak_ref, mass_ref):
    heads_n, rows_n = q_ref.shape[0], q_ref.shape[1]
    samples = tk_ref.shape[1]
    per_sample = rows_n // samples
    score_scale = 1.0 / math.sqrt(DH)
    dims_nt = (((1,), (1,)), ((), ()))
    for j in range(heads_n):
        cols = slice(j * DH, (j + 1) * DH)
        q = q_ref[j]
        p_scores = lax.dot_general(q, k_ref[0, :, cols], dims_nt, preferred_element_type=jnp.float32)
        p_scores = p_scores * score_scale
        t_parts = []
        for r in range(samples):
            qr = q[r * per_sample:(r + 1) * per_sample]
            sr = lax.dot_general(
                qr, tk_ref[0, r, :, cols], dims_nt, preferred_element_type=jnp.float32
            )
            sr = sr * score_scale
            t_parts.append(jnp.where(valid_ref[r:r + 1, :] > 0.0, sr, NEG_FILL))
        t_scores = jnp.concatenate(t_parts, axis=0)
        peak = jnp.maximum(
            jnp.max(p_scores, axis=1, keepdims=True), jnp.max(t_scores, axis=1, keepdims=True)
        )
        p_w = jnp.exp(p_scores - peak)
        t_w = jnp.exp(t_scores - peak)
        mass = jnp.sum(p_w, axis=1, keepdims=True) + jnp.sum(t_w, axis=1, keepdims=True)
        numer = jnp.dot(
            p_w.astype(jnp.bfloat16), v_ref[0, :, cols], preferred_element_type=jnp.float32
        )
        t_w16 = t_w.astype(jnp.bfloat16)
        t_numer = [
            jnp.dot(
                t_w16[r * per_sample:(r + 1) * per_sample], tv_ref[0, r, :, cols],
                preferred_element_type=jnp.float32,
            )
            for r in range(samples)
        ]
        numer_ref[j] = numer + jnp.concatenate(t_numer, axis=0)
        peak_ref[j] = jnp.broadcast_to(peak, peak_ref.shape[1:])
        mass_ref[j] = jnp.broadcast_to(mass, mass_ref.shape[1:])


def _attend_local(q_rows, prefix_kv, tail_kv, valid):
    kv_heads, rows_n, _ = q_rows.shape
    prefix_dev = prefix_kv.shape[1]
    samples, tail_dev = tail_kv.shape[1], tail_kv.shape[2]
    flops = 4 * kv_heads * rows_n * DH * (prefix_dev + tail_dev)
    bytes_in = 2 * (prefix_kv.size + tail_kv.size + q_rows.size)
    per_step = 4 if kv_heads % 4 == 0 else 1
    width = per_step * DH
    return pl.pallas_call(
        _attend_kernel,
        grid=(kv_heads // per_step,),
        in_specs=[
            pl.BlockSpec((per_step, rows_n, DH), lambda k: (k, 0, 0)),
            pl.BlockSpec((1, prefix_dev, width), lambda k: (0, 0, k)),
            pl.BlockSpec((1, prefix_dev, width), lambda k: (1, 0, k)),
            pl.BlockSpec((1, samples, tail_dev, width), lambda k: (0, 0, 0, k)),
            pl.BlockSpec((1, samples, tail_dev, width), lambda k: (1, 0, 0, k)),
            pl.BlockSpec((samples, tail_dev), lambda k: (0, 0)),
        ],
        out_specs=[
            pl.BlockSpec((per_step, rows_n, DH), lambda k: (k, 0, 0)),
            pl.BlockSpec((per_step, rows_n, DH), lambda k: (k, 0, 0)),
            pl.BlockSpec((per_step, rows_n, DH), lambda k: (k, 0, 0)),
        ],
        out_shape=[jax.ShapeDtypeStruct((kv_heads, rows_n, DH), jnp.float32)] * 3,
        cost_estimate=pl.CostEstimate(
            flops=flops,
            transcendentals=kv_heads * rows_n * (prefix_dev + tail_dev),
            bytes_accessed=bytes_in + 3 * 4 * kv_heads * rows_n * DH,
        ),
        compiler_params=pltpu.CompilerParams(vmem_limit_bytes=48 * 1024 * 1024),
    )(q_rows, prefix_kv, prefix_kv, tail_kv, tail_kv, valid)


def _attend_packed_kernel(
    group, q_ref, k_ref, v_ref, tk_ref, tv_ref, valid_ref, out_ref
):
    heads_n, rows_n = q_ref.shape[0], q_ref.shape[1]
    samples, tail_dev = tk_ref.shape[1], tk_ref.shape[2]
    score_scale = 1.0 / math.sqrt(DH)
    dims_nt = (((1,), (1,)), ((), ()))
    row_sample = (lax.broadcasted_iota(jnp.int32, (rows_n, tail_dev), 0) // group) % samples
    for j in range(heads_n):
        cols = slice(j * DH, (j + 1) * DH)
        q = q_ref[j]
        p_scores = lax.dot_general(q, k_ref[0, :, cols], dims_nt, preferred_element_type=jnp.float32)
        p_scores = p_scores * score_scale
        t_scores = jnp.full((rows_n, tail_dev), NEG_FILL, jnp.float32)
        for r in range(samples):
            sr = lax.dot_general(
                q, tk_ref[0, r, :, cols], dims_nt, preferred_element_type=jnp.float32
            )
            live = (row_sample == r) & (valid_ref[r:r + 1, :] > 0.0)
            t_scores = jnp.where(live, sr * score_scale, t_scores)
        peak = jnp.maximum(
            jnp.max(p_scores, axis=1, keepdims=True), jnp.max(t_scores, axis=1, keepdims=True)
        )
        p_w = jnp.exp(p_scores - peak)
        t_w = jnp.exp(t_scores - peak)
        mass = jnp.sum(p_w, axis=1, keepdims=True) + jnp.sum(t_w, axis=1, keepdims=True)
        numer = jnp.dot(
            p_w.astype(jnp.bfloat16), v_ref[0, :, cols], preferred_element_type=jnp.float32
        )
        for r in range(samples):
            t_w16 = jnp.where(row_sample == r, t_w, 0.0).astype(jnp.bfloat16)
            numer = numer + jnp.dot(t_w16, tv_ref[0, r, :, cols], preferred_element_type=jnp.float32)
        out_ref[j, :rows_n, :] = numer
        peak_row = jnp.transpose(jnp.broadcast_to(peak, (rows_n, DH)))[0:1]
        mass_row = jnp.transpose(jnp.broadcast_to(mass, (rows_n, DH)))[0:1]
        out_ref[j, rows_n:, :] = jnp.concatenate(
            [peak_row, mass_row, jnp.zeros((6, DH), jnp.float32)], axis=0
        )


def _attend_packed(q_rows, prefix_kv, tail_kv, valid, group):
    kv_heads, rows_n, _ = q_rows.shape
    prefix_dev = prefix_kv.shape[1]
    samples, tail_dev = tail_kv.shape[1], tail_kv.shape[2]
    flops = 4 * kv_heads * rows_n * DH * (prefix_dev + samples * tail_dev)
    bytes_in = 2 * (prefix_kv.size + tail_kv.size + q_rows.size)
    per_step = 4 if kv_heads % 4 == 0 else 1
    width = per_step * DH
    return pl.pallas_call(
        functools.partial(_attend_packed_kernel, group),
        grid=(kv_heads // per_step,),
        in_specs=[
            pl.BlockSpec((per_step, rows_n, DH), lambda k: (k, 0, 0)),
            pl.BlockSpec((1, prefix_dev, width), lambda k: (0, 0, k)),
            pl.BlockSpec((1, prefix_dev, width), lambda k: (1, 0, k)),
            pl.BlockSpec((1, samples, tail_dev, width), lambda k: (0, 0, 0, k)),
            pl.BlockSpec((1, samples, tail_dev, width), lambda k: (1, 0, 0, k)),
            pl.BlockSpec((samples, tail_dev), lambda k: (0, 0)),
        ],
        out_specs=pl.BlockSpec((per_step, rows_n + 8, DH), lambda k: (k, 0, 0)),
        out_shape=jax.ShapeDtypeStruct((kv_heads, rows_n + 8, DH), jnp.float32),
        cost_estimate=pl.CostEstimate(
            flops=flops,
            transcendentals=kv_heads * rows_n * (prefix_dev + tail_dev),
            bytes_accessed=bytes_in + 4 * kv_heads * (rows_n + 8) * DH,
        ),
        compiler_params=pltpu.CompilerParams(vmem_limit_bytes=48 * 1024 * 1024),
    )(q_rows, prefix_kv, prefix_kv, tail_kv, tail_kv, valid)


def _attend_packed_pairs(blk, q_rows, prefix_kv, tail_kv, valid, group):
    heads_n, rows_n, _ = q_rows.shape
    prefix_dev = prefix_kv.shape[1]
    samples, tail_dev = tail_kv.shape[1], tail_kv.shape[2]
    flops = 4 * heads_n * rows_n * DH * (prefix_dev + samples * tail_dev)
    width = 2 * DH
    grid_spec = pltpu.PrefetchScalarGridSpec(
        num_scalar_prefetch=1,
        grid=(heads_n // 2,),
        in_specs=[
            pl.BlockSpec((2, rows_n, DH), lambda g, b: (g, 0, 0)),
            pl.BlockSpec((1, prefix_dev, width), lambda g, b: (0, 0, b[g])),
            pl.BlockSpec((1, prefix_dev, width), lambda g, b: (1, 0, b[g])),
            pl.BlockSpec((1, samples, tail_dev, width), lambda g, b: (0, 0, 0, b[g])),
            pl.BlockSpec((1, samples, tail_dev, width), lambda g, b: (1, 0, 0, b[g])),
            pl.BlockSpec((samples, tail_dev), lambda g, b: (0, 0)),
        ],
        out_specs=pl.BlockSpec((2, rows_n + 8, DH), lambda g, b: (g, 0, 0)),
    )
    return pl.pallas_call(
        lambda b_ref, *refs: _attend_packed_kernel(group, *refs),
        grid_spec=grid_spec,
        out_shape=jax.ShapeDtypeStruct((heads_n, rows_n + 8, DH), jnp.float32),
        cost_estimate=pl.CostEstimate(
            flops=flops,
            transcendentals=heads_n * rows_n * (prefix_dev + tail_dev),
            bytes_accessed=2 * (2 * prefix_dev + 2 * samples * tail_dev) * heads_n * DH
            + 2 * q_rows.size + 4 * heads_n * (rows_n + 8) * DH,
        ),
        compiler_params=pltpu.CompilerParams(vmem_limit_bytes=48 * 1024 * 1024),
    )(blk.astype(jnp.int32), q_rows, prefix_kv, prefix_kv, tail_kv, tail_kv, valid)


def per_device(
    queries, prefix_kv, tail_kv, tail_lengths, fresh_kv, out_weight, scale_in, scale_out, residual
):
    steps_n, rows_dev, width_dev = queries.shape
    heads_dev = width_dev // DH
    tp_count = lax.axis_size("tp")
    tp_rank = lax.axis_index("tp")
    sub_rank = lax.axis_index("sub")
    kv_heads = prefix_kv.shape[2] // DH
    heads_all = heads_dev * tp_count
    group = heads_all // kv_heads
    prefix_dev = prefix_kv.shape[1]
    tail_dev = tail_kv.shape[2]
    score_scale = 1.0 / math.sqrt(DH)

    n_rows = steps_n * rows_dev * heads_dev
    pairs_ok = (tp_count == kv_heads and heads_dev == group and n_rows == DH
                and tp_count in (4, 8))
    if pairs_ok:
        t_pos = tp_rank * tail_dev + jnp.arange(tail_dev)
        valid = (t_pos[None, :] < tail_lengths[:, None]).astype(jnp.float32)
        half = tp_count // 2
        mine = tp_rank // 2
        other = lax.ppermute(queries, "tp", [(i, i ^ 1) for i in range(tp_count)])
        pair = jnp.where(tp_rank % 2 == 0, jnp.stack([queries, other]), jnp.stack([other, queries]))
        far = [
            lax.ppermute(pair, "tp", [(i, (i + 2 * d) % tp_count) for i in range(tp_count)])
            for d in range(1, half)
        ]
        out_near = _attend_packed_pairs(
            jnp.reshape(mine, (1,)), pair.reshape(2, -1, DH), prefix_kv, tail_kv, valid, group
        )
        far_blk = (mine - jnp.arange(1, half)) % half
        out_far = _attend_packed_pairs(
            far_blk, jnp.stack(far).reshape(2 * (half - 1), -1, DH), prefix_kv, tail_kv, valid,
            group,
        )
        outs = jnp.concatenate([out_near, out_far])

        def position(head):
            d = (mine - head // 2) % half
            return jnp.where(d == 0, head % 2, 2 * d + head % 2)

        got = [
            lax.dynamic_index_in_dim(out_near, tp_rank % 2, 0, keepdims=False),
            lax.ppermute(
                lax.dynamic_index_in_dim(out_near, 1 - tp_rank % 2, 0, keepdims=False),
                "tp", [(i, i ^ 1) for i in range(tp_count)],
            ),
        ]
        for d in range(1, half):
            for flip in (0, 1):
                dst = ((mine + d) % half) * 2 + (tp_rank % 2 ^ flip)
                perm = [(i, ((i // 2 + d) % half) * 2 + (i % 2 ^ flip)) for i in range(tp_count)]
                send = lax.dynamic_index_in_dim(outs, position(dst), 0, keepdims=False)
                got.append(lax.ppermute(send, "tp", perm))
        got = jnp.stack(got)
        got_numer = got[:, :n_rows].reshape(tp_count, steps_n, rows_dev, heads_dev, DH)
        got_peak = got[:, n_rows].reshape(tp_count, steps_n, rows_dev, heads_dev)
        got_mass = got[:, n_rows + 1].reshape(tp_count, steps_n, rows_dev, heads_dev)
        q_blocks = None
    else:
        q_blocks = _gather_blocks(queries, "tp", tp_count)
    if not pairs_ok:
        q_all = jnp.moveaxis(q_blocks, 0, 2).reshape(steps_n, rows_dev, kv_heads, group, DH)
        t_pos = tp_rank * tail_dev + jnp.arange(tail_dev)
        valid = (t_pos[None, :] < tail_lengths[:, None]).astype(jnp.float32)
        n_rows = steps_n * rows_dev * heads_dev
        if tp_count == kv_heads and heads_dev == group and n_rows == DH:
            q_rows = jnp.transpose(q_all, (2, 0, 1, 3, 4)).reshape(kv_heads, -1, DH)
            got = _exchange(_attend_packed(q_rows, prefix_kv, tail_kv, valid, group), "tp", tp_count)
            got_numer = got[:, :n_rows].reshape(tp_count, steps_n, rows_dev, heads_dev, DH)
            got_peak = got[:, n_rows].reshape(tp_count, steps_n, rows_dev, heads_dev)
            got_mass = got[:, n_rows + 1].reshape(tp_count, steps_n, rows_dev, heads_dev)
        else:

            q_rows = jnp.transpose(q_all, (2, 1, 0, 3, 4)).reshape(kv_heads, -1, DH)
            t_pos = tp_rank * tail_dev + jnp.arange(tail_dev)
            valid = (t_pos[None, :] < tail_lengths[:, None]).astype(jnp.float32)
            k_numer, k_peak, k_mass = _attend_local(q_rows, prefix_kv, tail_kv, valid)

            def by_owner(x):
                x = jnp.transpose(x, (2, 1, 0, 3) + tuple(range(4, x.ndim)))
                x = x.reshape((steps_n, rows_dev, tp_count, heads_dev) + x.shape[4:])
                return jnp.moveaxis(x, 2, 0)

            grid4 = (kv_heads, rows_dev, steps_n, group)
            o_numer = by_owner(k_numer.reshape(grid4 + (DH,))).reshape(tp_count, -1, DH)
            o_peak = by_owner(k_peak[..., 0].reshape(grid4)).reshape(tp_count, -1)
            o_mass = by_owner(k_mass[..., 0].reshape(grid4)).reshape(tp_count, -1)
            n_rows = steps_n * rows_dev * heads_dev
            n_stat = -(-2 * n_rows // DH)
            stats = jnp.concatenate([o_peak, o_mass], axis=1)
            stats = jnp.pad(stats, ((0, 0), (0, n_stat * DH - 2 * n_rows))).reshape(tp_count, n_stat, DH)
            got = _exchange(jnp.concatenate([o_numer, stats], axis=1), "tp", tp_count)
            got_numer = got[:, :n_rows].reshape(tp_count, steps_n, rows_dev, heads_dev, DH)
            got_stats = got[:, n_rows:].reshape(tp_count, -1)[:, : 2 * n_rows]
            got_stats = got_stats.reshape(tp_count, 2, steps_n, rows_dev, heads_dev)
            got_peak = got_stats[:, 0]
            got_mass = got_stats[:, 1]

    own_query = queries.reshape(steps_n, rows_dev, heads_dev, DH)
    f_kv = fresh_kv.reshape(2, steps_n, rows_dev, kv_heads, DH)
    if group % heads_dev == 0:
        one_kv = lax.dynamic_index_in_dim(f_kv, tp_rank * heads_dev // group, 3, keepdims=True)
        f_kv = jnp.broadcast_to(one_kv, (2, steps_n, rows_dev, heads_dev, DH))
    else:
        kv_of_head = (tp_rank * heads_dev + jnp.arange(heads_dev)) // group
        f_kv = jnp.take(f_kv, kv_of_head, axis=3)
    f_scores = (
        jnp.einsum("sbhd,ubhd->sbhu", own_query, f_kv[0], preferred_element_type=jnp.float32)
        * score_scale
    )
    fresh_live = jnp.arange(steps_n)[None, :] <= jnp.arange(steps_n)[:, None]
    f_scores = jnp.where(fresh_live[:, None, None, :], f_scores, NEG_FILL)

    peak = jnp.maximum(got_peak.max(0), f_scores.max(-1))
    rescale = jnp.exp(got_peak - peak[None])
    f_w = jnp.exp(f_scores - peak[..., None])
    mass = (got_mass * rescale).sum(0) + f_w.sum(-1)
    numer = (got_numer * rescale[..., None]).sum(0)
    numer = numer + jnp.einsum(
        "sbhu,ubhd->sbhd", f_w.astype(jnp.bfloat16), f_kv[1], preferred_element_type=jnp.float32
    )
    attended = (numer / mass[..., None]).astype(jnp.bfloat16).reshape(steps_n, rows_dev, width_dev)

    gathered = lax.all_gather(attended, "sub", axis=1, tiled=True)
    samples = gathered.shape[1]
    local_width = out_weight.shape[1]
    head_rows_in = gathered.reshape(steps_n * samples, heads_dev, DH)
    head_weights = out_weight.reshape(heads_dev, DH, local_width)
    scale_a = jnp.repeat(jnp.exp2(-scale_in.astype(jnp.float32)), 128)
    scale_b = jnp.repeat(jnp.exp2(-scale_out.astype(jnp.float32)), 128)
    local_a = lax.dynamic_slice_in_dim(scale_a, sub_rank * local_width, local_width, 0)
    local_b = lax.dynamic_slice_in_dim(scale_b, sub_rank * local_width, local_width, 0)
    per_head_term = jnp.einsum(
        "rhd,hdf->rhf", head_rows_in, head_weights, preferred_element_type=jnp.float32
    )
    clipped = jnp.clip(per_head_term / local_a[None, None, :], -127.0, 127.0).sum(1)

    piece_cols = local_width // tp_count
    pieces = jnp.moveaxis(clipped.reshape(steps_n * samples, tp_count, piece_cols), 1, 0)
    got_pieces = _exchange(pieces, "tp", tp_count)
    summed = got_pieces.sum(0)
    piece_start = sub_rank * local_width + tp_rank * piece_cols
    piece_a = lax.dynamic_slice_in_dim(scale_a, piece_start, piece_cols, 0)
    piece_b = lax.dynamic_slice_in_dim(scale_b, piece_start, piece_cols, 0)
    levels = jnp.clip(summed * piece_a / piece_b, -127.0, 127.0).astype(jnp.bfloat16)
    level_blocks = _gather_blocks(levels, "tp", tp_count)
    all_levels = jnp.moveaxis(level_blocks, 0, 1).reshape(steps_n * samples, local_width)
    restored = all_levels.astype(jnp.float32) * local_b
    hidden = residual.reshape(steps_n * samples, local_width).astype(jnp.float32) + restored
    return hidden.astype(jnp.bfloat16).reshape(steps_n, samples, local_width)


def solution(mesh):
    return jax.shard_map(
        per_device,
        mesh=mesh,
        in_specs=(
            P(None, ("rep", "sub"), "tp"),
            P(None, ("rep", "tp"), None),
            P(None, ("rep", "sub"), "tp", None),
            P(("rep", "sub")),
            P(None, None, ("rep", "sub"), None),
            P("tp", "sub"),
            P(),
            P(),
            P(None, "rep", "sub"),
        ),
        out_specs=P(None, "rep", "sub"),
        check_vma=False,
    )
```
